32 devices in a mesh: group: 2 (over y), ctx: 4 (over z), kvh: 2 (over x), sub: 2 (over core).
Axes of the slice: x: 2, y: 2, z: 4, core: 2. Of those that a mesh axis runs over, the one named last changes fastest.
Arguments:
- queries: bfloat16 [64, 128, 8192], P(('group', 'ctx'), 'sub', 'kvh'), parts along dimension 0, may hold values from -128 to 128
- cache_kv: bfloat16 [192, 128, 2048], P(('group', 'ctx'), None, 'kvh'), parts along dimension 0, may hold values from -4 to 4
- cache_scale: float32 [192, 16], P('group', 'kvh'), parts along dimension 0, may hold values from 0.29 to 3.01
- prompt_key_value: bfloat16 [64, 128, 2048], P(('group', 'ctx'), None, 'kvh'), parts along dimension 0, may hold values from -4 to 4
- prompt_scale: float32 [64, 16], P('group', 'kvh'), parts along dimension 0, may hold values from 0.3 to 3
- rand_blocks: int32 [64, 3], P('group'), parts along dimension 0, may hold values from 0 to 95, as said below
Outputs:
- attended: bfloat16 [64, 128, 8192], P(('group', 'ctx'), 'sub', 'kvh'), parts along dimension 0
The draws below stay inside these ranges and needn't reach their ends.
There are 2 independent parts, one for each index of `group`. The reference program is written for one: setup_inputs(seed, part) draws one part's arguments, and reference() takes and returns one part's arrays. A program takes and returns all parts, laid end to end along the dimension named above; each array names one. Nothing has to cross between parts.
Inputs may be any that keep to these rules, and one draw needn't show every extreme that they name: `rand_blocks`: within each aligned run of 8 prompt blocks, the run's entries name blocks of any one aligned range of 24 cache blocks at most 6 times; one and the same range is named exactly 6 times in every run, and each run has another range so named.
All inputs are finite; a program needn't handle non-finite values.
Results may differ from the reference program's by a relative error of at most 0.0051.
Values may be sent and summed in bfloat16 or wider, within the bound.
No kernel may reach another device: no remote copies, remote signals or barrier semaphores. Data moves between devices by JAX's collectives and lax.ppermute only.
A program may use at most 64 MiB of HBM per device.

```python
import math
import jax
import jax.numpy as jnp
from jax import lax

QUERY_HEADS = 64
KEY_VALUE_HEADS = 8
HEAD_SIZE = 128
BLOCK_TOKENS = 128
NG = 2
R = 3
WIN = 2
QB_DEV = 8
NB_DEV = 24
PROMPT_BLOCKS = 32
CACHE_BLOCK_COUNT = 96
CAP = 6
N_CTX = 4


def shared_tables(key):
    base = jax.random.fold_in(key, 11)
    key_scale_rows = jax.random.fold_in(base, 1)
    scale_factors = jnp.exp(jax.random.uniform(key_scale_rows, (CACHE_BLOCK_COUNT, 2 * KEY_VALUE_HEADS), jnp.float32, math.log(0.3), math.log(3.0)))
    return scale_factors


def draw_cache_scale(key, part):
    return shared_tables(key).astype(jnp.float32)


def draw_cache_kv(key, part):
    base = jax.random.fold_in(key, 23)
    array_shape = (CACHE_BLOCK_COUNT, BLOCK_TOKENS, KEY_VALUE_HEADS, 2, HEAD_SIZE)
    value_rows = jnp.clip(jax.random.normal(base, array_shape, jnp.float32), -4.0, 4.0)
    return value_rows.reshape(CACHE_BLOCK_COUNT, BLOCK_TOKENS, KEY_VALUE_HEADS * 2 * HEAD_SIZE).astype(jnp.bfloat16)


def draw_queries(key, part):
    base = jax.random.fold_in(key, 37)
    key_vals = jax.random.fold_in(base, 0)
    query_groups = QUERY_HEADS // KEY_VALUE_HEADS
    array_shape = (PROMPT_BLOCKS, BLOCK_TOKENS, KEY_VALUE_HEADS, query_groups, HEAD_SIZE)
    value_rows = jnp.clip(1.5 * jax.random.normal(key_vals, array_shape, jnp.float32), -6.0, 6.0)
    return value_rows.reshape(PROMPT_BLOCKS, BLOCK_TOKENS, QUERY_HEADS * HEAD_SIZE).astype(jnp.bfloat16)


def draw_rand_blocks(key, part):
    need = QB_DEV * R
    slot_total = N_CTX * CAP
    keys = jax.random.split(jax.random.fold_in(key, 41), 5)
    star = jax.random.randint(keys[0], (), 0, N_CTX)
    second = (star + 1 + jax.random.randint(keys[1], (N_CTX, 1), 0, N_CTX - 1)) % N_CTX
    slot_owner = (jnp.arange(slot_total, dtype=jnp.int32) // CAP)[None, :]
    forced = ((slot_owner == star) | (slot_owner == second)).astype(jnp.int32)
    noise = jax.random.randint(keys[2], (N_CTX, slot_total), 0, 1 << 16)
    priority = forced * (1 << 28) + noise * slot_total + jnp.arange(slot_total, dtype=jnp.int32)[None, :]
    order = jnp.argsort(-priority, axis=1, stable=True)[:, :need]
    chosen = order // CAP
    shuffle_noise = jax.random.randint(keys[3], (N_CTX, need), 0, 1 << 16) * need + jnp.arange(need, dtype=jnp.int32)[None, :]
    shuffle = jnp.argsort(shuffle_noise, axis=1, stable=True)
    chosen = jnp.take_along_axis(chosen, shuffle, axis=1)
    local = jax.random.randint(keys[4], (N_CTX, need), 0, NB_DEV)
    return (chosen * NB_DEV + local).reshape(N_CTX * QB_DEV, R).astype(jnp.int32)


def block_scale(rng, extent, pieces, least, largest):
    gain, own = 1.0, jax.random.fold_in(rng, 6)
    for axis_at, blocks in pieces:
        steps = jnp.exp(jax.random.uniform(jax.random.fold_in(own, axis_at), (blocks,), jnp.float32, least / len(pieces), largest / len(pieces)))
        gain = gain * jnp.repeat(steps, extent[axis_at] // blocks).reshape([-1 if axis == axis_at else 1 for axis in range(len(extent))])
    return gain


def scatter_about(stream_key, shape, deviation, reach, pieces=(), kind=jnp.bfloat16):
    gain = block_scale(stream_key, shape, pieces, -0.22, 0.18) if pieces else 1.0
    array = jax.random.normal(stream_key, shape, jnp.float32) * deviation * gain
    return jnp.minimum(jnp.maximum(array, -reach), reach).astype(kind)


def setup_inputs(seed: int = 0, part: int = 0) -> dict:
    arg_keys = jax.random.split(jax.random.key(seed), 7)
    own_keys = jax.random.split(jax.random.fold_in(arg_keys[6], part), 7)
    queries = draw_queries(jax.random.fold_in(jax.random.fold_in(arg_keys[6], part), 71), part)
    cache_kv = draw_cache_kv(jax.random.fold_in(jax.random.fold_in(arg_keys[6], part), 71), part)
    cache_scale = draw_cache_scale(jax.random.fold_in(jax.random.fold_in(arg_keys[6], part), 71), part)
    prompt_key_value = scatter_about(own_keys[3], (PROMPT_BLOCKS, BLOCK_TOKENS, KEY_VALUE_HEADS * 2 * HEAD_SIZE), 1.0, 4.0, ((0, 4), (2, 2)))
    prompt_scale = jnp.clip(jnp.exp(math.log(3.0) - 2.3025851 * jax.random.uniform(own_keys[4], (PROMPT_BLOCKS, KEY_VALUE_HEADS * 2), jnp.float32) ** block_scale(own_keys[4], (PROMPT_BLOCKS, KEY_VALUE_HEADS * 2), ((1, 2),), -0.2, 0.2)), 0.3, 3.0)
    rand_blocks = draw_rand_blocks(jax.random.fold_in(jax.random.fold_in(arg_keys[6], part), 71), part)
    return {"queries": queries, "cache_kv": cache_kv, "cache_scale": cache_scale, "prompt_key_value": prompt_key_value, "prompt_scale": prompt_scale, "rand_blocks": rand_blocks}


def reference(queries, cache_kv, cache_scale, prompt_key_value, prompt_scale, rand_blocks):
    query_groups = QUERY_HEADS // KEY_VALUE_HEADS
    key_total = NG + R + WIN + 1
    steps_back = jnp.arange(WIN, 0, -1, dtype=jnp.int32)
    row_ids = jnp.arange(BLOCK_TOKENS, dtype=jnp.int32)
    key_ids = jnp.arange(key_total * BLOCK_TOKENS, dtype=jnp.int32)
    last_start = (key_total - 1) * BLOCK_TOKENS

    def one_block(block_number):
        cache_ids = jnp.concatenate([jnp.arange(NG, dtype=jnp.int32), rand_blocks[block_number].astype(jnp.int32)])
        back_ids = block_number - steps_back
        prompt_ids = jnp.concatenate([jnp.maximum(back_ids, 0), jnp.reshape(block_number, (1,))]).astype(jnp.int32)
        prompt_ok = jnp.concatenate([back_ids >= 0, jnp.ones((1,), dtype=bool)])
        block_ok = jnp.concatenate([jnp.ones((NG + R,), dtype=bool), prompt_ok])
        collected_rows = jnp.concatenate([cache_kv[cache_ids], prompt_key_value[prompt_ids]], axis=0)
        scale_row_table = jnp.concatenate([cache_scale[cache_ids], prompt_scale[prompt_ids]], axis=0)
        collected_rows = collected_rows.reshape(key_total * BLOCK_TOKENS, KEY_VALUE_HEADS, 2, HEAD_SIZE)
        key_vals = collected_rows[:, :, 0].astype(jnp.float32)
        value_vals = collected_rows[:, :, 1].astype(jnp.float32)
        scale_row_table = scale_row_table.reshape(key_total, KEY_VALUE_HEADS, 2)
        key_scale = jnp.repeat(scale_row_table[:, :, 0], BLOCK_TOKENS, axis=0).T
        value_scale = jnp.repeat(scale_row_table[:, :, 1], BLOCK_TOKENS, axis=0).T
        query_entries = queries[block_number].reshape(BLOCK_TOKENS, KEY_VALUE_HEADS, query_groups, HEAD_SIZE).astype(jnp.float32)
        scores = jnp.einsum('rhgd,khd->hgrk', query_entries, key_vals)
        scores = scores * (key_scale / math.sqrt(HEAD_SIZE))[:, None, None, :]
        causal = (key_ids[None, :] < last_start) | (key_ids[None, :] - last_start <= row_ids[:, None])
        allowed = causal & jnp.repeat(block_ok, BLOCK_TOKENS)[None, :]
        scores = jnp.where(allowed[None, None], scores, -jnp.inf)
        row_max = lax.optimization_barrier(jnp.max(scores, axis=-1, keepdims=True))
        probs = jnp.exp(scores - row_max)
        totals = lax.optimization_barrier(jnp.sum(probs, axis=-1))
        weights = (probs * value_scale[:, None, None, :]).astype(jnp.bfloat16)
        result = jnp.einsum('hgrk,khd->rhgd', weights.astype(jnp.float32), value_vals)
        result = result / jnp.transpose(totals, (2, 0, 1))[..., None]
        return result.astype(jnp.bfloat16).reshape(BLOCK_TOKENS, QUERY_HEADS * HEAD_SIZE)
    return lax.map(one_block, jnp.arange(PROMPT_BLOCKS, dtype=jnp.int32))
```

```python
import math

import jax
import jax.numpy as jnp
from jax import lax
from jax.experimental import pallas as pl
from jax.experimental.pallas import tpu as pltpu
from jax.sharding import PartitionSpec as P

HEAD_SIZE = 128
NG = 2
WIN = 2


def passed_along(block, axis, distance):
    devices = range(lax.axis_size(axis))
    route = [(i - distance, i) for i in devices if i - distance in devices]
    return lax.ppermute(block, axis, route)


def from_root(block, axis):
    count = lax.axis_size(axis)
    index = lax.axis_index(axis)
    have = block
    reach = 1
    while reach < count:
        route = [(i, i + reach) for i in range(reach) if i + reach < count]
        got = lax.ppermute(have, axis, route)
        have = jnp.where((index >= reach) & (index < 2 * reach), got, have)
        reach *= 2
    return have


def attention_kernel(
    rpos_ref, meta_ref,
    q_ref, ks_ref, vs_ref,
    g0_ref, g1_ref, r0_ref, r1_ref, r2_ref, wr5_ref, wl5_ref, wr6_ref, wl6_ref, own_ref,
    o_ref,
):
    b = pl.program_id(1)
    base = meta_ref[0]
    sub = meta_ref[1]
    rows = q_ref.shape[1]
    groups = q_ref.shape[2] // HEAD_SIZE
    block_rows = own_ref.shape[1]
    d = HEAD_SIZE

    q = q_ref[0]
    q2 = jnp.concatenate([q[:, h * d:(h + 1) * d] for h in range(groups)], axis=0)

    first = b < 2
    w5 = jnp.where(first, wr5_ref[0], wl5_ref[0])
    w6 = jnp.where(b < 1, wr6_ref[0], wl6_ref[0])
    blocks = [g0_ref[0], g1_ref[0], r0_ref[0], r1_ref[0], r2_ref[0], w5, w6, own_ref[0]]
    keys = jnp.concatenate([blk[:, :d] for blk in blocks], axis=0)
    vals = jnp.concatenate([blk[:, d:] for blk in blocks], axis=0)

    s = lax.dot_general(q2, keys, (((1,), (1,)), ((), ())), preferred_element_type=jnp.float32)
    s = s * ks_ref[0, 0]

    total = s.shape[1]
    col = lax.broadcasted_iota(jnp.int32, (1, total), 1)
    row = lax.broadcasted_iota(jnp.int32, (groups * rows, 1), 0) % rows + sub * rows
    last_start = total - block_rows
    glob_b = base + b
    ok5 = glob_b - 2 >= 0
    ok6 = glob_b - 1 >= 0
    col_ok = (
        ((col < 5 * block_rows) | (col >= 7 * block_rows))
        | ((col < 6 * block_rows) & ok5)
        | ((col >= 6 * block_rows) & ok6)
    )
    allowed = col_ok & ((col < last_start) | (col - last_start <= row))
    s = jnp.where(allowed, s, -jnp.inf)
    m = jnp.max(s, axis=1, keepdims=True)
    p = jnp.exp(s - m)
    totals = jnp.sum(p, axis=1, keepdims=True)
    w = (p * vs_ref[0, 0]).astype(jnp.bfloat16)
    acc = lax.dot_general(w, vals, (((1,), (0,)), ((), ())), preferred_element_type=jnp.float32)
    res = (acc / totals).astype(o_ref.dtype)
    for h in range(groups):
        o_ref[0, :, h * d:(h + 1) * d] = res[h * rows:(h + 1) * rows]


def body(queries, cache_kv, cache_scale, prompt_key_value, prompt_scale, rand_blocks):
    ctx_count = lax.axis_size("ctx")
    ctx_index = lax.axis_index("ctx")
    sub_count = lax.axis_size("sub")
    sub_index = lax.axis_index("sub")
    local_blocks, row_count, query_width = queries.shape
    cache_blocks, block_rows, kv_width = cache_kv.shape
    head_dim = HEAD_SIZE
    local_heads = kv_width // (2 * head_dim)
    query_groups = query_width // (local_heads * head_dim)
    rand_count = rand_blocks.shape[1]
    capacity = max(2, (local_blocks * rand_count + ctx_count - 1) // ctx_count)
    part_rows = block_rows // sub_count

    def my_part(x):
        return lax.dynamic_slice_in_dim(x, sub_index * part_rows, part_rows, axis=1)

    window_part = passed_along(my_part(prompt_key_value[local_blocks - WIN:]), "ctx", 1)
    global_part = from_root(my_part(cache_kv[:NG]), "ctx")

    per_reader = rand_blocks.reshape(ctx_count, local_blocks * rand_count)
    owners = per_reader // cache_blocks
    owner_hot = (
        owners[:, :, None] == jnp.arange(ctx_count, dtype=jnp.int32)[None, None, :]
    ).astype(jnp.int32)
    slot_rank = jnp.sum((jnp.cumsum(owner_hot, axis=1) - 1) * owner_hot, axis=2)
    picked = (
        (owners == ctx_index)[:, :, None]
        & (slot_rank[:, :, None] == jnp.arange(capacity, dtype=jnp.int32)[None, None, :])
    ).astype(jnp.int32)
    local_ids = jnp.sum(picked * (per_reader % cache_blocks)[:, :, None], axis=1)
    outgoing = jnp.take(my_part(cache_kv), local_ids.reshape(-1), axis=0)
    incoming = lax.all_to_all(outgoing, "ctx", split_axis=0, concat_axis=0, tiled=True)

    remote_part = jnp.concatenate([window_part, global_part, incoming], axis=0)
    remote = lax.all_gather(remote_part, "sub", axis=1, tiled=True)

    own_refs = lax.dynamic_index_in_dim(per_reader, ctx_index, 0, keepdims=False)
    own_ranks = lax.dynamic_index_in_dim(slot_rank, ctx_index, 0, keepdims=False)
    own_ranks = jnp.minimum(own_ranks, capacity - 1)
    rpos = (WIN + NG + own_refs // cache_blocks * capacity + own_ranks).astype(jnp.int32)

    local_order = jnp.arange(local_blocks, dtype=jnp.int32)
    global_order = ctx_index * local_blocks + local_order
    steps_back = jnp.arange(WIN, 0, -1, dtype=jnp.int32)
    back_global = global_order[:, None] - steps_back[None, :]
    cache_ids = jnp.concatenate(
        [
            jnp.broadcast_to(jnp.arange(NG, dtype=jnp.int32)[None, :], (local_blocks, NG)),
            own_refs.reshape(local_blocks, rand_count),
        ],
        axis=1,
    )
    prompt_ids = jnp.concatenate([jnp.maximum(back_global, 0), global_order[:, None]], axis=1)
    scale_row_table = jnp.concatenate(
        [jnp.take(cache_scale, cache_ids, axis=0), jnp.take(prompt_scale, prompt_ids, axis=0)],
        axis=1,
    )
    key_total = scale_row_table.shape[1]
    scale_row_table = scale_row_table.reshape(local_blocks, key_total, local_heads, 2)
    scale_row_table = jnp.transpose(scale_row_table, (0, 2, 3, 1))
    key_scale = jnp.repeat(scale_row_table[:, :, 0] / math.sqrt(head_dim), block_rows, axis=-1)
    value_scale = jnp.repeat(scale_row_table[:, :, 1], block_rows, axis=-1)
    key_scale = key_scale.reshape(local_blocks, local_heads, 1, key_total * block_rows)
    value_scale = value_scale.reshape(local_blocks, local_heads, 1, key_total * block_rows)

    meta = jnp.stack([ctx_index * local_blocks, sub_index]).astype(jnp.int32)
    qw = query_groups * head_dim
    kvw = 2 * head_dim
    n_remote = remote.shape[0]

    def kv_spec(index_fn):
        return pl.BlockSpec((1, block_rows, kvw), index_fn)

    in_specs = [
        pl.BlockSpec((1, row_count, qw), lambda g, b, rp, mt: (b, 0, g)),
        pl.BlockSpec((1, 1, 1, key_total * block_rows), lambda g, b, rp, mt: (b, g, 0, 0)),
        pl.BlockSpec((1, 1, 1, key_total * block_rows), lambda g, b, rp, mt: (b, g, 0, 0)),
        kv_spec(lambda g, b, rp, mt: (WIN, 0, g)),
        kv_spec(lambda g, b, rp, mt: (WIN + 1, 0, g)),
        kv_spec(lambda g, b, rp, mt: (rp[b * 3], 0, g)),
        kv_spec(lambda g, b, rp, mt: (rp[b * 3 + 1], 0, g)),
        kv_spec(lambda g, b, rp, mt: (rp[b * 3 + 2], 0, g)),
        kv_spec(lambda g, b, rp, mt: (jnp.minimum(b, 1), 0, g)),
        kv_spec(lambda g, b, rp, mt: (jnp.maximum(b - 2, 0), 0, g)),
        kv_spec(lambda g, b, rp, mt: (1, 0, g)),
        kv_spec(lambda g, b, rp, mt: (jnp.maximum(b - 1, 0), 0, g)),
        kv_spec(lambda g, b, rp, mt: (b, 0, g)),
    ]
    out_spec = pl.BlockSpec((1, row_count, qw), lambda g, b, rp, mt: (b, 0, g))
    call = pl.pallas_call(
        attention_kernel,
        out_shape=jax.ShapeDtypeStruct(queries.shape, queries.dtype),
        grid_spec=pltpu.PrefetchScalarGridSpec(
            num_scalar_prefetch=2,
            grid=(local_heads, local_blocks),
            in_specs=in_specs,
            out_specs=out_spec,
        ),
        compiler_params=pltpu.CompilerParams(
            dimension_semantics=("arbitrary", "arbitrary"),
            vmem_limit_bytes=48 * 1024 * 1024,
        ),
    )
    del n_remote
    return call(
        rpos.reshape(-1), meta,
        queries, key_scale, value_scale,
        remote, remote, remote, remote, remote,
        remote, prompt_key_value, remote, prompt_key_value, prompt_key_value,
    )


def solution(mesh):
    in_specs = (
        P(("group", "ctx"), "sub", "kvh"),
        P(("group", "ctx"), None, "kvh"),
        P("group", "kvh"),
        P(("group", "ctx"), None, "kvh"),
        P("group", "kvh"),
        P("group", None),
    )
    out_specs = P(("group", "ctx"), "sub", "kvh")
    return jax.shard_map(body, mesh=mesh, in_specs=in_specs, out_specs=out_specs, check_vma=False)
```

```python
import math

import jax
import jax.numpy as jnp
from jax import lax
from jax.experimental import pallas as pl
from jax.experimental.pallas import tpu as pltpu
from jax.sharding import PartitionSpec as P

HEAD_SIZE = 128

NG = 2
WIN = 2


def passed_along(block, axis, distance):
    devices = range(lax.axis_size(axis))
    route = [(i - distance, i) for i in devices if i - distance in devices]
    return lax.ppermute(block, axis, route)


def from_root(block, axis):
    count = lax.axis_size(axis)
    index = lax.axis_index(axis)
    have = block
    reach = 1
    while reach < count:
        route = [(i, i + reach) for i in range(reach) if i + reach < count]
        got = lax.ppermute(have, axis, route)
        have = jnp.where((index >= reach) & (index < 2 * reach), got, have)
        reach *= 2
    return have


def attention_kernel(
    rpos_ref, meta_ref,
    q_ref, ks_ref, vs_ref,
    g0m, g0o, g1m, g1o, r0m, r0o, r1m, r1o, r2m, r2o, w5m, w5o, w6m, w6o,
    wl5_ref, wl6_ref, own_ref, *rest,
):
    o_ref = rest[-1]
    b = pl.program_id(1)
    base = meta_ref[0]
    sub = meta_ref[1]
    rows = q_ref.shape[1]
    groups = q_ref.shape[2] // HEAD_SIZE
    block_rows = own_ref.shape[1]
    d = HEAD_SIZE

    q = q_ref[0]
    q2 = jnp.concatenate([q[:, h * d:(h + 1) * d] for h in range(groups)], axis=0)

    def joined(mine, other):
        return jnp.concatenate([mine[0], other[0]], axis=0)

    w5 = jnp.where(b < 2, joined(w5m, w5o), wl5_ref[0])
    w6 = jnp.where(b < 1, joined(w6m, w6o), wl6_ref[0])
    blocks = [
        joined(g0m, g0o), joined(g1m, g1o),
        joined(r0m, r0o), joined(r1m, r1o), joined(r2m, r2o),
        w5, w6,
    ]
    own = own_ref[0]
    keys = jnp.concatenate([blk[:, :d] for blk in blocks], axis=0)
    vals = jnp.concatenate([blk[:, d:] for blk in blocks], axis=0)
    front = keys.shape[0]

    dims = (((1,), (1,)), ((), ()))
    ks = ks_ref[0, 0]
    vs = vs_ref[0, 0]
    col = lax.broadcasted_iota(jnp.int32, (1, front), 1)
    glob_b = base + b
    bad = ((col >= 5 * block_rows) & (col < 6 * block_rows) & (glob_b < 2)) | (
        (col >= 6 * block_rows) & (glob_b < 1)
    )
    bias = jnp.where(bad, -jnp.inf, 0.0).astype(jnp.float32)
    s_a = lax.dot_general(q2, keys, dims, preferred_element_type=jnp.float32)
    s_a = s_a * ks[:, :front] + bias
    s_b = lax.dot_general(q2, own[:, :d], dims, preferred_element_type=jnp.float32)
    s_b = s_b * ks[:, front:]
    kcol = lax.broadcasted_iota(jnp.int32, (1, block_rows), 1)
    row = lax.broadcasted_iota(jnp.int32, (groups * rows, 1), 0) % rows + sub * rows
    s_b = jnp.where(kcol <= row, s_b, -jnp.inf)
    m = jnp.maximum(jnp.max(s_a, axis=1, keepdims=True), jnp.max(s_b, axis=1, keepdims=True))
    p_a = jnp.exp(s_a - m)
    p_b = jnp.exp(s_b - m)
    totals = jnp.sum(p_a, axis=1, keepdims=True) + jnp.sum(p_b, axis=1, keepdims=True)
    w_a = (p_a * vs[:, :front]).astype(jnp.bfloat16)
    w_b = (p_b * vs[:, front:]).astype(jnp.bfloat16)
    pv = (((1,), (0,)), ((), ()))
    acc = lax.dot_general(w_a, vals, pv, preferred_element_type=jnp.float32)
    acc = acc + lax.dot_general(w_b, own[:, d:], pv, preferred_element_type=jnp.float32)
    res = (acc / totals).astype(o_ref.dtype)
    for h in range(groups):
        o_ref[0, :, h * d:(h + 1) * d] = res[h * rows:(h + 1) * rows]


def body(queries, cache_kv, cache_scale, prompt_key_value, prompt_scale, rand_blocks):
    ctx_count = lax.axis_size("ctx")
    ctx_index = lax.axis_index("ctx")
    sub_count = lax.axis_size("sub")
    sub_index = lax.axis_index("sub")
    local_blocks, row_count, query_width = queries.shape
    cache_blocks, block_rows, kv_width = cache_kv.shape
    head_dim = HEAD_SIZE
    kvw = 2 * head_dim
    local_heads = kv_width // kvw
    query_groups = query_width // (local_heads * head_dim)
    rand_count = rand_blocks.shape[1]
    capacity = max(2, (local_blocks * rand_count + ctx_count - 1) // ctx_count)
    part_rows = block_rows // sub_count
    chunks = 2 if local_heads % 2 == 0 else 1
    chunk_heads = local_heads // chunks
    chunk_width = chunk_heads * kvw

    cache_parts = cache_kv.reshape(cache_blocks * sub_count, part_rows, kv_width)
    prompt_parts = prompt_key_value.reshape(local_blocks * sub_count, part_rows, kv_width)
    window_ids = (jnp.arange(local_blocks - WIN, local_blocks) * sub_count + sub_index)
    global_ids = jnp.arange(NG) * sub_count + sub_index

    per_reader = rand_blocks.reshape(ctx_count, local_blocks * rand_count)
    owners = per_reader // cache_blocks
    owner_hot = (
        owners[:, :, None] == jnp.arange(ctx_count, dtype=jnp.int32)[None, None, :]
    ).astype(jnp.int32)
    slot_rank = jnp.sum((jnp.cumsum(owner_hot, axis=1) - 1) * owner_hot, axis=2)
    picked = (
        (owners == ctx_index)[:, :, None]
        & (slot_rank[:, :, None] == jnp.arange(capacity, dtype=jnp.int32)[None, None, :])
    ).astype(jnp.int32)
    local_ids = jnp.sum(picked * (per_reader % cache_blocks)[:, :, None], axis=1)
    send_ids = local_ids.reshape(-1) * sub_count + sub_index

    swap = [(i, i ^ 1) for i in range(sub_count)] if sub_count == 2 else None
    pieces = []
    for c in range(chunks):
        cols = slice(c * chunk_width, (c + 1) * chunk_width)
        window_part = passed_along(jnp.take(prompt_parts[:, :, cols], window_ids, axis=0), "ctx", 1)
        global_part = from_root(jnp.take(cache_parts[:, :, cols], global_ids, axis=0), "ctx")
        outgoing = jnp.take(cache_parts[:, :, cols], send_ids, axis=0)
        incoming = []
        for dist in range(ctx_count):
            reader = (ctx_index + dist) % ctx_count
            slots = lax.dynamic_slice_in_dim(outgoing, reader * capacity, capacity, axis=0)
            if dist:
                route = [(i, (i + dist) % ctx_count) for i in range(ctx_count)]
                slots = lax.ppermute(slots, "ctx", route)
            incoming.append(slots)
        mine = jnp.concatenate([window_part, global_part] + incoming, axis=0)
        other = lax.ppermute(mine, "sub", swap)
        pieces.append((mine, other))

    own_refs = lax.dynamic_index_in_dim(per_reader, ctx_index, 0, keepdims=False)
    own_ranks = lax.dynamic_index_in_dim(slot_rank, ctx_index, 0, keepdims=False)
    own_ranks = jnp.minimum(own_ranks, capacity - 1)
    back = (ctx_index - own_refs // cache_blocks) % ctx_count
    rpos = (WIN + NG + back * capacity + own_ranks).astype(jnp.int32)

    local_order = jnp.arange(local_blocks, dtype=jnp.int32)
    global_order = ctx_index * local_blocks + local_order
    steps_back = jnp.arange(WIN, 0, -1, dtype=jnp.int32)
    back_global = global_order[:, None] - steps_back[None, :]
    cache_ids = jnp.concatenate(
        [
            jnp.broadcast_to(jnp.arange(NG, dtype=jnp.int32)[None, :], (local_blocks, NG)),
            own_refs.reshape(local_blocks, rand_count),
        ],
        axis=1,
    )
    prompt_ids = jnp.concatenate([jnp.maximum(back_global, 0), global_order[:, None]], axis=1)
    scale_row_table = jnp.concatenate(
        [jnp.take(cache_scale, cache_ids, axis=0), jnp.take(prompt_scale, prompt_ids, axis=0)],
        axis=1,
    )
    key_total = scale_row_table.shape[1]
    scale_row_table = scale_row_table.reshape(local_blocks, key_total, local_heads, 2)
    scale_row_table = jnp.transpose(scale_row_table, (0, 2, 3, 1))
    key_scale = jnp.repeat(scale_row_table[:, :, 0] / math.sqrt(head_dim), block_rows, axis=-1)
    value_scale = jnp.repeat(scale_row_table[:, :, 1], block_rows, axis=-1)
    key_scale = key_scale.reshape(local_blocks, local_heads, 1, key_total * block_rows)
    value_scale = value_scale.reshape(local_blocks, local_heads, 1, key_total * block_rows)

    meta = jnp.stack([ctx_index * local_blocks, sub_index]).astype(jnp.int32)
    qw = query_groups * head_dim
    rpos = rpos.reshape(-1)

    out = None
    for c in range(chunks):
        off = c * chunk_heads
        mine, other = pieces[c]

        def part_spec(index_fn):
            return pl.BlockSpec((1, part_rows, kvw), index_fn)

        def full_spec(index_fn):
            return pl.BlockSpec((1, block_rows, kvw), index_fn)

        slot_maps = [
            lambda g, b, rp, mt: (WIN, 0, g),
            lambda g, b, rp, mt: (WIN + 1, 0, g),
            lambda g, b, rp, mt: (rp[b * 3], 0, g),
            lambda g, b, rp, mt: (rp[b * 3 + 1], 0, g),
            lambda g, b, rp, mt: (rp[b * 3 + 2], 0, g),
            lambda g, b, rp, mt: (jnp.minimum(b, 1), 0, g),
            lambda g, b, rp, mt: (1, 0, g),
        ]
        in_specs = [
            pl.BlockSpec((1, row_count, qw), lambda g, b, rp, mt, off=off: (b, 0, g + off)),
            pl.BlockSpec((1, 1, 1, key_total * block_rows), lambda g, b, rp, mt, off=off: (b, g + off, 0, 0)),
            pl.BlockSpec((1, 1, 1, key_total * block_rows), lambda g, b, rp, mt, off=off: (b, g + off, 0, 0)),
        ]
        args = [queries, key_scale, value_scale]
        for fn in slot_maps:
            in_specs += [part_spec(fn), part_spec(fn)]
            args += [mine, other]
        in_specs += [
            full_spec(lambda g, b, rp, mt, off=off: (jnp.maximum(b - 2, 0), 0, g + off)),
            full_spec(lambda g, b, rp, mt, off=off: (jnp.maximum(b - 1, 0), 0, g + off)),
            full_spec(lambda g, b, rp, mt, off=off: (b, 0, g + off)),
        ]
        args += [prompt_key_value, prompt_key_value, prompt_key_value]
        aliases = {}
        if out is not None:
            in_specs.append(pl.BlockSpec(memory_space=pl.ANY))
            aliases = {2 + len(args): 0}
            args.append(out)
        out_spec = pl.BlockSpec((1, row_count, qw), lambda g, b, rp, mt, off=off: (b, 0, g + off))
        steps = chunk_heads * local_blocks
        call = pl.pallas_call(
            attention_kernel,
            out_shape=jax.ShapeDtypeStruct(queries.shape, queries.dtype),
            grid_spec=pltpu.PrefetchScalarGridSpec(
                num_scalar_prefetch=2,
                grid=(chunk_heads, local_blocks),
                in_specs=in_specs,
                out_specs=out_spec,
            ),
            input_output_aliases=aliases,
            cost_estimate=pl.CostEstimate(
                flops=steps * 4 * query_groups * row_count * key_total * block_rows * head_dim,
                transcendentals=steps * query_groups * row_count * key_total * block_rows,
                bytes_accessed=steps * 2 * (2 * row_count * qw + key_total * block_rows * kvw),
            ),
            compiler_params=pltpu.CompilerParams(
                dimension_semantics=("arbitrary", "arbitrary"),
                vmem_limit_bytes=48 * 1024 * 1024,
            ),
        )
        out = call(rpos, meta, *args)
    return out


def solution(mesh):
    in_specs = (
        P(("group", "ctx"), "sub", "kvh"),
        P(("group", "ctx"), None, "kvh"),
        P("group", "kvh"),
        P(("group", "ctx"), None, "kvh"),
        P("group", "kvh"),
        P("group", None),
    )
    out_specs = P(("group", "ctx"), "sub", "kvh")
    return jax.shard_map(body, mesh=mesh, in_specs=in_specs, out_specs=out_specs, check_vma=False)
```

```python
import math

import jax
import jax.numpy as jnp
from jax import lax
from jax.experimental import pallas as pl
from jax.experimental.pallas import tpu as pltpu
from jax.sharding import PartitionSpec as P

HEAD_SIZE = 128

NG = 2
WIN = 2


def passed_along(block, axis, distance):
    devices = range(lax.axis_size(axis))
    route = [(i - distance, i) for i in devices if i - distance in devices]
    return lax.ppermute(block, axis, route)


def from_root(block, axis):
    count = lax.axis_size(axis)
    index = lax.axis_index(axis)
    have = block
    reach = 1
    while reach < count:
        route = [(i, i + reach) for i in range(reach) if i + reach < count]
        got = lax.ppermute(have, axis, route)
        have = jnp.where((index >= reach) & (index < 2 * reach), got, have)
        reach *= 2
    return have


def attention_kernel(
    rpos_ref, meta_ref,
    q_ref, ks_ref, vs_ref,
    g0_ref, g1_ref, r0_ref, r1_ref, r2_ref, w5r_ref, w6r_ref,
    wl5_ref, wl6_ref, own_ref,
    o_ref,
):
    b = pl.program_id(1)
    base = meta_ref[0]
    row_off = meta_ref[1]
    rows = q_ref.shape[1]
    groups = q_ref.shape[2] // HEAD_SIZE
    block_rows = own_ref.shape[1]
    d = HEAD_SIZE

    q = q_ref[0]
    q2 = jnp.concatenate([q[:, h * d:(h + 1) * d] for h in range(groups)], axis=0)

    w5 = jnp.where(b < 2, w5r_ref[0], wl5_ref[0])
    w6 = jnp.where(b < 1, w6r_ref[0], wl6_ref[0])
    blocks = [g0_ref[0], g1_ref[0], r0_ref[0], r1_ref[0], r2_ref[0], w5, w6]
    own = own_ref[0]
    keys = jnp.concatenate([blk[:, :d] for blk in blocks], axis=0)
    vals = jnp.concatenate([blk[:, d:] for blk in blocks], axis=0)
    front = keys.shape[0]

    dims = (((1,), (1,)), ((), ()))
    ks = ks_ref[0, 0]
    vs = vs_ref[0, 0]
    col = lax.broadcasted_iota(jnp.int32, (1, front), 1)
    glob_b = base + b
    bad = ((col >= 5 * block_rows) & (col < 6 * block_rows) & (glob_b < 2)) | (
        (col >= 6 * block_rows) & (glob_b < 1)
    )
    bias = jnp.where(bad, -jnp.inf, 0.0).astype(jnp.float32)
    s_a = lax.dot_general(q2, keys, dims, preferred_element_type=jnp.float32)
    s_a = s_a * ks[:, :front] + bias
    s_b = lax.dot_general(q2, own[:, :d], dims, preferred_element_type=jnp.float32)
    s_b = s_b * ks[:, front:]
    kcol = lax.broadcasted_iota(jnp.int32, (1, block_rows), 1)
    row = lax.broadcasted_iota(jnp.int32, (groups * rows, 1), 0) % rows + row_off
    s_b = jnp.where(kcol <= row, s_b, -jnp.inf)
    m = jnp.maximum(jnp.max(s_a, axis=1, keepdims=True), jnp.max(s_b, axis=1, keepdims=True))
    p_a = jnp.exp(s_a - m)
    p_b = jnp.exp(s_b - m)
    totals = jnp.sum(p_a, axis=1, keepdims=True) + jnp.sum(p_b, axis=1, keepdims=True)
    w_a = (p_a * vs[:, :front]).astype(jnp.bfloat16)
    w_b = (p_b * vs[:, front:]).astype(jnp.bfloat16)
    pv = (((1,), (0,)), ((), ()))
    acc = lax.dot_general(w_a, vals, pv, preferred_element_type=jnp.float32)
    acc = acc + lax.dot_general(w_b, own[:, d:], pv, preferred_element_type=jnp.float32)
    res = (acc / totals).astype(o_ref.dtype)
    for h in range(groups):
        o_ref[0, :, h * d:(h + 1) * d] = res[h * rows:(h + 1) * rows]


def body(queries, cache_kv, cache_scale, prompt_key_value, prompt_scale, rand_blocks):
    ctx_count = lax.axis_size("ctx")
    ctx_index = lax.axis_index("ctx")
    sub_count = lax.axis_size("sub")
    sub_index = lax.axis_index("sub")
    local_blocks, row_count, query_width = queries.shape
    cache_blocks, block_rows, kv_width = cache_kv.shape
    head_dim = HEAD_SIZE
    kvw = 2 * head_dim
    local_heads = kv_width // kvw
    query_groups = query_width // (local_heads * head_dim)
    qw = query_groups * head_dim
    rand_count = rand_blocks.shape[1]
    capacity = max(2, (local_blocks * rand_count + ctx_count - 1) // ctx_count)
    split = sub_count == 2 and local_heads % 2 == 0
    my_heads = local_heads // 2 if split else local_heads
    head_off = sub_index * my_heads if split else jnp.int32(0)
    swap = [(0, 1), (1, 0)]

    if split:
        partner_q = lax.dynamic_slice_in_dim(
            queries, (1 - sub_index) * my_heads * qw, my_heads * qw, axis=2
        )
        partner_q = lax.ppermute(partner_q, "sub", swap)
        cache_mine = lax.dynamic_slice_in_dim(cache_kv, head_off * kvw, my_heads * kvw, axis=2)
        prompt_mine = lax.dynamic_slice_in_dim(
            prompt_key_value[local_blocks - WIN:], head_off * kvw, my_heads * kvw, axis=2
        )
    else:
        cache_mine = cache_kv
        prompt_mine = prompt_key_value[local_blocks - WIN:]

    window_part = passed_along(prompt_mine, "ctx", 1)
    global_part = from_root(cache_mine[:NG], "ctx")

    per_reader = rand_blocks.reshape(ctx_count, local_blocks * rand_count)
    owners = per_reader // cache_blocks
    owner_hot = (
        owners[:, :, None] == jnp.arange(ctx_count, dtype=jnp.int32)[None, None, :]
    ).astype(jnp.int32)
    slot_rank = jnp.sum((jnp.cumsum(owner_hot, axis=1) - 1) * owner_hot, axis=2)
    picked = (
        (owners == ctx_index)[:, :, None]
        & (slot_rank[:, :, None] == jnp.arange(capacity, dtype=jnp.int32)[None, None, :])
    ).astype(jnp.int32)
    local_ids = jnp.sum(picked * (per_reader % cache_blocks)[:, :, None], axis=1)
    outgoing = jnp.take(cache_mine, local_ids.reshape(-1), axis=0)
    incoming = lax.all_to_all(outgoing, "ctx", split_axis=0, concat_axis=0, tiled=True)
    remote = jnp.concatenate([window_part, global_part, incoming], axis=0)

    own_refs = lax.dynamic_index_in_dim(per_reader, ctx_index, 0, keepdims=False)
    own_ranks = lax.dynamic_index_in_dim(slot_rank, ctx_index, 0, keepdims=False)
    own_ranks = jnp.minimum(own_ranks, capacity - 1)
    rpos = (WIN + NG + own_refs // cache_blocks * capacity + own_ranks).astype(jnp.int32)
    rpos = rpos.reshape(-1)

    local_order = jnp.arange(local_blocks, dtype=jnp.int32)
    global_order = ctx_index * local_blocks + local_order
    steps_back = jnp.arange(WIN, 0, -1, dtype=jnp.int32)
    back_global = global_order[:, None] - steps_back[None, :]
    cache_ids = jnp.concatenate(
        [
            jnp.broadcast_to(jnp.arange(NG, dtype=jnp.int32)[None, :], (local_blocks, NG)),
            own_refs.reshape(local_blocks, rand_count),
        ],
        axis=1,
    )
    prompt_ids = jnp.concatenate([jnp.maximum(back_global, 0), global_order[:, None]], axis=1)
    scale_row_table = jnp.concatenate(
        [jnp.take(cache_scale, cache_ids, axis=0), jnp.take(prompt_scale, prompt_ids, axis=0)],
        axis=1,
    )
    key_total = scale_row_table.shape[1]
    scale_row_table = scale_row_table.reshape(local_blocks, key_total, local_heads, 2)
    scale_row_table = jnp.transpose(scale_row_table, (0, 2, 3, 1))
    key_scale = jnp.repeat(scale_row_table[:, :, 0] / math.sqrt(head_dim), block_rows, axis=-1)
    value_scale = jnp.repeat(scale_row_table[:, :, 1], block_rows, axis=-1)
    key_scale = key_scale.reshape(local_blocks, local_heads, 1, key_total * block_rows)
    value_scale = value_scale.reshape(local_blocks, local_heads, 1, key_total * block_rows)

    def run(q_array, q_head_off, row_off, out_width, out_head_off):
        meta = jnp.stack([ctx_index * local_blocks, row_off, q_head_off, head_off, out_head_off])
        meta = meta.astype(jnp.int32)

        def kv_spec(index_fn):
            return pl.BlockSpec((1, block_rows, kvw), index_fn)

        in_specs = [
            pl.BlockSpec((1, row_count, qw), lambda g, b, rp, mt: (b, 0, mt[2] + g)),
            pl.BlockSpec((1, 1, 1, key_total * block_rows), lambda g, b, rp, mt: (b, mt[3] + g, 0, 0)),
            pl.BlockSpec((1, 1, 1, key_total * block_rows), lambda g, b, rp, mt: (b, mt[3] + g, 0, 0)),
            kv_spec(lambda g, b, rp, mt: (WIN, 0, g)),
            kv_spec(lambda g, b, rp, mt: (WIN + 1, 0, g)),
            kv_spec(lambda g, b, rp, mt: (rp[b * 3], 0, g)),
            kv_spec(lambda g, b, rp, mt: (rp[b * 3 + 1], 0, g)),
            kv_spec(lambda g, b, rp, mt: (rp[b * 3 + 2], 0, g)),
            kv_spec(lambda g, b, rp, mt: (jnp.minimum(b, 1), 0, g)),
            kv_spec(lambda g, b, rp, mt: (1, 0, g)),
            kv_spec(lambda g, b, rp, mt: (jnp.maximum(b - 2, 0), 0, mt[3] + g)),
            kv_spec(lambda g, b, rp, mt: (jnp.maximum(b - 1, 0), 0, mt[3] + g)),
            kv_spec(lambda g, b, rp, mt: (b, 0, mt[3] + g)),
        ]
        steps = my_heads * local_blocks
        out_spec = pl.BlockSpec((1, row_count, qw), lambda g, b, rp, mt: (b, 0, mt[4] + g))
        call = pl.pallas_call(
            attention_kernel,
            out_shape=jax.ShapeDtypeStruct((local_blocks, row_count, out_width), queries.dtype),
            grid_spec=pltpu.PrefetchScalarGridSpec(
                num_scalar_prefetch=2,
                grid=(my_heads, local_blocks),
                in_specs=in_specs,
                out_specs=out_spec,
            ),
            cost_estimate=pl.CostEstimate(
                flops=steps * 4 * query_groups * row_count * key_total * block_rows * head_dim,
                transcendentals=steps * query_groups * row_count * key_total * block_rows,
                bytes_accessed=steps * 2 * (2 * row_count * qw + key_total * block_rows * kvw),
            ),
            compiler_params=pltpu.CompilerParams(
                dimension_semantics=("arbitrary", "arbitrary"),
                vmem_limit_bytes=48 * 1024 * 1024,
            ),
        )
        return call(
            rpos, meta, q_array, key_scale, value_scale,
            remote, remote, remote, remote, remote, remote, remote,
            prompt_key_value, prompt_key_value, prompt_key_value,
        )

    if not split:
        return run(queries, jnp.int32(0), sub_index * row_count, query_width, jnp.int32(0))
    for_partner = run(partner_q, jnp.int32(0), (1 - sub_index) * row_count, my_heads * qw, jnp.int32(0))
    from_partner = lax.ppermute(for_partner, "sub", swap)
    mine = run(queries, head_off, sub_index * row_count, query_width, head_off)
    return lax.dynamic_update_slice_in_dim(mine, from_partner, (1 - sub_index) * my_heads * qw, axis=2)


def solution(mesh):
    in_specs = (
        P(("group", "ctx"), "sub", "kvh"),
        P(("group", "ctx"), None, "kvh"),
        P("group", "kvh"),
        P(("group", "ctx"), None, "kvh"),
        P("group", "kvh"),
        P("group", None),
    )
    out_specs = P(("group", "ctx"), "sub", "kvh")
    return jax.shard_map(body, mesh=mesh, in_specs=in_specs, out_specs=out_specs, check_vma=False)
```

```python
import math

import jax
import jax.numpy as jnp
from jax import lax
from jax.experimental import pallas as pl
from jax.experimental.pallas import tpu as pltpu
from jax.sharding import PartitionSpec as P

HEAD_SIZE = 128

NG = 2
WIN = 2


def passed_along(block, axis, distance):
    devices = range(lax.axis_size(axis))
    route = [(i - distance, i) for i in devices if i - distance in devices]
    return lax.ppermute(block, axis, route)


def from_root(block, axis):
    count = lax.axis_size(axis)
    index = lax.axis_index(axis)
    have = block
    reach = 1
    while reach < count:
        route = [(i, i + reach) for i in range(reach) if i + reach < count]
        got = lax.ppermute(have, axis, route)
        have = jnp.where((index >= reach) & (index < 2 * reach), got, have)
        reach *= 2
    return have


def attention_kernel(
    rpos_ref, meta_ref,
    q_ref, ks_ref, vs_ref,
    g0_ref, g1_ref, r0_ref, r1_ref, r2_ref, w5r_ref, w6r_ref,
    wl5_ref, wl6_ref, own_ref,
    o_ref,
):
    b = pl.program_id(1)
    base = meta_ref[0]
    row_off = meta_ref[1]
    rows = q_ref.shape[1]
    groups = q_ref.shape[2] // HEAD_SIZE
    block_rows = own_ref.shape[1]
    d = HEAD_SIZE

    q = q_ref[0]
    q2 = jnp.concatenate([q[:, h * d:(h + 1) * d] for h in range(groups)], axis=0)

    w5 = jnp.where(b < 2, w5r_ref[0], wl5_ref[0])
    w6 = jnp.where(b < 1, w6r_ref[0], wl6_ref[0])
    blocks = [g0_ref[0], g1_ref[0], r0_ref[0], r1_ref[0], r2_ref[0], w5, w6]
    own = own_ref[0]
    keys = jnp.concatenate([blk[:, :d] for blk in blocks], axis=0)
    vals = jnp.concatenate([blk[:, d:] for blk in blocks], axis=0)
    front = keys.shape[0]

    dims = (((1,), (1,)), ((), ()))
    ks = ks_ref[0, 0]
    vs = vs_ref[0, 0]
    col = lax.broadcasted_iota(jnp.int32, (1, front), 1)
    glob_b = base + b
    bad = ((col >= 5 * block_rows) & (col < 6 * block_rows) & (glob_b < 2)) | (
        (col >= 6 * block_rows) & (glob_b < 1)
    )
    bias = jnp.where(bad, -jnp.inf, 0.0).astype(jnp.float32)
    s_a = lax.dot_general(q2, keys, dims, preferred_element_type=jnp.float32)
    s_a = lax.cond(
        glob_b < 2,
        lambda x: x * ks[:, :front] + bias,
        lambda x: x * ks[:, :front],
        s_a,
    )
    s_b = lax.dot_general(q2, own[:, :d], dims, preferred_element_type=jnp.float32)
    s_b = s_b * ks[:, front:]
    kcol = lax.broadcasted_iota(jnp.int32, (1, block_rows), 1)
    row = lax.broadcasted_iota(jnp.int32, (groups * rows, 1), 0) % rows + row_off
    s_b = jnp.where(kcol <= row, s_b, -jnp.inf)
    m = jnp.maximum(jnp.max(s_a, axis=1, keepdims=True), jnp.max(s_b, axis=1, keepdims=True))
    p_a = jnp.exp(s_a - m)
    p_b = jnp.exp(s_b - m)
    totals = jnp.sum(p_a, axis=1, keepdims=True) + jnp.sum(p_b, axis=1, keepdims=True)
    w_a = (p_a * vs[:, :front]).astype(jnp.bfloat16)
    w_b = (p_b * vs[:, front:]).astype(jnp.bfloat16)
    pv = (((1,), (0,)), ((), ()))
    acc = lax.dot_general(w_a, vals, pv, preferred_element_type=jnp.float32)
    acc = acc + lax.dot_general(w_b, own[:, d:], pv, preferred_element_type=jnp.float32)
    res = (acc / totals).astype(o_ref.dtype)
    for h in range(groups):
        o_ref[0, :, h * d:(h + 1) * d] = res[h * rows:(h + 1) * rows]


def body(queries, cache_kv, cache_scale, prompt_key_value, prompt_scale, rand_blocks):
    ctx_count = lax.axis_size("ctx")
    ctx_index = lax.axis_index("ctx")
    sub_count = lax.axis_size("sub")
    sub_index = lax.axis_index("sub")
    local_blocks, row_count, query_width = queries.shape
    cache_blocks, block_rows, kv_width = cache_kv.shape
    head_dim = HEAD_SIZE
    kvw = 2 * head_dim
    local_heads = kv_width // kvw
    query_groups = query_width // (local_heads * head_dim)
    qw = query_groups * head_dim
    rand_count = rand_blocks.shape[1]
    capacity = max(2, (local_blocks * rand_count + ctx_count - 1) // ctx_count)
    split = sub_count == 2 and local_heads % 2 == 0
    my_heads = local_heads // 2 if split else local_heads
    head_off = sub_index * my_heads if split else jnp.int32(0)
    swap = [(0, 1), (1, 0)]

    if split:
        partner_q = lax.dynamic_slice_in_dim(
            queries, (1 - sub_index) * my_heads * qw, my_heads * qw, axis=2
        )
        partner_q = lax.ppermute(partner_q, "sub", swap)
        cache_mine = None
        prompt_mine = lax.dynamic_slice_in_dim(
            prompt_key_value[local_blocks - WIN:], head_off * kvw, my_heads * kvw, axis=2
        )
    else:
        cache_mine = cache_kv
        prompt_mine = prompt_key_value[local_blocks - WIN:]

    def cache_rows(ids):
        if cache_mine is not None:
            return jnp.take(cache_mine, ids, axis=0)
        starts = jnp.stack(
            [ids, jnp.zeros_like(ids), jnp.full_like(ids, head_off * kvw)], axis=1
        )
        numbers = lax.GatherDimensionNumbers(
            offset_dims=(1, 2), collapsed_slice_dims=(0,), start_index_map=(0, 1, 2)
        )
        return lax.gather(
            cache_kv, starts, numbers, (1, block_rows, my_heads * kvw),
            mode=lax.GatherScatterMode.PROMISE_IN_BOUNDS,
        )

    window_part = passed_along(prompt_mine, "ctx", 1)
    global_part = from_root(cache_rows(jnp.arange(NG, dtype=jnp.int32)), "ctx")

    per_reader = rand_blocks.reshape(ctx_count, local_blocks * rand_count)
    owners = per_reader // cache_blocks
    owner_hot = (
        owners[:, :, None] == jnp.arange(ctx_count, dtype=jnp.int32)[None, None, :]
    ).astype(jnp.int32)
    slot_rank = jnp.sum((jnp.cumsum(owner_hot, axis=1) - 1) * owner_hot, axis=2)
    picked = (
        (owners == ctx_index)[:, :, None]
        & (slot_rank[:, :, None] == jnp.arange(capacity, dtype=jnp.int32)[None, None, :])
    ).astype(jnp.int32)
    local_ids = jnp.sum(picked * (per_reader % cache_blocks)[:, :, None], axis=1)
    outgoing = cache_rows(local_ids.reshape(-1).astype(jnp.int32))
    incoming = lax.all_to_all(outgoing, "ctx", split_axis=0, concat_axis=0, tiled=True)

    own_refs = lax.dynamic_index_in_dim(per_reader, ctx_index, 0, keepdims=False)
    own_ranks = lax.dynamic_index_in_dim(slot_rank, ctx_index, 0, keepdims=False)
    own_ranks = jnp.minimum(own_ranks, capacity - 1)
    rpos = (own_refs // cache_blocks * capacity + own_ranks).astype(jnp.int32)
    rpos = rpos.reshape(-1)

    local_order = jnp.arange(local_blocks, dtype=jnp.int32)
    global_order = ctx_index * local_blocks + local_order
    steps_back = jnp.arange(WIN, 0, -1, dtype=jnp.int32)
    back_global = global_order[:, None] - steps_back[None, :]
    cache_ids = jnp.concatenate(
        [
            jnp.broadcast_to(jnp.arange(NG, dtype=jnp.int32)[None, :], (local_blocks, NG)),
            own_refs.reshape(local_blocks, rand_count),
        ],
        axis=1,
    )
    prompt_ids = jnp.concatenate([jnp.maximum(back_global, 0), global_order[:, None]], axis=1)
    scale_row_table = jnp.concatenate(
        [jnp.take(cache_scale, cache_ids, axis=0), jnp.take(prompt_scale, prompt_ids, axis=0)],
        axis=1,
    )
    key_total = scale_row_table.shape[1]
    scale_row_table = scale_row_table.reshape(local_blocks, key_total, local_heads, 2)
    scale_row_table = jnp.transpose(scale_row_table, (0, 2, 3, 1))
    key_scale = jnp.repeat(scale_row_table[:, :, 0] / math.sqrt(head_dim), block_rows, axis=-1)
    value_scale = jnp.repeat(scale_row_table[:, :, 1], block_rows, axis=-1)
    key_scale = key_scale.reshape(local_blocks, local_heads, 1, key_total * block_rows)
    value_scale = value_scale.reshape(local_blocks, local_heads, 1, key_total * block_rows)

    def run(q_array, q_head_off, row_off, out_width, out_head_off):
        meta = jnp.stack([ctx_index * local_blocks, row_off, q_head_off, head_off, out_head_off])
        meta = meta.astype(jnp.int32)

        def kv_spec(index_fn):
            return pl.BlockSpec((1, block_rows, kvw), index_fn)

        in_specs = [
            pl.BlockSpec((1, row_count, qw), lambda g, b, rp, mt: (b, 0, mt[2] + g)),
            pl.BlockSpec((1, 1, 1, key_total * block_rows), lambda g, b, rp, mt: (b, mt[3] + g, 0, 0)),
            pl.BlockSpec((1, 1, 1, key_total * block_rows), lambda g, b, rp, mt: (b, mt[3] + g, 0, 0)),
            kv_spec(lambda g, b, rp, mt: (0, 0, g)),
            kv_spec(lambda g, b, rp, mt: (1, 0, g)),
            kv_spec(lambda g, b, rp, mt: (rp[b * 3], 0, g)),
            kv_spec(lambda g, b, rp, mt: (rp[b * 3 + 1], 0, g)),
            kv_spec(lambda g, b, rp, mt: (rp[b * 3 + 2], 0, g)),
            kv_spec(lambda g, b, rp, mt: (jnp.minimum(b, 1), 0, g)),
            kv_spec(lambda g, b, rp, mt: (1, 0, g)),
            kv_spec(lambda g, b, rp, mt: (jnp.maximum(b - 2, 0), 0, mt[3] + g)),
            kv_spec(lambda g, b, rp, mt: (jnp.maximum(b - 1, 0), 0, mt[3] + g)),
            kv_spec(lambda g, b, rp, mt: (b, 0, mt[3] + g)),
        ]
        steps = my_heads * local_blocks
        out_spec = pl.BlockSpec((1, row_count, qw), lambda g, b, rp, mt: (b, 0, mt[4] + g))
        call = pl.pallas_call(
            attention_kernel,
            out_shape=jax.ShapeDtypeStruct((local_blocks, row_count, out_width), queries.dtype),
            grid_spec=pltpu.PrefetchScalarGridSpec(
                num_scalar_prefetch=2,
                grid=(my_heads, local_blocks),
                in_specs=in_specs,
                out_specs=out_spec,
            ),
            cost_estimate=pl.CostEstimate(
                flops=steps * 4 * query_groups * row_count * key_total * block_rows * head_dim,
                transcendentals=steps * query_groups * row_count * key_total * block_rows,
                bytes_accessed=steps * 2 * (2 * row_count * qw + key_total * block_rows * kvw),
            ),
            compiler_params=pltpu.CompilerParams(
                dimension_semantics=("arbitrary", "arbitrary"),
                vmem_limit_bytes=48 * 1024 * 1024,
            ),
        )
        return call(
            rpos, meta, q_array, key_scale, value_scale,
            global_part, global_part, incoming, incoming, incoming, window_part, window_part,
            prompt_key_value, prompt_key_value, prompt_key_value,
        )

    if not split:
        return run(queries, jnp.int32(0), sub_index * row_count, query_width, jnp.int32(0))
    for_partner = run(partner_q, jnp.int32(0), (1 - sub_index) * row_count, my_heads * qw, jnp.int32(0))
    from_partner = lax.ppermute(for_partner, "sub", swap)
    mine = run(queries, head_off, sub_index * row_count, query_width, head_off)
    return lax.dynamic_update_slice_in_dim(mine, from_partner, (1 - sub_index) * my_heads * qw, axis=2)


def solution(mesh):
    in_specs = (
        P(("group", "ctx"), "sub", "kvh"),
        P(("group", "ctx"), None, "kvh"),
        P("group", "kvh"),
        P(("group", "ctx"), None, "kvh"),
        P("group", "kvh"),
        P("group", None),
    )
    out_specs = P(("group", "ctx"), "sub", "kvh")
    return jax.shard_map(body, mesh=mesh, in_specs=in_specs, out_specs=out_specs, check_vma=False)
```

```python
import math

import jax
import jax.numpy as jnp
from jax import lax
from jax.experimental import pallas as pl
from jax.experimental.pallas import tpu as pltpu
from jax.sharding import PartitionSpec as P

HEAD_SIZE = 128

NG = 2
WIN = 2


def passed_along(block, axis, distance):
    devices = range(lax.axis_size(axis))
    route = [(i - distance, i) for i in devices if i - distance in devices]
    return lax.ppermute(block, axis, route)


def from_root(block, axis):
    count = lax.axis_size(axis)
    index = lax.axis_index(axis)
    have = block
    reach = 1
    while reach < count:
        route = [(i, i + reach) for i in range(reach) if i + reach < count]
        got = lax.ppermute(have, axis, route)
        have = jnp.where((index >= reach) & (index < 2 * reach), got, have)
        reach *= 2
    return have


def attention_kernel(
    rpos_ref, meta_ref,
    q_ref, ks_ref, vs_ref,
    g0_ref, g1_ref, r0_ref, r1_ref, r2_ref, w5r_ref, w6r_ref,
    wl5_ref, wl6_ref, own_ref,
    o_ref,
):
    b = pl.program_id(1)
    base = meta_ref[0]
    row_off = meta_ref[1]
    rows = q_ref.shape[1]
    groups = q_ref.shape[2] // HEAD_SIZE
    block_rows = own_ref.shape[1]
    d = HEAD_SIZE

    q = q_ref[0]
    q2 = jnp.concatenate([q[:, h * d:(h + 1) * d] for h in range(groups)], axis=0)

    w5 = jnp.where(b < 2, w5r_ref[0], wl5_ref[0])
    w6 = jnp.where(b < 1, w6r_ref[0], wl6_ref[0])
    blocks = [g0_ref[0], g1_ref[0], r0_ref[0], r1_ref[0], r2_ref[0], w5, w6]
    own = own_ref[0]
    keys = jnp.concatenate([blk[:, :d] for blk in blocks], axis=0)
    vals = jnp.concatenate([blk[:, d:] for blk in blocks], axis=0)
    front = keys.shape[0]

    dims = (((1,), (1,)), ((), ()))
    pv = (((1,), (0,)), ((), ()))
    glob_b = base + b

    def compute(masked):
        ks = ks_ref[0, 0]
        vs = vs_ref[0, 0]
        s_a = lax.dot_general(q2, keys, dims, preferred_element_type=jnp.float32)
        s_a = s_a * ks[:, :front]
        if masked:
            col = lax.broadcasted_iota(jnp.int32, (1, front), 1)
            bad = ((col >= 5 * block_rows) & (col < 6 * block_rows) & (glob_b < 2)) | (
                (col >= 6 * block_rows) & (glob_b < 1)
            )
            s_a = jnp.where(bad, -jnp.inf, s_a)
        s_b = lax.dot_general(q2, own[:, :d], dims, preferred_element_type=jnp.float32)
        s_b = s_b * ks[:, front:]
        kcol = lax.broadcasted_iota(jnp.int32, (1, block_rows), 1)
        row = lax.broadcasted_iota(jnp.int32, (groups * rows, 1), 0) % rows + row_off
        s_b = jnp.where(kcol <= row, s_b, -jnp.inf)
        m = jnp.maximum(jnp.max(s_a, axis=1, keepdims=True), jnp.max(s_b, axis=1, keepdims=True))
        p_a = jnp.exp2(s_a - m)
        p_b = jnp.exp2(s_b - m)
        totals = jnp.sum(p_a, axis=1, keepdims=True) + jnp.sum(p_b, axis=1, keepdims=True)
        w_a = (p_a * vs[:, :front]).astype(jnp.bfloat16)
        w_b = (p_b * vs[:, front:]).astype(jnp.bfloat16)
        acc = lax.dot_general(w_a, vals, pv, preferred_element_type=jnp.float32)
        acc = acc + lax.dot_general(w_b, own[:, d:], pv, preferred_element_type=jnp.float32)
        res = (acc / totals).astype(o_ref.dtype)
        for h in range(groups):
            o_ref[0, :, h * d:(h + 1) * d] = res[h * rows:(h + 1) * rows]

    @pl.when(glob_b < 2)
    def _():
        compute(True)

    @pl.when(glob_b >= 2)
    def _():
        compute(False)


def body(queries, cache_kv, cache_scale, prompt_key_value, prompt_scale, rand_blocks):
    ctx_count = lax.axis_size("ctx")
    ctx_index = lax.axis_index("ctx")
    sub_count = lax.axis_size("sub")
    sub_index = lax.axis_index("sub")
    local_blocks, row_count, query_width = queries.shape
    cache_blocks, block_rows, kv_width = cache_kv.shape
    head_dim = HEAD_SIZE
    kvw = 2 * head_dim
    local_heads = kv_width // kvw
    query_groups = query_width // (local_heads * head_dim)
    qw = query_groups * head_dim
    rand_count = rand_blocks.shape[1]
    capacity = max(2, (local_blocks * rand_count + ctx_count - 1) // ctx_count)
    split = sub_count == 2 and local_heads % 2 == 0
    my_heads = local_heads // 2 if split else local_heads
    head_off = sub_index * my_heads if split else jnp.int32(0)
    swap = [(0, 1), (1, 0)]

    if split:
        partner_q = lax.dynamic_slice_in_dim(
            queries, (1 - sub_index) * my_heads * qw, my_heads * qw, axis=2
        )
        partner_q = lax.ppermute(partner_q, "sub", swap)
        cache_mine = lax.dynamic_slice_in_dim(cache_kv, head_off * kvw, my_heads * kvw, axis=2)
        prompt_mine = lax.dynamic_slice_in_dim(
            prompt_key_value[local_blocks - WIN:], head_off * kvw, my_heads * kvw, axis=2
        )
    else:
        cache_mine = cache_kv
        prompt_mine = prompt_key_value[local_blocks - WIN:]

    window_part = passed_along(prompt_mine, "ctx", 1)
    global_part = from_root(cache_mine[:NG], "ctx")

    per_reader = rand_blocks.reshape(ctx_count, local_blocks * rand_count)
    owners = per_reader // cache_blocks
    owner_hot = (
        owners[:, :, None] == jnp.arange(ctx_count, dtype=jnp.int32)[None, None, :]
    ).astype(jnp.int32)
    slot_rank = jnp.sum((jnp.cumsum(owner_hot, axis=1) - 1) * owner_hot, axis=2)
    picked = (
        (owners == ctx_index)[:, :, None]
        & (slot_rank[:, :, None] == jnp.arange(capacity, dtype=jnp.int32)[None, None, :])
    ).astype(jnp.int32)
    local_ids = jnp.sum(picked * (per_reader % cache_blocks)[:, :, None], axis=1)
    outgoing = jnp.take(cache_mine, local_ids.reshape(-1), axis=0)
    incoming = lax.all_to_all(outgoing, "ctx", split_axis=0, concat_axis=0, tiled=True)

    own_refs = lax.dynamic_index_in_dim(per_reader, ctx_index, 0, keepdims=False)
    own_ranks = lax.dynamic_index_in_dim(slot_rank, ctx_index, 0, keepdims=False)
    own_ranks = jnp.minimum(own_ranks, capacity - 1)
    rpos = (own_refs // cache_blocks * capacity + own_ranks).astype(jnp.int32)
    rpos = rpos.reshape(-1)

    local_order = jnp.arange(local_blocks, dtype=jnp.int32)
    global_order = ctx_index * local_blocks + local_order
    steps_back = jnp.arange(WIN, 0, -1, dtype=jnp.int32)
    back_global = global_order[:, None] - steps_back[None, :]
    cache_ids = jnp.concatenate(
        [
            jnp.broadcast_to(jnp.arange(NG, dtype=jnp.int32)[None, :], (local_blocks, NG)),
            own_refs.reshape(local_blocks, rand_count),
        ],
        axis=1,
    )
    prompt_ids = jnp.concatenate([jnp.maximum(back_global, 0), global_order[:, None]], axis=1)
    scale_row_table = jnp.concatenate(
        [jnp.take(cache_scale, cache_ids, axis=0), jnp.take(prompt_scale, prompt_ids, axis=0)],
        axis=1,
    )
    key_total = scale_row_table.shape[1]
    scale_row_table = scale_row_table.reshape(local_blocks, key_total, local_heads, 2)
    scale_row_table = jnp.transpose(scale_row_table, (0, 2, 3, 1))
    key_scale = scale_row_table[:, :, 0] / math.sqrt(head_dim) * math.log2(math.e)
    key_scale = jnp.repeat(key_scale, block_rows, axis=-1)
    value_scale = jnp.repeat(scale_row_table[:, :, 1], block_rows, axis=-1)
    key_scale = key_scale.reshape(local_blocks, local_heads, 1, key_total * block_rows)
    value_scale = value_scale.reshape(local_blocks, local_heads, 1, key_total * block_rows)

    def run(q_array, q_head_off, row_off, out_width, out_head_off):
        meta = jnp.stack([ctx_index * local_blocks, row_off, q_head_off, head_off, out_head_off])
        meta = meta.astype(jnp.int32)

        def kv_spec(index_fn):
            return pl.BlockSpec((1, block_rows, kvw), index_fn)

        in_specs = [
            pl.BlockSpec((1, row_count, qw), lambda g, b, rp, mt: (b, 0, mt[2] + g)),
            pl.BlockSpec((1, 1, 1, key_total * block_rows), lambda g, b, rp, mt: (b, mt[3] + g, 0, 0)),
            pl.BlockSpec((1, 1, 1, key_total * block_rows), lambda g, b, rp, mt: (b, mt[3] + g, 0, 0)),
            kv_spec(lambda g, b, rp, mt: (0, 0, g)),
            kv_spec(lambda g, b, rp, mt: (1, 0, g)),
            kv_spec(lambda g, b, rp, mt: (rp[b * 3], 0, g)),
            kv_spec(lambda g, b, rp, mt: (rp[b * 3 + 1], 0, g)),
            kv_spec(lambda g, b, rp, mt: (rp[b * 3 + 2], 0, g)),
            kv_spec(lambda g, b, rp, mt: (jnp.minimum(b, 1), 0, g)),
            kv_spec(lambda g, b, rp, mt: (1, 0, g)),
            kv_spec(lambda g, b, rp, mt: (jnp.maximum(b - 2, 0), 0, mt[3] + g)),
            kv_spec(lambda g, b, rp, mt: (jnp.maximum(b - 1, 0), 0, mt[3] + g)),
            kv_spec(lambda g, b, rp, mt: (b, 0, mt[3] + g)),
        ]
        steps = my_heads * local_blocks
        out_spec = pl.BlockSpec((1, row_count, qw), lambda g, b, rp, mt: (b, 0, mt[4] + g))
        call = pl.pallas_call(
            attention_kernel,
            out_shape=jax.ShapeDtypeStruct((local_blocks, row_count, out_width), queries.dtype),
            grid_spec=pltpu.PrefetchScalarGridSpec(
                num_scalar_prefetch=2,
                grid=(my_heads, local_blocks),
                in_specs=in_specs,
                out_specs=out_spec,
            ),
            cost_estimate=pl.CostEstimate(
                flops=steps * 4 * query_groups * row_count * key_total * block_rows * head_dim,
                transcendentals=steps * query_groups * row_count * key_total * block_rows,
                bytes_accessed=steps * 2 * (2 * row_count * qw + key_total * block_rows * kvw),
            ),
            compiler_params=pltpu.CompilerParams(
                dimension_semantics=("arbitrary", "arbitrary"),
                vmem_limit_bytes=48 * 1024 * 1024,
            ),
        )
        return call(
            rpos, meta, q_array, key_scale, value_scale,
            global_part, global_part, incoming, incoming, incoming, window_part, window_part,
            prompt_key_value, prompt_key_value, prompt_key_value,
        )

    if not split:
        return run(queries, jnp.int32(0), sub_index * row_count, query_width, jnp.int32(0))
    for_partner = run(partner_q, jnp.int32(0), (1 - sub_index) * row_count, my_heads * qw, jnp.int32(0))
    from_partner = lax.ppermute(for_partner, "sub", swap)
    mine = run(queries, head_off, sub_index * row_count, query_width, head_off)
    return lax.dynamic_update_slice_in_dim(mine, from_partner, (1 - sub_index) * my_heads * qw, axis=2)


def solution(mesh):
    in_specs = (
        P(("group", "ctx"), "sub", "kvh"),
        P(("group", "ctx"), None, "kvh"),
        P("group", "kvh"),
        P(("group", "ctx"), None, "kvh"),
        P("group", "kvh"),
        P("group", None),
    )
    out_specs = P(("group", "ctx"), "sub", "kvh")
    return jax.shard_map(body, mesh=mesh, in_specs=in_specs, out_specs=out_specs, check_vma=False)
```

```python
import math

import jax
import jax.numpy as jnp
from jax import lax
from jax.experimental import pallas as pl
from jax.experimental.pallas import tpu as pltpu
from jax.sharding import PartitionSpec as P

HEAD_SIZE = 128

NG = 2
WIN = 2


def passed_along(block, axis, distance):
    devices = range(lax.axis_size(axis))
    route = [(i - distance, i) for i in devices if i - distance in devices]
    return lax.ppermute(block, axis, route)


def from_root(block, axis):
    count = lax.axis_size(axis)
    index = lax.axis_index(axis)
    have = block
    reach = 1
    while reach < count:
        route = [(i, i + reach) for i in range(reach) if i + reach < count]
        got = lax.ppermute(have, axis, route)
        have = jnp.where((index >= reach) & (index < 2 * reach), got, have)
        reach *= 2
    return have


def attention_kernel(
    rpos_ref, meta_ref,
    q_ref, ks_ref, vs_ref,
    g0_ref, g1_ref, r0_ref, r1_ref, r2_ref, w5r_ref, w6r_ref,
    wl5_ref, wl6_ref, own_ref, *rest,
):
    o_ref = rest[-1]
    b = pl.program_id(1)
    base = meta_ref[0]
    row_off = meta_ref[1]
    rows = q_ref.shape[1]
    groups = q_ref.shape[2] // HEAD_SIZE
    block_rows = own_ref.shape[1]
    d = HEAD_SIZE

    q = q_ref[0]
    q2 = jnp.concatenate([q[:, h * d:(h + 1) * d] for h in range(groups)], axis=0)

    w5 = jnp.where(b < 2, w5r_ref[0], wl5_ref[0])
    w6 = jnp.where(b < 1, w6r_ref[0], wl6_ref[0])
    blocks = [g0_ref[0], g1_ref[0], r0_ref[0], r1_ref[0], r2_ref[0], w5, w6]
    own = own_ref[0]
    keys = jnp.concatenate([blk[:, :d] for blk in blocks], axis=0)
    vals = jnp.concatenate([blk[:, d:] for blk in blocks], axis=0)
    front = keys.shape[0]

    dims = (((1,), (1,)), ((), ()))
    pv = (((1,), (0,)), ((), ()))
    glob_b = base + b

    def compute(masked):
        ks = ks_ref[0, 0]
        vs = vs_ref[0, 0]
        s_a = lax.dot_general(q2, keys, dims, preferred_element_type=jnp.float32)
        s_a = s_a * ks[:, :front]
        if masked:
            col = lax.broadcasted_iota(jnp.int32, (1, front), 1)
            bad = ((col >= 5 * block_rows) & (col < 6 * block_rows) & (glob_b < 2)) | (
                (col >= 6 * block_rows) & (glob_b < 1)
            )
            s_a = jnp.where(bad, -jnp.inf, s_a)
        s_b = lax.dot_general(q2, own[:, :d], dims, preferred_element_type=jnp.float32)
        s_b = s_b * ks[:, front:]
        kcol = lax.broadcasted_iota(jnp.int32, (1, block_rows), 1)
        row = lax.broadcasted_iota(jnp.int32, (groups * rows, 1), 0) % rows + row_off
        s_b = jnp.where(kcol <= row, s_b, -jnp.inf)
        m = jnp.maximum(jnp.max(s_a, axis=1, keepdims=True), jnp.max(s_b, axis=1, keepdims=True))
        p_a = jnp.exp2(s_a - m)
        p_b = jnp.exp2(s_b - m)
        totals = jnp.sum(p_a, axis=1, keepdims=True) + jnp.sum(p_b, axis=1, keepdims=True)
        w_a = (p_a * vs[:, :front]).astype(jnp.bfloat16)
        w_b = (p_b * vs[:, front:]).astype(jnp.bfloat16)
        acc = lax.dot_general(w_a, vals, pv, preferred_element_type=jnp.float32)
        acc = acc + lax.dot_general(w_b, own[:, d:], pv, preferred_element_type=jnp.float32)
        res = (acc / totals).astype(o_ref.dtype)
        for h in range(groups):
            o_ref[0, :, h * d:(h + 1) * d] = res[h * rows:(h + 1) * rows]

    @pl.when(glob_b < 2)
    def _():
        compute(True)

    @pl.when(glob_b >= 2)
    def _():
        compute(False)


def body(queries, cache_kv, cache_scale, prompt_key_value, prompt_scale, rand_blocks):
    ctx_count = lax.axis_size("ctx")
    ctx_index = lax.axis_index("ctx")
    sub_count = lax.axis_size("sub")
    sub_index = lax.axis_index("sub")
    local_blocks, row_count, query_width = queries.shape
    cache_blocks, block_rows, kv_width = cache_kv.shape
    head_dim = HEAD_SIZE
    kvw = 2 * head_dim
    local_heads = kv_width // kvw
    query_groups = query_width // (local_heads * head_dim)
    qw = query_groups * head_dim
    rand_count = rand_blocks.shape[1]
    capacity = max(2, (local_blocks * rand_count + ctx_count - 1) // ctx_count)
    split = sub_count == 2 and local_heads % 2 == 0
    my_heads = local_heads // 2 if split else local_heads
    head_off = sub_index * my_heads if split else jnp.int32(0)
    swap = [(0, 1), (1, 0)]

    if split:
        partner_q = lax.dynamic_slice_in_dim(
            queries, (1 - sub_index) * my_heads * qw, my_heads * qw, axis=2
        )
        partner_q = lax.ppermute(partner_q, "sub", swap)
        cache_mine = lax.dynamic_slice_in_dim(cache_kv, head_off * kvw, my_heads * kvw, axis=2)
        prompt_mine = lax.dynamic_slice_in_dim(
            prompt_key_value[local_blocks - WIN:], head_off * kvw, my_heads * kvw, axis=2
        )
    else:
        cache_mine = cache_kv
        prompt_mine = prompt_key_value[local_blocks - WIN:]

    window_part = passed_along(prompt_mine, "ctx", 1)
    global_part = from_root(cache_mine[:NG], "ctx")

    per_reader = rand_blocks.reshape(ctx_count, local_blocks * rand_count)
    owners = per_reader // cache_blocks
    owner_hot = (
        owners[:, :, None] == jnp.arange(ctx_count, dtype=jnp.int32)[None, None, :]
    ).astype(jnp.int32)
    slot_rank = jnp.sum((jnp.cumsum(owner_hot, axis=1) - 1) * owner_hot, axis=2)
    picked = (
        (owners == ctx_index)[:, :, None]
        & (slot_rank[:, :, None] == jnp.arange(capacity, dtype=jnp.int32)[None, None, :])
    ).astype(jnp.int32)
    local_ids = jnp.sum(picked * (per_reader % cache_blocks)[:, :, None], axis=1)
    outgoing = jnp.take(cache_mine, local_ids.reshape(-1), axis=0)
    chunks = 2 if my_heads % 2 == 0 else 1
    chunk_heads = my_heads // chunks
    chunk_width = chunk_heads * kvw
    incoming = []
    for c in range(chunks):
        piece = outgoing[:, :, c * chunk_width:(c + 1) * chunk_width]
        if incoming:
            piece, _ = lax.optimization_barrier((piece, incoming[-1]))
        incoming.append(lax.all_to_all(piece, "ctx", split_axis=0, concat_axis=0, tiled=True))

    own_refs = lax.dynamic_index_in_dim(per_reader, ctx_index, 0, keepdims=False)
    own_ranks = lax.dynamic_index_in_dim(slot_rank, ctx_index, 0, keepdims=False)
    own_ranks = jnp.minimum(own_ranks, capacity - 1)
    rpos = (own_refs // cache_blocks * capacity + own_ranks).astype(jnp.int32)
    rpos = rpos.reshape(-1)

    local_order = jnp.arange(local_blocks, dtype=jnp.int32)
    global_order = ctx_index * local_blocks + local_order
    steps_back = jnp.arange(WIN, 0, -1, dtype=jnp.int32)
    back_global = global_order[:, None] - steps_back[None, :]
    cache_ids = jnp.concatenate(
        [
            jnp.broadcast_to(jnp.arange(NG, dtype=jnp.int32)[None, :], (local_blocks, NG)),
            own_refs.reshape(local_blocks, rand_count),
        ],
        axis=1,
    )
    prompt_ids = jnp.concatenate([jnp.maximum(back_global, 0), global_order[:, None]], axis=1)
    scale_row_table = jnp.concatenate(
        [jnp.take(cache_scale, cache_ids, axis=0), jnp.take(prompt_scale, prompt_ids, axis=0)],
        axis=1,
    )
    key_total = scale_row_table.shape[1]
    scale_row_table = scale_row_table.reshape(local_blocks, key_total, local_heads, 2)
    scale_row_table = jnp.transpose(scale_row_table, (0, 2, 3, 1))
    key_scale = scale_row_table[:, :, 0] / math.sqrt(head_dim) * math.log2(math.e)
    key_scale = jnp.repeat(key_scale, block_rows, axis=-1)
    value_scale = jnp.repeat(scale_row_table[:, :, 1], block_rows, axis=-1)
    key_scale = key_scale.reshape(local_blocks, local_heads, 1, key_total * block_rows)
    value_scale = value_scale.reshape(local_blocks, local_heads, 1, key_total * block_rows)

    def run(q_array, q_head_off, row_off, out_width, out_head_off, c, prev):
        c_off = c * chunk_heads
        meta = jnp.stack(
            [ctx_index * local_blocks, row_off, q_head_off + c_off, head_off + c_off,
             out_head_off + c_off, jnp.int32(c_off)]
        )
        meta = meta.astype(jnp.int32)

        def kv_spec(index_fn):
            return pl.BlockSpec((1, block_rows, kvw), index_fn)

        in_specs = [
            pl.BlockSpec((1, row_count, qw), lambda g, b, rp, mt: (b, 0, mt[2] + g)),
            pl.BlockSpec((1, 1, 1, key_total * block_rows), lambda g, b, rp, mt: (b, mt[3] + g, 0, 0)),
            pl.BlockSpec((1, 1, 1, key_total * block_rows), lambda g, b, rp, mt: (b, mt[3] + g, 0, 0)),
            kv_spec(lambda g, b, rp, mt: (0, 0, mt[5] + g)),
            kv_spec(lambda g, b, rp, mt: (1, 0, mt[5] + g)),
            kv_spec(lambda g, b, rp, mt: (rp[b * 3], 0, g)),
            kv_spec(lambda g, b, rp, mt: (rp[b * 3 + 1], 0, g)),
            kv_spec(lambda g, b, rp, mt: (rp[b * 3 + 2], 0, g)),
            kv_spec(lambda g, b, rp, mt: (jnp.minimum(b, 1), 0, mt[5] + g)),
            kv_spec(lambda g, b, rp, mt: (1, 0, mt[5] + g)),
            kv_spec(lambda g, b, rp, mt: (jnp.maximum(b - 2, 0), 0, mt[3] + g)),
            kv_spec(lambda g, b, rp, mt: (jnp.maximum(b - 1, 0), 0, mt[3] + g)),
            kv_spec(lambda g, b, rp, mt: (b, 0, mt[3] + g)),
        ]
        args = [
            q_array, key_scale, value_scale,
            global_part, global_part, incoming[c], incoming[c], incoming[c], window_part, window_part,
            prompt_key_value, prompt_key_value, prompt_key_value,
        ]
        aliases = {}
        if prev is not None:
            in_specs.append(pl.BlockSpec(memory_space=pl.ANY))
            aliases = {2 + len(args): 0}
            args.append(prev)
        steps = chunk_heads * local_blocks
        out_spec = pl.BlockSpec((1, row_count, qw), lambda g, b, rp, mt: (b, 0, mt[4] + g))
        call = pl.pallas_call(
            attention_kernel,
            out_shape=jax.ShapeDtypeStruct((local_blocks, row_count, out_width), queries.dtype),
            grid_spec=pltpu.PrefetchScalarGridSpec(
                num_scalar_prefetch=2,
                grid=(chunk_heads, local_blocks),
                in_specs=in_specs,
                out_specs=out_spec,
            ),
            input_output_aliases=aliases,
            cost_estimate=pl.CostEstimate(
                flops=steps * 4 * query_groups * row_count * key_total * block_rows * head_dim,
                transcendentals=steps * query_groups * row_count * key_total * block_rows,
                bytes_accessed=steps * 2 * (2 * row_count * qw + key_total * block_rows * kvw),
            ),
            compiler_params=pltpu.CompilerParams(
                dimension_semantics=("arbitrary", "arbitrary"),
                vmem_limit_bytes=48 * 1024 * 1024,
            ),
        )
        return call(rpos, meta, *args)

    zero = jnp.int32(0)
    if not split:
        out = None
        for c in range(chunks):
            out = run(queries, zero, sub_index * row_count, query_width, zero, c, out)
        return out
    for_partner = None
    mine = None
    from_partner = None
    for c in range(chunks):
        for_partner = run(
            partner_q, zero, (1 - sub_index) * row_count, my_heads * qw, zero, c, for_partner
        )
        if c == chunks - 1:
            from_partner = lax.ppermute(for_partner, "sub", swap)
        mine = run(queries, head_off, sub_index * row_count, query_width, head_off, c, mine)
    return lax.dynamic_update_slice_in_dim(mine, from_partner, (1 - sub_index) * my_heads * qw, axis=2)


def solution(mesh):
    in_specs = (
        P(("group", "ctx"), "sub", "kvh"),
        P(("group", "ctx"), None, "kvh"),
        P("group", "kvh"),
        P(("group", "ctx"), None, "kvh"),
        P("group", "kvh"),
        P("group", None),
    )
    out_specs = P(("group", "ctx"), "sub", "kvh")
    return jax.shard_map(body, mesh=mesh, in_specs=in_specs, out_specs=out_specs, check_vma=False)
```

```python
import math

import jax
import jax.numpy as jnp
from jax import lax
from jax.experimental import pallas as pl
from jax.experimental.pallas import tpu as pltpu
from jax.sharding import PartitionSpec as P

HEAD_SIZE = 128

NG = 2
WIN = 2


def passed_along(block, axis, distance):
    devices = range(lax.axis_size(axis))
    route = [(i - distance, i) for i in devices if i - distance in devices]
    return lax.ppermute(block, axis, route)


def from_root(block, axis):
    count = lax.axis_size(axis)
    index = lax.axis_index(axis)
    have = block
    for dist in range(1, count):
        got = lax.ppermute(block, axis, [(0, dist)])
        have = jnp.where(index == dist, got, have)
    return have


def attention_kernel(
    rpos_ref, meta_ref,
    q_ref, ks_ref, vs_ref,
    g0_ref, g1_ref, r0_ref, r1_ref, r2_ref, w5r_ref, w6r_ref,
    wl5_ref, wl6_ref, own_ref, *rest,
):
    o_ref = rest[-1]
    b = pl.program_id(1)
    base = meta_ref[0]
    row_off = meta_ref[1]
    rows = q_ref.shape[1]
    groups = q_ref.shape[2] // HEAD_SIZE
    block_rows = own_ref.shape[1]
    d = HEAD_SIZE

    q = q_ref[0]
    q2 = jnp.concatenate([q[:, h * d:(h + 1) * d] for h in range(groups)], axis=0)

    w5 = jnp.where(b < 2, w5r_ref[0], wl5_ref[0])
    w6 = jnp.where(b < 1, w6r_ref[0], wl6_ref[0])
    blocks = [g0_ref[0], g1_ref[0], r0_ref[0], r1_ref[0], r2_ref[0], w5, w6]
    own = own_ref[0]
    keys = jnp.concatenate([blk[:, :d] for blk in blocks], axis=0)
    vals = jnp.concatenate([blk[:, d:] for blk in blocks], axis=0)
    front = keys.shape[0]

    dims = (((1,), (1,)), ((), ()))
    pv = (((1,), (0,)), ((), ()))
    glob_b = base + b

    def compute(masked):
        ks = ks_ref[0, 0]
        vs = vs_ref[0, 0]
        s_a = lax.dot_general(q2, keys, dims, preferred_element_type=jnp.float32)
        s_a = s_a * ks[:, :front]
        if masked:
            col = lax.broadcasted_iota(jnp.int32, (1, front), 1)
            bad = ((col >= 5 * block_rows) & (col < 6 * block_rows) & (glob_b < 2)) | (
                (col >= 6 * block_rows) & (glob_b < 1)
            )
            s_a = jnp.where(bad, -jnp.inf, s_a)
        s_b = lax.dot_general(q2, own[:, :d], dims, preferred_element_type=jnp.float32)
        s_b = s_b * ks[:, front:]
        kcol = lax.broadcasted_iota(jnp.int32, (1, block_rows), 1)
        row = lax.broadcasted_iota(jnp.int32, (groups * rows, 1), 0) % rows + row_off
        s_b = jnp.where(kcol <= row, s_b, -jnp.inf)
        m = jnp.maximum(jnp.max(s_a, axis=1, keepdims=True), jnp.max(s_b, axis=1, keepdims=True))
        p_a = jnp.exp2(s_a - m)
        p_b = jnp.exp2(s_b - m)
        totals = jnp.sum(p_a, axis=1, keepdims=True) + jnp.sum(p_b, axis=1, keepdims=True)
        w_a = (p_a * vs[:, :front]).astype(jnp.bfloat16)
        w_b = (p_b * vs[:, front:]).astype(jnp.bfloat16)
        acc = lax.dot_general(w_a, vals, pv, preferred_element_type=jnp.float32)
        acc = acc + lax.dot_general(w_b, own[:, d:], pv, preferred_element_type=jnp.float32)
        res = (acc / totals).astype(o_ref.dtype)
        for h in range(groups):
            o_ref[0, :, h * d:(h + 1) * d] = res[h * rows:(h + 1) * rows]

    @pl.when(glob_b < 2)
    def _():
        compute(True)

    @pl.when(glob_b >= 2)
    def _():
        compute(False)


def body(queries, cache_kv, cache_scale, prompt_key_value, prompt_scale, rand_blocks):
    ctx_count = lax.axis_size("ctx")
    ctx_index = lax.axis_index("ctx")
    sub_count = lax.axis_size("sub")
    sub_index = lax.axis_index("sub")
    local_blocks, row_count, query_width = queries.shape
    cache_blocks, block_rows, kv_width = cache_kv.shape
    head_dim = HEAD_SIZE
    kvw = 2 * head_dim
    local_heads = kv_width // kvw
    query_groups = query_width // (local_heads * head_dim)
    qw = query_groups * head_dim
    rand_count = rand_blocks.shape[1]
    capacity = max(2, (local_blocks * rand_count + ctx_count - 1) // ctx_count)
    split = sub_count == 2 and local_heads % 2 == 0
    my_heads = local_heads // 2 if split else local_heads
    head_off = sub_index * my_heads if split else jnp.int32(0)
    swap = [(0, 1), (1, 0)]

    if split:
        partner_q = lax.dynamic_slice_in_dim(
            queries, (1 - sub_index) * my_heads * qw, my_heads * qw, axis=2
        )
        partner_q = lax.ppermute(partner_q, "sub", swap)
        cache_mine = lax.dynamic_slice_in_dim(cache_kv, head_off * kvw, my_heads * kvw, axis=2)
        prompt_mine = lax.dynamic_slice_in_dim(
            prompt_key_value[local_blocks - WIN:], head_off * kvw, my_heads * kvw, axis=2
        )
    else:
        cache_mine = cache_kv
        prompt_mine = prompt_key_value[local_blocks - WIN:]

    window_part = passed_along(prompt_mine, "ctx", 1)
    global_part = from_root(cache_mine[:NG], "ctx")

    per_reader = rand_blocks.reshape(ctx_count, local_blocks * rand_count)
    owners = per_reader // cache_blocks
    owner_hot = (
        owners[:, :, None] == jnp.arange(ctx_count, dtype=jnp.int32)[None, None, :]
    ).astype(jnp.int32)
    slot_rank = jnp.sum((jnp.cumsum(owner_hot, axis=1) - 1) * owner_hot, axis=2)
    picked = (
        (owners == ctx_index)[:, :, None]
        & (slot_rank[:, :, None] == jnp.arange(capacity, dtype=jnp.int32)[None, None, :])
    ).astype(jnp.int32)
    local_ids = jnp.sum(picked * (per_reader % cache_blocks)[:, :, None], axis=1)
    outgoing = jnp.take(cache_mine, local_ids.reshape(-1), axis=0)
    chunks = 2 if my_heads % 2 == 0 else 1
    chunk_heads = my_heads // chunks
    chunk_width = chunk_heads * kvw
    incoming = []
    for c in range(chunks):
        piece = outgoing[:, :, c * chunk_width:(c + 1) * chunk_width]
        if incoming:
            piece, _ = lax.optimization_barrier((piece, incoming[-1]))
        incoming.append(lax.all_to_all(piece, "ctx", split_axis=0, concat_axis=0, tiled=True))

    own_refs = lax.dynamic_index_in_dim(per_reader, ctx_index, 0, keepdims=False)
    own_ranks = lax.dynamic_index_in_dim(slot_rank, ctx_index, 0, keepdims=False)
    own_ranks = jnp.minimum(own_ranks, capacity - 1)
    rpos = (own_refs // cache_blocks * capacity + own_ranks).astype(jnp.int32)
    rpos = rpos.reshape(-1)

    local_order = jnp.arange(local_blocks, dtype=jnp.int32)
    global_order = ctx_index * local_blocks + local_order
    steps_back = jnp.arange(WIN, 0, -1, dtype=jnp.int32)
    back_global = global_order[:, None] - steps_back[None, :]
    cache_ids = jnp.concatenate(
        [
            jnp.broadcast_to(jnp.arange(NG, dtype=jnp.int32)[None, :], (local_blocks, NG)),
            own_refs.reshape(local_blocks, rand_count),
        ],
        axis=1,
    )
    prompt_ids = jnp.concatenate([jnp.maximum(back_global, 0), global_order[:, None]], axis=1)
    scale_row_table = jnp.concatenate(
        [jnp.take(cache_scale, cache_ids, axis=0), jnp.take(prompt_scale, prompt_ids, axis=0)],
        axis=1,
    )
    key_total = scale_row_table.shape[1]
    scale_row_table = scale_row_table.reshape(local_blocks, key_total, local_heads, 2)
    scale_row_table = jnp.transpose(scale_row_table, (0, 2, 3, 1))
    key_scale = scale_row_table[:, :, 0] / math.sqrt(head_dim) * math.log2(math.e)
    key_scale = jnp.repeat(key_scale, block_rows, axis=-1)
    value_scale = jnp.repeat(scale_row_table[:, :, 1], block_rows, axis=-1)
    key_scale = key_scale.reshape(local_blocks, local_heads, 1, key_total * block_rows)
    value_scale = value_scale.reshape(local_blocks, local_heads, 1, key_total * block_rows)

    def run(q_array, q_head_off, row_off, out_width, out_head_off, c, prev):
        c_off = c * chunk_heads
        meta = jnp.stack(
            [ctx_index * local_blocks, row_off, q_head_off + c_off, head_off + c_off,
             out_head_off + c_off, jnp.int32(c_off)]
        )
        meta = meta.astype(jnp.int32)

        def kv_spec(index_fn):
            return pl.BlockSpec((1, block_rows, kvw), index_fn)

        in_specs = [
            pl.BlockSpec((1, row_count, qw), lambda g, b, rp, mt: (b, 0, mt[2] + g)),
            pl.BlockSpec((1, 1, 1, key_total * block_rows), lambda g, b, rp, mt: (b, mt[3] + g, 0, 0)),
            pl.BlockSpec((1, 1, 1, key_total * block_rows), lambda g, b, rp, mt: (b, mt[3] + g, 0, 0)),
            kv_spec(lambda g, b, rp, mt: (0, 0, mt[5] + g)),
            kv_spec(lambda g, b, rp, mt: (1, 0, mt[5] + g)),
            kv_spec(lambda g, b, rp, mt: (rp[b * 3], 0, g)),
            kv_spec(lambda g, b, rp, mt: (rp[b * 3 + 1], 0, g)),
            kv_spec(lambda g, b, rp, mt: (rp[b * 3 + 2], 0, g)),
            kv_spec(lambda g, b, rp, mt: (jnp.minimum(b, 1), 0, mt[5] + g)),
            kv_spec(lambda g, b, rp, mt: (1, 0, mt[5] + g)),
            kv_spec(lambda g, b, rp, mt: (jnp.maximum(b - 2, 0), 0, mt[3] + g)),
            kv_spec(lambda g, b, rp, mt: (jnp.maximum(b - 1, 0), 0, mt[3] + g)),
            kv_spec(lambda g, b, rp, mt: (b, 0, mt[3] + g)),
        ]
        args = [
            q_array, key_scale, value_scale,
            global_part, global_part, incoming[c], incoming[c], incoming[c], window_part, window_part,
            prompt_key_value, prompt_key_value, prompt_key_value,
        ]
        aliases = {}
        if prev is not None:
            in_specs.append(pl.BlockSpec(memory_space=pl.ANY))
            aliases = {2 + len(args): 0}
            args.append(prev)
        steps = chunk_heads * local_blocks
        out_spec = pl.BlockSpec((1, row_count, qw), lambda g, b, rp, mt: (b, 0, mt[4] + g))
        call = pl.pallas_call(
            attention_kernel,
            out_shape=jax.ShapeDtypeStruct((local_blocks, row_count, out_width), queries.dtype),
            grid_spec=pltpu.PrefetchScalarGridSpec(
                num_scalar_prefetch=2,
                grid=(chunk_heads, local_blocks),
                in_specs=in_specs,
                out_specs=out_spec,
            ),
            input_output_aliases=aliases,
            cost_estimate=pl.CostEstimate(
                flops=steps * 4 * query_groups * row_count * key_total * block_rows * head_dim,
                transcendentals=steps * query_groups * row_count * key_total * block_rows,
                bytes_accessed=steps * 2 * (2 * row_count * qw + key_total * block_rows * kvw),
            ),
            compiler_params=pltpu.CompilerParams(
                dimension_semantics=("arbitrary", "arbitrary"),
                vmem_limit_bytes=48 * 1024 * 1024,
            ),
        )
        return call(rpos, meta, *args)

    zero = jnp.int32(0)
    if not split:
        out = None
        for c in range(chunks):
            out = run(queries, zero, sub_index * row_count, query_width, zero, c, out)
        return out
    for_partner = None
    mine = None
    from_partner = None
    for c in range(chunks):
        for_partner = run(
            partner_q, zero, (1 - sub_index) * row_count, my_heads * qw, zero, c, for_partner
        )
        if c == chunks - 1:
            from_partner = lax.ppermute(for_partner, "sub", swap)
        mine = run(queries, head_off, sub_index * row_count, query_width, head_off, c, mine)
    return lax.dynamic_update_slice_in_dim(mine, from_partner, (1 - sub_index) * my_heads * qw, axis=2)


def solution(mesh):
    in_specs = (
        P(("group", "ctx"), "sub", "kvh"),
        P(("group", "ctx"), None, "kvh"),
        P("group", "kvh"),
        P(("group", "ctx"), None, "kvh"),
        P("group", "kvh"),
        P("group", None),
    )
    out_specs = P(("group", "ctx"), "sub", "kvh")
    return jax.shard_map(body, mesh=mesh, in_specs=in_specs, out_specs=out_specs, check_vma=False)
```

```python
import math

import jax
import jax.numpy as jnp
from jax import lax
from jax.experimental import pallas as pl
from jax.experimental.pallas import tpu as pltpu
from jax.sharding import PartitionSpec as P

HEAD_SIZE = 128

NG = 2
WIN = 2


def passed_along(block, axis, distance):
    devices = range(lax.axis_size(axis))
    route = [(i - distance, i) for i in devices if i - distance in devices]
    return lax.ppermute(block, axis, route)


def from_root(block, axis):
    count = lax.axis_size(axis)
    index = lax.axis_index(axis)
    have = block
    for dist in range(1, count):
        got = lax.ppermute(block, axis, [(0, dist)])
        have = jnp.where(index == dist, got, have)
    return have


def attention_kernel(
    rpos_ref, meta_ref,
    q_ref, ks_ref, vs_ref,
    g0_ref, g1_ref, r0_ref, r1_ref, r2_ref, w5r_ref, w6r_ref,
    wl5_ref, wl6_ref, own_ref, *rest,
):
    o_ref = rest[-1]
    b = pl.program_id(1)
    base = meta_ref[0]
    row_off = meta_ref[1]
    rows = q_ref.shape[1]
    groups = q_ref.shape[2] // HEAD_SIZE
    block_rows = own_ref.shape[1]
    d = HEAD_SIZE

    q = q_ref[0]
    q2 = jnp.concatenate([q[:, h * d:(h + 1) * d] for h in range(groups)], axis=0)

    w5 = jnp.where(b < 2, w5r_ref[0], wl5_ref[0])
    w6 = jnp.where(b < 1, w6r_ref[0], wl6_ref[0])
    blocks = [g0_ref[0], g1_ref[0], r0_ref[0], r1_ref[0], r2_ref[0], w5, w6]
    own = own_ref[0]
    keys = jnp.concatenate([blk[:, :d] for blk in blocks], axis=0)
    vals = jnp.concatenate([blk[:, d:] for blk in blocks], axis=0)
    front = keys.shape[0]

    dims = (((1,), (1,)), ((), ()))
    pv = (((1,), (0,)), ((), ()))
    glob_b = base + b

    def compute(masked):
        ks = ks_ref[0, 0]
        vs = vs_ref[0, 0]
        s_a = lax.dot_general(q2, keys, dims, preferred_element_type=jnp.float32)
        s_a = s_a * ks[:, :front]
        if masked:
            col = lax.broadcasted_iota(jnp.int32, (1, front), 1)
            bad = ((col >= 5 * block_rows) & (col < 6 * block_rows) & (glob_b < 2)) | (
                (col >= 6 * block_rows) & (glob_b < 1)
            )
            s_a = jnp.where(bad, -jnp.inf, s_a)
        s_b = lax.dot_general(q2, own[:, :d], dims, preferred_element_type=jnp.float32)
        s_b = s_b * ks[:, front:]
        kcol = lax.broadcasted_iota(jnp.int32, (1, block_rows), 1)
        row = lax.broadcasted_iota(jnp.int32, (groups * rows, 1), 0) % rows + row_off
        s_b = jnp.where(kcol <= row, s_b, -jnp.inf)
        m = jnp.maximum(jnp.max(s_a, axis=1, keepdims=True), jnp.max(s_b, axis=1, keepdims=True))
        p_a = jnp.exp2(s_a - m)
        p_b = jnp.exp2(s_b - m)
        totals = jnp.sum(p_a, axis=1, keepdims=True) + jnp.sum(p_b, axis=1, keepdims=True)
        w_a = (p_a * vs[:, :front]).astype(jnp.bfloat16)
        w_b = (p_b * vs[:, front:]).astype(jnp.bfloat16)
        acc = lax.dot_general(w_a, vals, pv, preferred_element_type=jnp.float32)
        acc = acc + lax.dot_general(w_b, own[:, d:], pv, preferred_element_type=jnp.float32)
        res = (acc / totals).astype(o_ref.dtype)
        for h in range(groups):
            o_ref[0, :, h * d:(h + 1) * d] = res[h * rows:(h + 1) * rows]

    @pl.when(glob_b < 2)
    def _():
        compute(True)

    @pl.when(glob_b >= 2)
    def _():
        compute(False)


def body(queries, cache_kv, cache_scale, prompt_key_value, prompt_scale, rand_blocks):
    ctx_count = lax.axis_size("ctx")
    ctx_index = lax.axis_index("ctx")
    sub_count = lax.axis_size("sub")
    sub_index = lax.axis_index("sub")
    local_blocks, row_count, query_width = queries.shape
    cache_blocks, block_rows, kv_width = cache_kv.shape
    head_dim = HEAD_SIZE
    kvw = 2 * head_dim
    local_heads = kv_width // kvw
    query_groups = query_width // (local_heads * head_dim)
    qw = query_groups * head_dim
    rand_count = rand_blocks.shape[1]
    capacity = max(2, (local_blocks * rand_count + ctx_count - 1) // ctx_count)
    split = sub_count == 2 and local_heads % 2 == 0
    my_heads = local_heads // 2 if split else local_heads
    head_off = sub_index * my_heads if split else jnp.int32(0)
    swap = [(0, 1), (1, 0)]

    if split:
        partner_q = lax.dynamic_slice_in_dim(
            queries, (1 - sub_index) * my_heads * qw, my_heads * qw, axis=2
        )
        partner_q = lax.ppermute(partner_q, "sub", swap)
        cache_mine = lax.dynamic_slice_in_dim(cache_kv, head_off * kvw, my_heads * kvw, axis=2)
        prompt_mine = lax.dynamic_slice_in_dim(
            prompt_key_value[local_blocks - WIN:], head_off * kvw, my_heads * kvw, axis=2
        )
    else:
        cache_mine = cache_kv
        prompt_mine = prompt_key_value[local_blocks - WIN:]

    window_part = passed_along(prompt_mine, "ctx", 1)
    global_part = from_root(cache_mine[:NG], "ctx")

    per_reader = rand_blocks.reshape(ctx_count, local_blocks * rand_count)
    owners = per_reader // cache_blocks
    owner_hot = (
        owners[:, :, None] == jnp.arange(ctx_count, dtype=jnp.int32)[None, None, :]
    ).astype(jnp.int32)
    slot_rank = jnp.sum((jnp.cumsum(owner_hot, axis=1) - 1) * owner_hot, axis=2)
    picked = (
        (owners == ctx_index)[:, :, None]
        & (slot_rank[:, :, None] == jnp.arange(capacity, dtype=jnp.int32)[None, None, :])
    ).astype(jnp.int32)
    local_ids = jnp.sum(picked * (per_reader % cache_blocks)[:, :, None], axis=1)
    outgoing = jnp.take(cache_mine, local_ids.reshape(-1), axis=0)
    chunks = 2 if my_heads % 2 == 0 else 1
    chunk_heads = my_heads // chunks
    chunk_width = chunk_heads * kvw
    incoming = []
    for c in range(chunks):
        piece = outgoing[:, :, c * chunk_width:(c + 1) * chunk_width]
        if incoming:
            piece, _ = lax.optimization_barrier((piece, incoming[-1]))
        incoming.append(lax.all_to_all(piece, "ctx", split_axis=0, concat_axis=0, tiled=True))

    own_refs = lax.dynamic_index_in_dim(per_reader, ctx_index, 0, keepdims=False)
    own_ranks = lax.dynamic_index_in_dim(slot_rank, ctx_index, 0, keepdims=False)
    own_ranks = jnp.minimum(own_ranks, capacity - 1)
    rpos = (own_refs // cache_blocks * capacity + own_ranks).astype(jnp.int32)
    rpos = rpos.reshape(-1)

    local_order = jnp.arange(local_blocks, dtype=jnp.int32)
    global_order = ctx_index * local_blocks + local_order
    steps_back = jnp.arange(WIN, 0, -1, dtype=jnp.int32)
    back_global = global_order[:, None] - steps_back[None, :]
    cache_ids = jnp.concatenate(
        [
            jnp.broadcast_to(jnp.arange(NG, dtype=jnp.int32)[None, :], (local_blocks, NG)),
            own_refs.reshape(local_blocks, rand_count),
        ],
        axis=1,
    )
    prompt_ids = jnp.concatenate([jnp.maximum(back_global, 0), global_order[:, None]], axis=1)
    scale_row_table = jnp.concatenate(
        [jnp.take(cache_scale, cache_ids, axis=0), jnp.take(prompt_scale, prompt_ids, axis=0)],
        axis=1,
    )
    key_total = scale_row_table.shape[1]
    scale_row_table = scale_row_table.reshape(local_blocks, key_total, local_heads, 2)
    scale_row_table = jnp.transpose(scale_row_table, (0, 2, 3, 1))
    key_scale = scale_row_table[:, :, 0] / math.sqrt(head_dim) * math.log2(math.e)
    key_scale = jnp.repeat(key_scale, block_rows, axis=-1)
    value_scale = jnp.repeat(scale_row_table[:, :, 1], block_rows, axis=-1)
    key_scale = key_scale.reshape(local_blocks, local_heads, 1, key_total * block_rows)
    value_scale = value_scale.reshape(local_blocks, local_heads, 1, key_total * block_rows)

    def run(q_array, q_head_off, row_off, out_width, out_head_off, c, prev):
        c_off = c * chunk_heads
        meta = jnp.stack(
            [ctx_index * local_blocks, row_off, q_head_off + c_off, head_off + c_off,
             out_head_off + c_off, jnp.int32(c_off)]
        )
        meta = meta.astype(jnp.int32)

        def kv_spec(index_fn):
            return pl.BlockSpec((1, block_rows, kvw), index_fn)

        in_specs = [
            pl.BlockSpec((1, row_count, qw), lambda g, b, rp, mt: (b, 0, mt[2] + g)),
            pl.BlockSpec((1, 1, 1, key_total * block_rows), lambda g, b, rp, mt: (b, mt[3] + g, 0, 0)),
            pl.BlockSpec((1, 1, 1, key_total * block_rows), lambda g, b, rp, mt: (b, mt[3] + g, 0, 0)),
            kv_spec(lambda g, b, rp, mt: (0, 0, mt[5] + g)),
            kv_spec(lambda g, b, rp, mt: (1, 0, mt[5] + g)),
            kv_spec(lambda g, b, rp, mt: (rp[b * 3], 0, g)),
            kv_spec(lambda g, b, rp, mt: (rp[b * 3 + 1], 0, g)),
            kv_spec(lambda g, b, rp, mt: (rp[b * 3 + 2], 0, g)),
            kv_spec(lambda g, b, rp, mt: (jnp.minimum(b, 1), 0, mt[5] + g)),
            kv_spec(lambda g, b, rp, mt: (1, 0, mt[5] + g)),
            kv_spec(lambda g, b, rp, mt: (jnp.maximum(b - 2, 0), 0, mt[3] + g)),
            kv_spec(lambda g, b, rp, mt: (jnp.maximum(b - 1, 0), 0, mt[3] + g)),
            kv_spec(lambda g, b, rp, mt: (b, 0, mt[3] + g)),
        ]
        args = [
            q_array, key_scale, value_scale,
            global_part, global_part, incoming[c], incoming[c], incoming[c], window_part, window_part,
            prompt_key_value, prompt_key_value, prompt_key_value,
        ]
        aliases = {}
        if prev is not None:
            in_specs.append(pl.BlockSpec(memory_space=pl.ANY))
            aliases = {2 + len(args): 0}
            args.append(prev)
        steps = chunk_heads * local_blocks
        out_spec = pl.BlockSpec((1, row_count, qw), lambda g, b, rp, mt: (b, 0, mt[4] + g))
        call = pl.pallas_call(
            attention_kernel,
            out_shape=jax.ShapeDtypeStruct((local_blocks, row_count, out_width), queries.dtype),
            grid_spec=pltpu.PrefetchScalarGridSpec(
                num_scalar_prefetch=2,
                grid=(chunk_heads, local_blocks),
                in_specs=in_specs,
                out_specs=out_spec,
            ),
            input_output_aliases=aliases,
            cost_estimate=pl.CostEstimate(
                flops=steps * 4 * query_groups * row_count * key_total * block_rows * head_dim,
                transcendentals=steps * query_groups * row_count * key_total * block_rows,
                bytes_accessed=steps * 2 * (2 * row_count * qw + key_total * block_rows * kvw),
            ),
            compiler_params=pltpu.CompilerParams(
                dimension_semantics=("arbitrary", "arbitrary"),
                vmem_limit_bytes=48 * 1024 * 1024,
            ),
        )
        return call(rpos, meta, *args)

    zero = jnp.int32(0)
    if not split:
        out = None
        for c in range(chunks):
            out = run(queries, zero, sub_index * row_count, query_width, zero, c, out)
        return out
    for_partner = None
    mine = None
    from_partner = None
    partner_in = partner_q
    for c in range(chunks):
        if mine is not None:
            partner_in, mine = lax.optimization_barrier((partner_q, mine))
        for_partner = run(
            partner_in, zero, (1 - sub_index) * row_count, my_heads * qw, zero, c, for_partner
        )
        if c == chunks - 1:
            from_partner = lax.ppermute(for_partner, "sub", swap)
        mine = run(queries, head_off, sub_index * row_count, query_width, head_off, c, mine)
    return lax.dynamic_update_slice_in_dim(mine, from_partner, (1 - sub_index) * my_heads * qw, axis=2)


def solution(mesh):
    in_specs = (
        P(("group", "ctx"), "sub", "kvh"),
        P(("group", "ctx"), None, "kvh"),
        P("group", "kvh"),
        P(("group", "ctx"), None, "kvh"),
        P("group", "kvh"),
        P("group", None),
    )
    out_specs = P(("group", "ctx"), "sub", "kvh")
    return jax.shard_map(body, mesh=mesh, in_specs=in_specs, out_specs=out_specs, check_vma=False)
```

```python
import math

import jax
import jax.numpy as jnp
from jax import lax
from jax.experimental import pallas as pl
from jax.experimental.pallas import tpu as pltpu
from jax.sharding import PartitionSpec as P

HEAD_SIZE = 128

NG = 2
WIN = 2


def passed_along(block, axis, distance):
    devices = range(lax.axis_size(axis))
    route = [(i - distance, i) for i in devices if i - distance in devices]
    return lax.ppermute(block, axis, route)


def from_root(block, axis):
    count = lax.axis_size(axis)
    index = lax.axis_index(axis)
    have = block
    for dist in range(1, count):
        got = lax.ppermute(block, axis, [(0, dist)])
        have = jnp.where(index == dist, got, have)
    return have


def attention_kernel(
    rpos_ref, meta_ref,
    q_ref, ks_ref, vs_ref,
    g0_ref, g1_ref, r0_ref, r1_ref, r2_ref, w5r_ref, w6r_ref,
    wl5_ref, wl6_ref, own_ref, *rest,
):
    o_ref = rest[-1]
    b = pl.program_id(1)
    base = meta_ref[0]
    row_off = meta_ref[1]
    rows = q_ref.shape[1]
    groups = q_ref.shape[2] // HEAD_SIZE
    block_rows = own_ref.shape[1]
    d = HEAD_SIZE

    q = q_ref[0]
    q2 = jnp.concatenate([q[:, h * d:(h + 1) * d] for h in range(groups)], axis=0)

    w5 = jnp.where(b < 2, w5r_ref[0], wl5_ref[0])
    w6 = jnp.where(b < 1, w6r_ref[0], wl6_ref[0])
    blocks = [g0_ref[0], g1_ref[0], r0_ref[0], r1_ref[0], r2_ref[0], w5, w6]
    own = own_ref[0]
    keys = jnp.concatenate([blk[:, :d] for blk in blocks], axis=0)
    vals = jnp.concatenate([blk[:, d:] for blk in blocks], axis=0)
    front = keys.shape[0]

    dims = (((1,), (1,)), ((), ()))
    pv = (((1,), (0,)), ((), ()))
    glob_b = base + b

    def compute(masked):
        ks = ks_ref[0, 0]
        vs = vs_ref[0, 0]
        s_a = lax.dot_general(q2, keys, dims, preferred_element_type=jnp.float32)
        s_a = s_a * ks[:, :front]
        if masked:
            col = lax.broadcasted_iota(jnp.int32, (1, front), 1)
            bad = ((col >= 5 * block_rows) & (col < 6 * block_rows) & (glob_b < 2)) | (
                (col >= 6 * block_rows) & (glob_b < 1)
            )
            s_a = jnp.where(bad, -jnp.inf, s_a)
        s_b = lax.dot_general(q2, own[:, :d], dims, preferred_element_type=jnp.float32)
        s_b = s_b * ks[:, front:]
        kcol = lax.broadcasted_iota(jnp.int32, (1, block_rows), 1)
        row = lax.broadcasted_iota(jnp.int32, (groups * rows, 1), 0) % rows + row_off
        s_b = jnp.where(kcol <= row, s_b, -jnp.inf)
        m = jnp.maximum(jnp.max(s_a, axis=1, keepdims=True), jnp.max(s_b, axis=1, keepdims=True))
        p_a = jnp.exp2(s_a - m)
        p_b = jnp.exp2(s_b - m)
        totals = jnp.sum(p_a, axis=1, keepdims=True) + jnp.sum(p_b, axis=1, keepdims=True)
        w_a = (p_a * vs[:, :front]).astype(jnp.bfloat16)
        w_b = (p_b * vs[:, front:]).astype(jnp.bfloat16)
        acc = lax.dot_general(w_a, vals, pv, preferred_element_type=jnp.float32)
        acc = acc + lax.dot_general(w_b, own[:, d:], pv, preferred_element_type=jnp.float32)
        res = (acc / totals).astype(o_ref.dtype)
        for h in range(groups):
            o_ref[0, :, h * d:(h + 1) * d] = res[h * rows:(h + 1) * rows]

    @pl.when(glob_b < 2)
    def _():
        compute(True)

    @pl.when(glob_b >= 2)
    def _():
        compute(False)


def body(queries, cache_kv, cache_scale, prompt_key_value, prompt_scale, rand_blocks):
    ctx_count = lax.axis_size("ctx")
    ctx_index = lax.axis_index("ctx")
    sub_count = lax.axis_size("sub")
    sub_index = lax.axis_index("sub")
    local_blocks, row_count, query_width = queries.shape
    cache_blocks, block_rows, kv_width = cache_kv.shape
    head_dim = HEAD_SIZE
    kvw = 2 * head_dim
    local_heads = kv_width // kvw
    query_groups = query_width // (local_heads * head_dim)
    qw = query_groups * head_dim
    rand_count = rand_blocks.shape[1]
    capacity = max(2, (local_blocks * rand_count + ctx_count - 1) // ctx_count)
    split = sub_count == 2 and local_heads % 2 == 0
    my_heads = local_heads // 2 if split else local_heads
    head_off = sub_index * my_heads if split else jnp.int32(0)
    swap = [(0, 1), (1, 0)]

    if split:
        partner_q = lax.dynamic_slice_in_dim(
            queries, (1 - sub_index) * my_heads * qw, my_heads * qw, axis=2
        )
        partner_q = lax.ppermute(partner_q, "sub", swap)
        cache_mine = None
        prompt_mine = lax.dynamic_slice_in_dim(
            prompt_key_value[local_blocks - WIN:], head_off * kvw, my_heads * kvw, axis=2
        )
    else:
        cache_mine = cache_kv
        prompt_mine = prompt_key_value[local_blocks - WIN:]

    window_part = passed_along(prompt_mine, "ctx", 1)
    if split:
        global_src = lax.dynamic_slice_in_dim(cache_kv[:NG], head_off * kvw, my_heads * kvw, axis=2)
    else:
        global_src = cache_kv[:NG]
    global_part = from_root(global_src, "ctx")

    per_reader = rand_blocks.reshape(ctx_count, local_blocks * rand_count)
    owners = per_reader // cache_blocks
    owner_hot = (
        owners[:, :, None] == jnp.arange(ctx_count, dtype=jnp.int32)[None, None, :]
    ).astype(jnp.int32)
    slot_rank = jnp.sum((jnp.cumsum(owner_hot, axis=1) - 1) * owner_hot, axis=2)
    picked = (
        (owners == ctx_index)[:, :, None]
        & (slot_rank[:, :, None] == jnp.arange(capacity, dtype=jnp.int32)[None, None, :])
    ).astype(jnp.int32)
    local_ids = jnp.sum(picked * (per_reader % cache_blocks)[:, :, None], axis=1)
    send_ids = local_ids.reshape(-1)
    chunks = 2 if my_heads % 2 == 0 else 1
    chunk_heads = my_heads // chunks
    chunk_width = chunk_heads * kvw
    incoming = []
    for c in range(chunks):
        if split:
            source = lax.dynamic_slice_in_dim(
                cache_kv, (head_off + c * chunk_heads) * kvw, chunk_width, axis=2
            )
        else:
            source = cache_mine[:, :, c * chunk_width:(c + 1) * chunk_width]
        piece = jnp.take(source, send_ids, axis=0)
        if incoming:
            piece, _ = lax.optimization_barrier((piece, incoming[-1]))
        incoming.append(lax.all_to_all(piece, "ctx", split_axis=0, concat_axis=0, tiled=True))

    own_refs = lax.dynamic_index_in_dim(per_reader, ctx_index, 0, keepdims=False)
    own_ranks = lax.dynamic_index_in_dim(slot_rank, ctx_index, 0, keepdims=False)
    own_ranks = jnp.minimum(own_ranks, capacity - 1)
    rpos = (own_refs // cache_blocks * capacity + own_ranks).astype(jnp.int32)
    rpos = rpos.reshape(-1)

    local_order = jnp.arange(local_blocks, dtype=jnp.int32)
    global_order = ctx_index * local_blocks + local_order
    steps_back = jnp.arange(WIN, 0, -1, dtype=jnp.int32)
    back_global = global_order[:, None] - steps_back[None, :]
    cache_ids = jnp.concatenate(
        [
            jnp.broadcast_to(jnp.arange(NG, dtype=jnp.int32)[None, :], (local_blocks, NG)),
            own_refs.reshape(local_blocks, rand_count),
        ],
        axis=1,
    )
    prompt_ids = jnp.concatenate([jnp.maximum(back_global, 0), global_order[:, None]], axis=1)
    scale_row_table = jnp.concatenate(
        [jnp.take(cache_scale, cache_ids, axis=0), jnp.take(prompt_scale, prompt_ids, axis=0)],
        axis=1,
    )
    key_total = scale_row_table.shape[1]
    scale_row_table = scale_row_table.reshape(local_blocks, key_total, local_heads, 2)
    scale_row_table = jnp.transpose(scale_row_table, (0, 2, 3, 1))
    key_scale = scale_row_table[:, :, 0] / math.sqrt(head_dim) * math.log2(math.e)
    key_scale = jnp.repeat(key_scale, block_rows, axis=-1)
    value_scale = jnp.repeat(scale_row_table[:, :, 1], block_rows, axis=-1)
    key_scale = key_scale.reshape(local_blocks, local_heads, 1, key_total * block_rows)
    value_scale = value_scale.reshape(local_blocks, local_heads, 1, key_total * block_rows)

    def run(q_array, q_head_off, row_off, out_width, out_head_off, c, prev):
        c_off = c * chunk_heads
        meta = jnp.stack(
            [ctx_index * local_blocks, row_off, q_head_off + c_off, head_off + c_off,
             out_head_off + c_off, jnp.int32(c_off)]
        )
        meta = meta.astype(jnp.int32)

        def kv_spec(index_fn):
            return pl.BlockSpec((1, block_rows, kvw), index_fn)

        in_specs = [
            pl.BlockSpec((1, row_count, qw), lambda g, b, rp, mt: (b, 0, mt[2] + g)),
            pl.BlockSpec((1, 1, 1, key_total * block_rows), lambda g, b, rp, mt: (b, mt[3] + g, 0, 0)),
            pl.BlockSpec((1, 1, 1, key_total * block_rows), lambda g, b, rp, mt: (b, mt[3] + g, 0, 0)),
            kv_spec(lambda g, b, rp, mt: (0, 0, mt[5] + g)),
            kv_spec(lambda g, b, rp, mt: (1, 0, mt[5] + g)),
            kv_spec(lambda g, b, rp, mt: (rp[b * 3], 0, g)),
            kv_spec(lambda g, b, rp, mt: (rp[b * 3 + 1], 0, g)),
            kv_spec(lambda g, b, rp, mt: (rp[b * 3 + 2], 0, g)),
            kv_spec(lambda g, b, rp, mt: (jnp.minimum(b, 1), 0, mt[5] + g)),
            kv_spec(lambda g, b, rp, mt: (1, 0, mt[5] + g)),
            kv_spec(lambda g, b, rp, mt: (jnp.maximum(b - 2, 0), 0, mt[3] + g)),
            kv_spec(lambda g, b, rp, mt: (jnp.maximum(b - 1, 0), 0, mt[3] + g)),
            kv_spec(lambda g, b, rp, mt: (b, 0, mt[3] + g)),
        ]
        args = [
            q_array, key_scale, value_scale,
            global_part, global_part, incoming[c], incoming[c], incoming[c], window_part, window_part,
            prompt_key_value, prompt_key_value, prompt_key_value,
        ]
        aliases = {}
        if prev is not None:
            in_specs.append(pl.BlockSpec(memory_space=pl.ANY))
            aliases = {2 + len(args): 0}
            args.append(prev)
        steps = chunk_heads * local_blocks
        out_spec = pl.BlockSpec((1, row_count, qw), lambda g, b, rp, mt: (b, 0, mt[4] + g))
        call = pl.pallas_call(
            attention_kernel,
            out_shape=jax.ShapeDtypeStruct((local_blocks, row_count, out_width), queries.dtype),
            grid_spec=pltpu.PrefetchScalarGridSpec(
                num_scalar_prefetch=2,
                grid=(chunk_heads, local_blocks),
                in_specs=in_specs,
                out_specs=out_spec,
            ),
            input_output_aliases=aliases,
            cost_estimate=pl.CostEstimate(
                flops=steps * 4 * query_groups * row_count * key_total * block_rows * head_dim,
                transcendentals=steps * query_groups * row_count * key_total * block_rows,
                bytes_accessed=steps * 2 * (2 * row_count * qw + key_total * block_rows * kvw),
            ),
            compiler_params=pltpu.CompilerParams(
                dimension_semantics=("arbitrary", "arbitrary"),
                vmem_limit_bytes=48 * 1024 * 1024,
            ),
        )
        return call(rpos, meta, *args)

    zero = jnp.int32(0)
    if not split:
        out = None
        for c in range(chunks):
            out = run(queries, zero, sub_index * row_count, query_width, zero, c, out)
        return out
    for_partner = None
    mine = None
    from_partner = None
    partner_in = partner_q
    for c in range(chunks):
        if mine is not None:
            partner_in, mine = lax.optimization_barrier((partner_q, mine))
        for_partner = run(
            partner_in, zero, (1 - sub_index) * row_count, my_heads * qw, zero, c, for_partner
        )
        if c == chunks - 1:
            from_partner = lax.ppermute(for_partner, "sub", swap)
        mine = run(queries, head_off, sub_index * row_count, query_width, head_off, c, mine)
    return lax.dynamic_update_slice_in_dim(mine, from_partner, (1 - sub_index) * my_heads * qw, axis=2)


def solution(mesh):
    in_specs = (
        P(("group", "ctx"), "sub", "kvh"),
        P(("group", "ctx"), None, "kvh"),
        P("group", "kvh"),
        P(("group", "ctx"), None, "kvh"),
        P("group", "kvh"),
        P("group", None),
    )
    out_specs = P(("group", "ctx"), "sub", "kvh")
    return jax.shard_map(body, mesh=mesh, in_specs=in_specs, out_specs=out_specs, check_vma=False)
```

```python
import math

import jax
import jax.numpy as jnp
from jax import lax
from jax.experimental import pallas as pl
from jax.experimental.pallas import tpu as pltpu
from jax.sharding import PartitionSpec as P

HEAD_SIZE = 128

NG = 2
WIN = 2


def passed_along(block, axis, distance):
    devices = range(lax.axis_size(axis))
    route = [(i - distance, i) for i in devices if i - distance in devices]
    return lax.ppermute(block, axis, route)


def from_root(block, axis):
    count = lax.axis_size(axis)
    index = lax.axis_index(axis)
    have = block
    for dist in range(1, count):
        got = lax.ppermute(block, axis, [(0, dist)])
        have = jnp.where(index == dist, got, have)
    return have


def attention_kernel(
    rpos_ref, meta_ref,
    q_ref, ks_ref, vs_ref,
    g0_ref, g1_ref, r0_ref, r1_ref, r2_ref, w5r_ref, w6r_ref,
    wl5_ref, wl6_ref, own_ref, *rest,
):
    o_ref = rest[-1]
    b = pl.program_id(1)
    base = meta_ref[0]
    row_off = meta_ref[1]
    rows = q_ref.shape[1]
    groups = q_ref.shape[2] // HEAD_SIZE
    block_rows = own_ref.shape[1]
    d = HEAD_SIZE

    q = q_ref[0]
    q2 = jnp.concatenate([q[:, h * d:(h + 1) * d] for h in range(groups)], axis=0)

    w5 = jnp.where(b < 2, w5r_ref[0], wl5_ref[0])
    w6 = jnp.where(b < 1, w6r_ref[0], wl6_ref[0])
    blocks = [g0_ref[0], g1_ref[0], r0_ref[0], r1_ref[0], r2_ref[0], w5, w6]
    own = own_ref[0]
    keys = jnp.concatenate([blk[:, :d] for blk in blocks], axis=0)
    vals = jnp.concatenate([blk[:, d:] for blk in blocks], axis=0)
    front = keys.shape[0]

    dims = (((1,), (1,)), ((), ()))
    pv = (((1,), (0,)), ((), ()))
    glob_b = base + b

    def compute(masked):
        ks = ks_ref[0, 0]
        vs = vs_ref[0, 0]
        s_a = lax.dot_general(q2, keys, dims, preferred_element_type=jnp.float32)
        s_a = s_a * ks[:, :front]
        if masked:
            col = lax.broadcasted_iota(jnp.int32, (1, front), 1)
            bad = ((col >= 5 * block_rows) & (col < 6 * block_rows) & (glob_b < 2)) | (
                (col >= 6 * block_rows) & (glob_b < 1)
            )
            s_a = jnp.where(bad, -jnp.inf, s_a)
        s_b = lax.dot_general(q2, own[:, :d], dims, preferred_element_type=jnp.float32)
        s_b = s_b * ks[:, front:]
        kcol = lax.broadcasted_iota(jnp.int32, (1, block_rows), 1)
        row = lax.broadcasted_iota(jnp.int32, (groups * rows, 1), 0) % rows + row_off
        s_b = jnp.where(kcol <= row, s_b, -jnp.inf)
        m = jnp.maximum(jnp.max(s_a, axis=1, keepdims=True), jnp.max(s_b, axis=1, keepdims=True))
        p_a = jnp.exp2(s_a - m)
        p_b = jnp.exp2(s_b - m)
        totals = jnp.sum(p_a, axis=1, keepdims=True) + jnp.sum(p_b, axis=1, keepdims=True)
        w_a = (p_a * vs[:, :front]).astype(jnp.bfloat16)
        w_b = (p_b * vs[:, front:]).astype(jnp.bfloat16)
        acc = lax.dot_general(w_a, vals, pv, preferred_element_type=jnp.float32)
        acc = acc + lax.dot_general(w_b, own[:, d:], pv, preferred_element_type=jnp.float32)
        res = (acc / totals).astype(o_ref.dtype)
        for h in range(groups):
            o_ref[0, :, h * d:(h + 1) * d] = res[h * rows:(h + 1) * rows]

    @pl.when(glob_b < 2)
    def _():
        compute(True)

    @pl.when(glob_b >= 2)
    def _():
        compute(False)


def body(queries, cache_kv, cache_scale, prompt_key_value, prompt_scale, rand_blocks):
    ctx_count = lax.axis_size("ctx")
    ctx_index = lax.axis_index("ctx")
    sub_count = lax.axis_size("sub")
    sub_index = lax.axis_index("sub")
    local_blocks, row_count, query_width = queries.shape
    cache_blocks, block_rows, kv_width = cache_kv.shape
    head_dim = HEAD_SIZE
    kvw = 2 * head_dim
    local_heads = kv_width // kvw
    query_groups = query_width // (local_heads * head_dim)
    qw = query_groups * head_dim
    rand_count = rand_blocks.shape[1]
    capacity = max(2, (local_blocks * rand_count + ctx_count - 1) // ctx_count)
    split = sub_count == 2 and local_heads % 2 == 0
    my_heads = local_heads // 2 if split else local_heads
    head_off = sub_index * my_heads if split else jnp.int32(0)
    swap = [(0, 1), (1, 0)]

    if split:
        partner_q = lax.dynamic_slice_in_dim(
            queries, (1 - sub_index) * my_heads * qw, my_heads * qw, axis=2
        )
        partner_q = lax.ppermute(partner_q, "sub", swap)
        cache_mine = None
        prompt_mine = lax.dynamic_slice_in_dim(
            prompt_key_value[local_blocks - WIN:], head_off * kvw, my_heads * kvw, axis=2
        )
    else:
        cache_mine = cache_kv
        prompt_mine = prompt_key_value[local_blocks - WIN:]

    window_part = passed_along(prompt_mine, "ctx", 1)
    if split:
        global_src = lax.dynamic_slice_in_dim(cache_kv[:NG], head_off * kvw, my_heads * kvw, axis=2)
    else:
        global_src = cache_kv[:NG]
    global_part = from_root(global_src, "ctx")

    per_reader = rand_blocks.reshape(ctx_count, local_blocks * rand_count)
    owners = per_reader // cache_blocks
    owner_hot = (
        owners[:, :, None] == jnp.arange(ctx_count, dtype=jnp.int32)[None, None, :]
    ).astype(jnp.int32)
    slot_rank = jnp.sum((jnp.cumsum(owner_hot, axis=1) - 1) * owner_hot, axis=2)
    picked = (
        (owners == ctx_index)[:, :, None]
        & (slot_rank[:, :, None] == jnp.arange(capacity, dtype=jnp.int32)[None, None, :])
    ).astype(jnp.int32)
    local_ids = jnp.sum(picked * (per_reader % cache_blocks)[:, :, None], axis=1)
    send_ids = local_ids.reshape(-1)
    chunks = 2 if my_heads % 2 == 0 else 1
    chunk_heads = my_heads // chunks
    chunk_width = chunk_heads * kvw
    incoming = []
    for c in range(chunks):
        if split:
            source = lax.dynamic_slice_in_dim(
                cache_kv, (head_off + c * chunk_heads) * kvw, chunk_width, axis=2
            )
        else:
            source = cache_mine[:, :, c * chunk_width:(c + 1) * chunk_width]
        piece = jnp.take(source, send_ids, axis=0, mode="clip")
        if incoming:
            piece, _ = lax.optimization_barrier((piece, incoming[-1]))
        incoming.append(lax.all_to_all(piece, "ctx", split_axis=0, concat_axis=0, tiled=True))

    own_refs = lax.dynamic_index_in_dim(per_reader, ctx_index, 0, keepdims=False)
    own_ranks = lax.dynamic_index_in_dim(slot_rank, ctx_index, 0, keepdims=False)
    own_ranks = jnp.minimum(own_ranks, capacity - 1)
    rpos = (own_refs // cache_blocks * capacity + own_ranks).astype(jnp.int32)
    rpos = rpos.reshape(-1)

    local_order = jnp.arange(local_blocks, dtype=jnp.int32)
    global_order = ctx_index * local_blocks + local_order
    steps_back = jnp.arange(WIN, 0, -1, dtype=jnp.int32)
    back_global = global_order[:, None] - steps_back[None, :]
    cache_ids = jnp.concatenate(
        [
            jnp.broadcast_to(jnp.arange(NG, dtype=jnp.int32)[None, :], (local_blocks, NG)),
            own_refs.reshape(local_blocks, rand_count),
        ],
        axis=1,
    )
    prompt_ids = jnp.concatenate([jnp.maximum(back_global, 0), global_order[:, None]], axis=1)
    scale_row_table = jnp.concatenate(
        [jnp.take(cache_scale, cache_ids, axis=0), jnp.take(prompt_scale, prompt_ids, axis=0)],
        axis=1,
    )
    key_total = scale_row_table.shape[1]
    scale_row_table = scale_row_table.reshape(local_blocks, key_total, local_heads, 2)
    scale_row_table = jnp.transpose(scale_row_table, (0, 2, 3, 1))
    key_scale = scale_row_table[:, :, 0] / math.sqrt(head_dim) * math.log2(math.e)
    key_scale = jnp.repeat(key_scale, block_rows, axis=-1)
    value_scale = jnp.repeat(scale_row_table[:, :, 1], block_rows, axis=-1)
    key_scale = key_scale.reshape(local_blocks, local_heads, 1, key_total * block_rows)
    value_scale = value_scale.reshape(local_blocks, local_heads, 1, key_total * block_rows)

    def run(q_array, q_head_off, row_off, out_width, out_head_off, c, prev):
        c_off = c * chunk_heads
        meta = jnp.stack(
            [ctx_index * local_blocks, row_off, q_head_off + c_off, head_off + c_off,
             out_head_off + c_off, jnp.int32(c_off)]
        )
        meta = meta.astype(jnp.int32)

        def kv_spec(index_fn):
            return pl.BlockSpec((1, block_rows, kvw), index_fn)

        in_specs = [
            pl.BlockSpec((1, row_count, qw), lambda g, b, rp, mt: (b, 0, mt[2] + g)),
            pl.BlockSpec((1, 1, 1, key_total * block_rows), lambda g, b, rp, mt: (b, mt[3] + g, 0, 0)),
            pl.BlockSpec((1, 1, 1, key_total * block_rows), lambda g, b, rp, mt: (b, mt[3] + g, 0, 0)),
            kv_spec(lambda g, b, rp, mt: (0, 0, mt[5] + g)),
            kv_spec(lambda g, b, rp, mt: (1, 0, mt[5] + g)),
            kv_spec(lambda g, b, rp, mt: (rp[b * 3], 0, g)),
            kv_spec(lambda g, b, rp, mt: (rp[b * 3 + 1], 0, g)),
            kv_spec(lambda g, b, rp, mt: (rp[b * 3 + 2], 0, g)),
            kv_spec(lambda g, b, rp, mt: (jnp.minimum(b, 1), 0, mt[5] + g)),
            kv_spec(lambda g, b, rp, mt: (1, 0, mt[5] + g)),
            kv_spec(lambda g, b, rp, mt: (jnp.maximum(b - 2, 0), 0, mt[3] + g)),
            kv_spec(lambda g, b, rp, mt: (jnp.maximum(b - 1, 0), 0, mt[3] + g)),
            kv_spec(lambda g, b, rp, mt: (b, 0, mt[3] + g)),
        ]
        args = [
            q_array, key_scale, value_scale,
            global_part, global_part, incoming[c], incoming[c], incoming[c], window_part, window_part,
            prompt_key_value, prompt_key_value, prompt_key_value,
        ]
        aliases = {}
        if prev is not None:
            in_specs.append(pl.BlockSpec(memory_space=pl.ANY))
            aliases = {2 + len(args): 0}
            args.append(prev)
        steps = chunk_heads * local_blocks
        out_spec = pl.BlockSpec((1, row_count, qw), lambda g, b, rp, mt: (b, 0, mt[4] + g))
        call = pl.pallas_call(
            attention_kernel,
            out_shape=jax.ShapeDtypeStruct((local_blocks, row_count, out_width), queries.dtype),
            grid_spec=pltpu.PrefetchScalarGridSpec(
                num_scalar_prefetch=2,
                grid=(chunk_heads, local_blocks),
                in_specs=in_specs,
                out_specs=out_spec,
            ),
            input_output_aliases=aliases,
            cost_estimate=pl.CostEstimate(
                flops=steps * 4 * query_groups * row_count * key_total * block_rows * head_dim,
                transcendentals=steps * query_groups * row_count * key_total * block_rows,
                bytes_accessed=steps * 2 * (2 * row_count * qw + key_total * block_rows * kvw),
            ),
            compiler_params=pltpu.CompilerParams(
                dimension_semantics=("arbitrary", "arbitrary"),
                vmem_limit_bytes=48 * 1024 * 1024,
            ),
        )
        return call(rpos, meta, *args)

    zero = jnp.int32(0)
    if not split:
        out = None
        for c in range(chunks):
            out = run(queries, zero, sub_index * row_count, query_width, zero, c, out)
        return out
    for_partner = None
    mine = None
    from_partner = None
    partner_in = partner_q
    for c in range(chunks):
        if mine is not None:
            partner_in, mine = lax.optimization_barrier((partner_q, mine))
        for_partner = run(
            partner_in, zero, (1 - sub_index) * row_count, my_heads * qw, zero, c, for_partner
        )
        if c == chunks - 1:
            from_partner = lax.ppermute(for_partner, "sub", swap)
        mine = run(queries, head_off, sub_index * row_count, query_width, head_off, c, mine)
    return lax.dynamic_update_slice_in_dim(mine, from_partner, (1 - sub_index) * my_heads * qw, axis=2)


def solution(mesh):
    in_specs = (
        P(("group", "ctx"), "sub", "kvh"),
        P(("group", "ctx"), None, "kvh"),
        P("group", "kvh"),
        P(("group", "ctx"), None, "kvh"),
        P("group", "kvh"),
        P("group", None),
    )
    out_specs = P(("group", "ctx"), "sub", "kvh")
    return jax.shard_map(body, mesh=mesh, in_specs=in_specs, out_specs=out_specs, check_vma=False)
```

```python
import math

import jax
import jax.numpy as jnp
from jax import lax
from jax.experimental import pallas as pl
from jax.experimental.pallas import tpu as pltpu
from jax.sharding import PartitionSpec as P

HEAD_SIZE = 128

NG = 2
WIN = 2


def passed_along(block, axis, distance):
    devices = range(lax.axis_size(axis))
    route = [(i - distance, i) for i in devices if i - distance in devices]
    return lax.ppermute(block, axis, route)


def from_root(block, axis):
    count = lax.axis_size(axis)
    index = lax.axis_index(axis)
    have = block
    for dist in range(1, count):
        got = lax.ppermute(block, axis, [(0, dist)])
        have = jnp.where(index == dist, got, have)
    return have


def gather_kernel(ids_ref, col_ref, src_ref, out_ref, sems):
    width = out_ref.shape[2]
    copies = [
        pltpu.make_async_copy(
            src_ref.at[ids_ref[i], :, pl.ds(pl.multiple_of(col_ref[0], 128), width)],
            out_ref.at[i],
            sems.at[i],
        )
        for i in range(out_ref.shape[0])
    ]
    for copy in copies:
        copy.start()
    for copy in copies:
        copy.wait()


def gather_blocks(src, ids, col, width):
    count = ids.shape[0]
    return pl.pallas_call(
        gather_kernel,
        out_shape=jax.ShapeDtypeStruct((count, src.shape[1], width), src.dtype),
        grid_spec=pltpu.PrefetchScalarGridSpec(
            num_scalar_prefetch=2,
            grid=(1,),
            in_specs=[pl.BlockSpec(memory_space=pl.ANY)],
            out_specs=pl.BlockSpec(memory_space=pl.ANY),
            scratch_shapes=[pltpu.SemaphoreType.DMA((count,))],
        ),
    )(ids, col, src)


def attention_kernel(
    rpos_ref, meta_ref,
    q_ref, ks_ref, vs_ref,
    g0_ref, g1_ref, r0_ref, r1_ref, r2_ref, w5r_ref, w6r_ref,
    wl5_ref, wl6_ref, own_ref, *rest,
):
    o_ref = rest[-1]
    b = pl.program_id(1)
    base = meta_ref[0]
    row_off = meta_ref[1]
    rows = q_ref.shape[1]
    groups = q_ref.shape[2] // HEAD_SIZE
    block_rows = own_ref.shape[1]
    d = HEAD_SIZE

    q = q_ref[0]
    q2 = jnp.concatenate([q[:, h * d:(h + 1) * d] for h in range(groups)], axis=0)

    w5 = jnp.where(b < 2, w5r_ref[0], wl5_ref[0])
    w6 = jnp.where(b < 1, w6r_ref[0], wl6_ref[0])
    blocks = [g0_ref[0], g1_ref[0], r0_ref[0], r1_ref[0], r2_ref[0], w5, w6]
    own = own_ref[0]
    keys = jnp.concatenate([blk[:, :d] for blk in blocks], axis=0)
    vals = jnp.concatenate([blk[:, d:] for blk in blocks], axis=0)
    front = keys.shape[0]

    dims = (((1,), (1,)), ((), ()))
    pv = (((1,), (0,)), ((), ()))
    glob_b = base + b

    def compute(masked):
        ks = ks_ref[0, 0]
        vs = vs_ref[0, 0]
        s_a = lax.dot_general(q2, keys, dims, preferred_element_type=jnp.float32)
        s_a = s_a * ks[:, :front]
        if masked:
            col = lax.broadcasted_iota(jnp.int32, (1, front), 1)
            bad = ((col >= 5 * block_rows) & (col < 6 * block_rows) & (glob_b < 2)) | (
                (col >= 6 * block_rows) & (glob_b < 1)
            )
            s_a = jnp.where(bad, -jnp.inf, s_a)
        s_b = lax.dot_general(q2, own[:, :d], dims, preferred_element_type=jnp.float32)
        s_b = s_b * ks[:, front:]
        kcol = lax.broadcasted_iota(jnp.int32, (1, block_rows), 1)
        row = lax.broadcasted_iota(jnp.int32, (groups * rows, 1), 0) % rows + row_off
        s_b = jnp.where(kcol <= row, s_b, -jnp.inf)
        m = jnp.maximum(jnp.max(s_a, axis=1, keepdims=True), jnp.max(s_b, axis=1, keepdims=True))
        p_a = jnp.exp2(s_a - m)
        p_b = jnp.exp2(s_b - m)
        totals = jnp.sum(p_a, axis=1, keepdims=True) + jnp.sum(p_b, axis=1, keepdims=True)
        w_a = (p_a * vs[:, :front]).astype(jnp.bfloat16)
        w_b = (p_b * vs[:, front:]).astype(jnp.bfloat16)
        acc = lax.dot_general(w_a, vals, pv, preferred_element_type=jnp.float32)
        acc = acc + lax.dot_general(w_b, own[:, d:], pv, preferred_element_type=jnp.float32)
        res = (acc / totals).astype(o_ref.dtype)
        for h in range(groups):
            o_ref[0, :, h * d:(h + 1) * d] = res[h * rows:(h + 1) * rows]

    @pl.when(glob_b < 2)
    def _():
        compute(True)

    @pl.when(glob_b >= 2)
    def _():
        compute(False)


def body(queries, cache_kv, cache_scale, prompt_key_value, prompt_scale, rand_blocks):
    ctx_count = lax.axis_size("ctx")
    ctx_index = lax.axis_index("ctx")
    sub_count = lax.axis_size("sub")
    sub_index = lax.axis_index("sub")
    local_blocks, row_count, query_width = queries.shape
    cache_blocks, block_rows, kv_width = cache_kv.shape
    head_dim = HEAD_SIZE
    kvw = 2 * head_dim
    local_heads = kv_width // kvw
    query_groups = query_width // (local_heads * head_dim)
    qw = query_groups * head_dim
    rand_count = rand_blocks.shape[1]
    capacity = max(2, (local_blocks * rand_count + ctx_count - 1) // ctx_count)
    split = sub_count == 2 and local_heads % 2 == 0
    my_heads = local_heads // 2 if split else local_heads
    head_off = sub_index * my_heads if split else jnp.int32(0)
    swap = [(0, 1), (1, 0)]

    if split:
        partner_q = lax.dynamic_slice_in_dim(
            queries, (1 - sub_index) * my_heads * qw, my_heads * qw, axis=2
        )
        partner_q = lax.ppermute(partner_q, "sub", swap)
        cache_mine = None
        prompt_mine = lax.dynamic_slice_in_dim(
            prompt_key_value[local_blocks - WIN:], head_off * kvw, my_heads * kvw, axis=2
        )
    else:
        cache_mine = cache_kv
        prompt_mine = prompt_key_value[local_blocks - WIN:]

    window_part = passed_along(prompt_mine, "ctx", 1)
    if split:
        global_src = lax.dynamic_slice_in_dim(cache_kv[:NG], head_off * kvw, my_heads * kvw, axis=2)
    else:
        global_src = cache_kv[:NG]
    global_part = from_root(global_src, "ctx")

    per_reader = rand_blocks.reshape(ctx_count, local_blocks * rand_count)
    owners = per_reader // cache_blocks
    owner_hot = (
        owners[:, :, None] == jnp.arange(ctx_count, dtype=jnp.int32)[None, None, :]
    ).astype(jnp.int32)
    slot_rank = jnp.sum((jnp.cumsum(owner_hot, axis=1) - 1) * owner_hot, axis=2)
    picked = (
        (owners == ctx_index)[:, :, None]
        & (slot_rank[:, :, None] == jnp.arange(capacity, dtype=jnp.int32)[None, None, :])
    ).astype(jnp.int32)
    local_ids = jnp.sum(picked * (per_reader % cache_blocks)[:, :, None], axis=1)
    send_ids = jnp.clip(local_ids.reshape(-1), 0, cache_blocks - 1).astype(jnp.int32)
    chunks = 2 if my_heads % 2 == 0 else 1
    chunk_heads = my_heads // chunks
    chunk_width = chunk_heads * kvw
    incoming = []
    for c in range(chunks):
        col = jnp.reshape((head_off + c * chunk_heads) * kvw, (1,)).astype(jnp.int32)
        piece = gather_blocks(cache_kv, send_ids, col, chunk_width)
        if incoming:
            piece, _ = lax.optimization_barrier((piece, incoming[-1]))
        incoming.append(lax.all_to_all(piece, "ctx", split_axis=0, concat_axis=0, tiled=True))

    own_refs = lax.dynamic_index_in_dim(per_reader, ctx_index, 0, keepdims=False)
    own_ranks = lax.dynamic_index_in_dim(slot_rank, ctx_index, 0, keepdims=False)
    own_ranks = jnp.minimum(own_ranks, capacity - 1)
    rpos = (own_refs // cache_blocks * capacity + own_ranks).astype(jnp.int32)
    rpos = rpos.reshape(-1)

    local_order = jnp.arange(local_blocks, dtype=jnp.int32)
    global_order = ctx_index * local_blocks + local_order
    steps_back = jnp.arange(WIN, 0, -1, dtype=jnp.int32)
    back_global = global_order[:, None] - steps_back[None, :]
    cache_ids = jnp.concatenate(
        [
            jnp.broadcast_to(jnp.arange(NG, dtype=jnp.int32)[None, :], (local_blocks, NG)),
            own_refs.reshape(local_blocks, rand_count),
        ],
        axis=1,
    )
    prompt_ids = jnp.concatenate([jnp.maximum(back_global, 0), global_order[:, None]], axis=1)
    scale_row_table = jnp.concatenate(
        [jnp.take(cache_scale, cache_ids, axis=0), jnp.take(prompt_scale, prompt_ids, axis=0)],
        axis=1,
    )
    key_total = scale_row_table.shape[1]
    scale_row_table = scale_row_table.reshape(local_blocks, key_total, local_heads, 2)
    scale_row_table = jnp.transpose(scale_row_table, (0, 2, 3, 1))
    key_scale = scale_row_table[:, :, 0] / math.sqrt(head_dim) * math.log2(math.e)
    key_scale = jnp.repeat(key_scale, block_rows, axis=-1)
    value_scale = jnp.repeat(scale_row_table[:, :, 1], block_rows, axis=-1)
    key_scale = key_scale.reshape(local_blocks, local_heads, 1, key_total * block_rows)
    value_scale = value_scale.reshape(local_blocks, local_heads, 1, key_total * block_rows)

    def run(q_array, q_head_off, row_off, out_width, out_head_off, c, prev):
        c_off = c * chunk_heads
        meta = jnp.stack(
            [ctx_index * local_blocks, row_off, q_head_off + c_off, head_off + c_off,
             out_head_off + c_off, jnp.int32(c_off)]
        )
        meta = meta.astype(jnp.int32)

        def kv_spec(index_fn):
            return pl.BlockSpec((1, block_rows, kvw), index_fn)

        in_specs = [
            pl.BlockSpec((1, row_count, qw), lambda g, b, rp, mt: (b, 0, mt[2] + g)),
            pl.BlockSpec((1, 1, 1, key_total * block_rows), lambda g, b, rp, mt: (b, mt[3] + g, 0, 0)),
            pl.BlockSpec((1, 1, 1, key_total * block_rows), lambda g, b, rp, mt: (b, mt[3] + g, 0, 0)),
            kv_spec(lambda g, b, rp, mt: (0, 0, mt[5] + g)),
            kv_spec(lambda g, b, rp, mt: (1, 0, mt[5] + g)),
            kv_spec(lambda g, b, rp, mt: (rp[b * 3], 0, g)),
            kv_spec(lambda g, b, rp, mt: (rp[b * 3 + 1], 0, g)),
            kv_spec(lambda g, b, rp, mt: (rp[b * 3 + 2], 0, g)),
            kv_spec(lambda g, b, rp, mt: (jnp.minimum(b, 1), 0, mt[5] + g)),
            kv_spec(lambda g, b, rp, mt: (1, 0, mt[5] + g)),
            kv_spec(lambda g, b, rp, mt: (jnp.maximum(b - 2, 0), 0, mt[3] + g)),
            kv_spec(lambda g, b, rp, mt: (jnp.maximum(b - 1, 0), 0, mt[3] + g)),
            kv_spec(lambda g, b, rp, mt: (b, 0, mt[3] + g)),
        ]
        args = [
            q_array, key_scale, value_scale,
            global_part, global_part, incoming[c], incoming[c], incoming[c], window_part, window_part,
            prompt_key_value, prompt_key_value, prompt_key_value,
        ]
        aliases = {}
        if prev is not None:
            in_specs.append(pl.BlockSpec(memory_space=pl.ANY))
            aliases = {2 + len(args): 0}
            args.append(prev)
        steps = chunk_heads * local_blocks
        out_spec = pl.BlockSpec((1, row_count, qw), lambda g, b, rp, mt: (b, 0, mt[4] + g))
        call = pl.pallas_call(
            attention_kernel,
            out_shape=jax.ShapeDtypeStruct((local_blocks, row_count, out_width), queries.dtype),
            grid_spec=pltpu.PrefetchScalarGridSpec(
                num_scalar_prefetch=2,
                grid=(chunk_heads, local_blocks),
                in_specs=in_specs,
                out_specs=out_spec,
            ),
            input_output_aliases=aliases,
            cost_estimate=pl.CostEstimate(
                flops=steps * 4 * query_groups * row_count * key_total * block_rows * head_dim,
                transcendentals=steps * query_groups * row_count * key_total * block_rows,
                bytes_accessed=steps * 2 * (2 * row_count * qw + key_total * block_rows * kvw),
            ),
            compiler_params=pltpu.CompilerParams(
                dimension_semantics=("arbitrary", "arbitrary"),
                vmem_limit_bytes=48 * 1024 * 1024,
            ),
        )
        return call(rpos, meta, *args)

    zero = jnp.int32(0)
    if not split:
        out = None
        for c in range(chunks):
            out = run(queries, zero, sub_index * row_count, query_width, zero, c, out)
        return out
    for_partner = None
    mine = None
    from_partner = None
    partner_in = partner_q
    for c in range(chunks):
        if mine is not None:
            partner_in, mine = lax.optimization_barrier((partner_q, mine))
        for_partner = run(
            partner_in, zero, (1 - sub_index) * row_count, my_heads * qw, zero, c, for_partner
        )
        if c == chunks - 1:
            from_partner = lax.ppermute(for_partner, "sub", swap)
        mine = run(queries, head_off, sub_index * row_count, query_width, head_off, c, mine)
    return lax.dynamic_update_slice_in_dim(mine, from_partner, (1 - sub_index) * my_heads * qw, axis=2)


def solution(mesh):
    in_specs = (
        P(("group", "ctx"), "sub", "kvh"),
        P(("group", "ctx"), None, "kvh"),
        P("group", "kvh"),
        P(("group", "ctx"), None, "kvh"),
        P("group", "kvh"),
        P("group", None),
    )
    out_specs = P(("group", "ctx"), "sub", "kvh")
    return jax.shard_map(body, mesh=mesh, in_specs=in_specs, out_specs=out_specs, check_vma=False)
```

```python
import math

import jax
import jax.numpy as jnp
from jax import lax
from jax.experimental import pallas as pl
from jax.experimental.pallas import tpu as pltpu
from jax.sharding import PartitionSpec as P

HEAD_SIZE = 128

NG = 2
WIN = 2


def passed_along(block, axis, distance):
    devices = range(lax.axis_size(axis))
    route = [(i - distance, i) for i in devices if i - distance in devices]
    return lax.ppermute(block, axis, route)


def from_root(block, axis):
    count = lax.axis_size(axis)
    index = lax.axis_index(axis)
    have = block
    for dist in range(1, count):
        got = lax.ppermute(block, axis, [(0, dist)])
        have = jnp.where(index == dist, got, have)
    return have


def place_kernel(off_ref, src_ref, prev_ref, out_ref):
    out_ref[...] = src_ref[...]


def place_columns(dest, src, block_index):
    return pl.pallas_call(
        place_kernel,
        out_shape=jax.ShapeDtypeStruct(dest.shape, dest.dtype),
        grid_spec=pltpu.PrefetchScalarGridSpec(
            num_scalar_prefetch=1,
            grid=(1,),
            in_specs=[
                pl.BlockSpec(src.shape, lambda i, off: (0, 0, 0)),
                pl.BlockSpec(memory_space=pl.ANY),
            ],
            out_specs=pl.BlockSpec(src.shape, lambda i, off: (0, 0, off[0])),
        ),
        input_output_aliases={2: 0},
        compiler_params=pltpu.CompilerParams(vmem_limit_bytes=48 * 1024 * 1024),
    )(block_index, src, dest)


def attention_kernel(
    rpos_ref, meta_ref,
    q_ref, ks_ref, vs_ref,
    g0_ref, g1_ref, r0_ref, r1_ref, r2_ref, w5r_ref, w6r_ref,
    wl5_ref, wl6_ref, own_ref, *rest,
):
    o_ref = rest[-1]
    b = pl.program_id(1)
    base = meta_ref[0]
    row_off = meta_ref[1]
    rows = q_ref.shape[1]
    groups = q_ref.shape[2] // HEAD_SIZE
    block_rows = own_ref.shape[1]
    d = HEAD_SIZE

    q = q_ref[0]
    q2 = jnp.concatenate([q[:, h * d:(h + 1) * d] for h in range(groups)], axis=0)

    w5 = jnp.where(b < 2, w5r_ref[0], wl5_ref[0])
    w6 = jnp.where(b < 1, w6r_ref[0], wl6_ref[0])
    blocks = [g0_ref[0], g1_ref[0], r0_ref[0], r1_ref[0], r2_ref[0], w5, w6]
    own = own_ref[0]
    keys = jnp.concatenate([blk[:, :d] for blk in blocks], axis=0)
    vals = jnp.concatenate([blk[:, d:] for blk in blocks], axis=0)
    front = keys.shape[0]

    dims = (((1,), (1,)), ((), ()))
    pv = (((1,), (0,)), ((), ()))
    glob_b = base + b

    def compute(masked):
        ks = ks_ref[0, 0]
        vs = vs_ref[0, 0]
        s_a = lax.dot_general(q2, keys, dims, preferred_element_type=jnp.float32)
        s_a = s_a * ks[:, :front]
        if masked:
            col = lax.broadcasted_iota(jnp.int32, (1, front), 1)
            bad = ((col >= 5 * block_rows) & (col < 6 * block_rows) & (glob_b < 2)) | (
                (col >= 6 * block_rows) & (glob_b < 1)
            )
            s_a = jnp.where(bad, -jnp.inf, s_a)
        s_b = lax.dot_general(q2, own[:, :d], dims, preferred_element_type=jnp.float32)
        s_b = s_b * ks[:, front:]
        kcol = lax.broadcasted_iota(jnp.int32, (1, block_rows), 1)
        row = lax.broadcasted_iota(jnp.int32, (groups * rows, 1), 0) % rows + row_off
        s_b = jnp.where(kcol <= row, s_b, -jnp.inf)
        m = jnp.maximum(jnp.max(s_a, axis=1, keepdims=True), jnp.max(s_b, axis=1, keepdims=True))
        p_a = jnp.exp2(s_a - m)
        p_b = jnp.exp2(s_b - m)
        totals = jnp.sum(p_a, axis=1, keepdims=True) + jnp.sum(p_b, axis=1, keepdims=True)
        w_a = (p_a * vs[:, :front]).astype(jnp.bfloat16)
        w_b = (p_b * vs[:, front:]).astype(jnp.bfloat16)
        acc = lax.dot_general(w_a, vals, pv, preferred_element_type=jnp.float32)
        acc = acc + lax.dot_general(w_b, own[:, d:], pv, preferred_element_type=jnp.float32)
        res = (acc / totals).astype(o_ref.dtype)
        for h in range(groups):
            o_ref[0, :, h * d:(h + 1) * d] = res[h * rows:(h + 1) * rows]

    @pl.when(glob_b < 2)
    def _():
        compute(True)

    @pl.when(glob_b >= 2)
    def _():
        compute(False)


def body(queries, cache_kv, cache_scale, prompt_key_value, prompt_scale, rand_blocks):
    ctx_count = lax.axis_size("ctx")
    ctx_index = lax.axis_index("ctx")
    sub_count = lax.axis_size("sub")
    sub_index = lax.axis_index("sub")
    local_blocks, row_count, query_width = queries.shape
    cache_blocks, block_rows, kv_width = cache_kv.shape
    head_dim = HEAD_SIZE
    kvw = 2 * head_dim
    local_heads = kv_width // kvw
    query_groups = query_width // (local_heads * head_dim)
    qw = query_groups * head_dim
    rand_count = rand_blocks.shape[1]
    capacity = max(2, (local_blocks * rand_count + ctx_count - 1) // ctx_count)
    split = sub_count == 2 and local_heads % 2 == 0
    my_heads = local_heads // 2 if split else local_heads
    head_off = sub_index * my_heads if split else jnp.int32(0)
    swap = [(0, 1), (1, 0)]

    if split:
        partner_q = lax.dynamic_slice_in_dim(
            queries, (1 - sub_index) * my_heads * qw, my_heads * qw, axis=2
        )
        partner_q = lax.ppermute(partner_q, "sub", swap)
        cache_mine = None
        prompt_mine = lax.dynamic_slice_in_dim(
            prompt_key_value[local_blocks - WIN:], head_off * kvw, my_heads * kvw, axis=2
        )
    else:
        cache_mine = cache_kv
        prompt_mine = prompt_key_value[local_blocks - WIN:]

    window_part = passed_along(prompt_mine, "ctx", 1)
    if split:
        global_src = lax.dynamic_slice_in_dim(cache_kv[:NG], head_off * kvw, my_heads * kvw, axis=2)
    else:
        global_src = cache_kv[:NG]
    global_part = from_root(global_src, "ctx")

    per_reader = rand_blocks.reshape(ctx_count, local_blocks * rand_count)
    owners = per_reader // cache_blocks
    owner_hot = (
        owners[:, :, None] == jnp.arange(ctx_count, dtype=jnp.int32)[None, None, :]
    ).astype(jnp.int32)
    slot_rank = jnp.sum((jnp.cumsum(owner_hot, axis=1) - 1) * owner_hot, axis=2)
    picked = (
        (owners == ctx_index)[:, :, None]
        & (slot_rank[:, :, None] == jnp.arange(capacity, dtype=jnp.int32)[None, None, :])
    ).astype(jnp.int32)
    local_ids = jnp.sum(picked * (per_reader % cache_blocks)[:, :, None], axis=1)
    send_ids = local_ids.reshape(-1)
    chunks = 2 if my_heads % 2 == 0 else 1
    chunk_heads = my_heads // chunks
    chunk_width = chunk_heads * kvw
    incoming = []
    for c in range(chunks):
        if split:
            source = lax.dynamic_slice_in_dim(
                cache_kv, (head_off + c * chunk_heads) * kvw, chunk_width, axis=2
            )
        else:
            source = cache_mine[:, :, c * chunk_width:(c + 1) * chunk_width]
        piece = jnp.take(source, send_ids, axis=0, mode="clip")
        if incoming:
            piece, _ = lax.optimization_barrier((piece, incoming[-1]))
        incoming.append(lax.all_to_all(piece, "ctx", split_axis=0, concat_axis=0, tiled=True))

    own_refs = lax.dynamic_index_in_dim(per_reader, ctx_index, 0, keepdims=False)
    own_ranks = lax.dynamic_index_in_dim(slot_rank, ctx_index, 0, keepdims=False)
    own_ranks = jnp.minimum(own_ranks, capacity - 1)
    rpos = (own_refs // cache_blocks * capacity + own_ranks).astype(jnp.int32)
    rpos = rpos.reshape(-1)

    local_order = jnp.arange(local_blocks, dtype=jnp.int32)
    global_order = ctx_index * local_blocks + local_order
    steps_back = jnp.arange(WIN, 0, -1, dtype=jnp.int32)
    back_global = global_order[:, None] - steps_back[None, :]
    cache_ids = jnp.concatenate(
        [
            jnp.broadcast_to(jnp.arange(NG, dtype=jnp.int32)[None, :], (local_blocks, NG)),
            own_refs.reshape(local_blocks, rand_count),
        ],
        axis=1,
    )
    prompt_ids = jnp.concatenate([jnp.maximum(back_global, 0), global_order[:, None]], axis=1)
    scale_row_table = jnp.concatenate(
        [jnp.take(cache_scale, cache_ids, axis=0), jnp.take(prompt_scale, prompt_ids, axis=0)],
        axis=1,
    )
    key_total = scale_row_table.shape[1]
    scale_row_table = scale_row_table.reshape(local_blocks, key_total, local_heads, 2)
    scale_row_table = jnp.transpose(scale_row_table, (0, 2, 3, 1))
    key_scale = scale_row_table[:, :, 0] / math.sqrt(head_dim) * math.log2(math.e)
    key_scale = jnp.repeat(key_scale, block_rows, axis=-1)
    value_scale = jnp.repeat(scale_row_table[:, :, 1], block_rows, axis=-1)
    key_scale = key_scale.reshape(local_blocks, local_heads, 1, key_total * block_rows)
    value_scale = value_scale.reshape(local_blocks, local_heads, 1, key_total * block_rows)

    def run(q_array, q_head_off, row_off, out_width, out_head_off, c, prev):
        c_off = c * chunk_heads
        meta = jnp.stack(
            [ctx_index * local_blocks, row_off, q_head_off + c_off, head_off + c_off,
             out_head_off + c_off, jnp.int32(c_off)]
        )
        meta = meta.astype(jnp.int32)

        def kv_spec(index_fn):
            return pl.BlockSpec((1, block_rows, kvw), index_fn)

        in_specs = [
            pl.BlockSpec((1, row_count, qw), lambda g, b, rp, mt: (b, 0, mt[2] + g)),
            pl.BlockSpec((1, 1, 1, key_total * block_rows), lambda g, b, rp, mt: (b, mt[3] + g, 0, 0)),
            pl.BlockSpec((1, 1, 1, key_total * block_rows), lambda g, b, rp, mt: (b, mt[3] + g, 0, 0)),
            kv_spec(lambda g, b, rp, mt: (0, 0, mt[5] + g)),
            kv_spec(lambda g, b, rp, mt: (1, 0, mt[5] + g)),
            kv_spec(lambda g, b, rp, mt: (rp[b * 3], 0, g)),
            kv_spec(lambda g, b, rp, mt: (rp[b * 3 + 1], 0, g)),
            kv_spec(lambda g, b, rp, mt: (rp[b * 3 + 2], 0, g)),
            kv_spec(lambda g, b, rp, mt: (jnp.minimum(b, 1), 0, mt[5] + g)),
            kv_spec(lambda g, b, rp, mt: (1, 0, mt[5] + g)),
            kv_spec(lambda g, b, rp, mt: (jnp.maximum(b - 2, 0), 0, mt[3] + g)),
            kv_spec(lambda g, b, rp, mt: (jnp.maximum(b - 1, 0), 0, mt[3] + g)),
            kv_spec(lambda g, b, rp, mt: (b, 0, mt[3] + g)),
        ]
        args = [
            q_array, key_scale, value_scale,
            global_part, global_part, incoming[c], incoming[c], incoming[c], window_part, window_part,
            prompt_key_value, prompt_key_value, prompt_key_value,
        ]
        aliases = {}
        if prev is not None:
            in_specs.append(pl.BlockSpec(memory_space=pl.ANY))
            aliases = {2 + len(args): 0}
            args.append(prev)
        steps = chunk_heads * local_blocks
        out_spec = pl.BlockSpec((1, row_count, qw), lambda g, b, rp, mt: (b, 0, mt[4] + g))
        call = pl.pallas_call(
            attention_kernel,
            out_shape=jax.ShapeDtypeStruct((local_blocks, row_count, out_width), queries.dtype),
            grid_spec=pltpu.PrefetchScalarGridSpec(
                num_scalar_prefetch=2,
                grid=(chunk_heads, local_blocks),
                in_specs=in_specs,
                out_specs=out_spec,
            ),
            input_output_aliases=aliases,
            cost_estimate=pl.CostEstimate(
                flops=steps * 4 * query_groups * row_count * key_total * block_rows * head_dim,
                transcendentals=steps * query_groups * row_count * key_total * block_rows,
                bytes_accessed=steps * 2 * (2 * row_count * qw + key_total * block_rows * kvw),
            ),
            compiler_params=pltpu.CompilerParams(
                dimension_semantics=("arbitrary", "arbitrary"),
                vmem_limit_bytes=48 * 1024 * 1024,
            ),
        )
        return call(rpos, meta, *args)

    zero = jnp.int32(0)
    if not split:
        out = None
        for c in range(chunks):
            out = run(queries, zero, sub_index * row_count, query_width, zero, c, out)
        return out
    for_partner = None
    mine = None
    from_partner = None
    partner_in = partner_q
    for c in range(chunks):
        if mine is not None:
            partner_in, mine = lax.optimization_barrier((partner_q, mine))
        for_partner = run(
            partner_in, zero, (1 - sub_index) * row_count, my_heads * qw, zero, c, for_partner
        )
        if c == chunks - 1:
            from_partner = lax.ppermute(for_partner, "sub", swap)
        mine = run(queries, head_off, sub_index * row_count, query_width, head_off, c, mine)
    return place_columns(mine, from_partner, jnp.reshape(1 - sub_index, (1,)).astype(jnp.int32))


def solution(mesh):
    in_specs = (
        P(("group", "ctx"), "sub", "kvh"),
        P(("group", "ctx"), None, "kvh"),
        P("group", "kvh"),
        P(("group", "ctx"), None, "kvh"),
        P("group", "kvh"),
        P("group", None),
    )
    out_specs = P(("group", "ctx"), "sub", "kvh")
    return jax.shard_map(body, mesh=mesh, in_specs=in_specs, out_specs=out_specs, check_vma=False)
```

```python
import math

import jax
import jax.numpy as jnp
from jax import lax
from jax.experimental import pallas as pl
from jax.experimental.pallas import tpu as pltpu
from jax.sharding import PartitionSpec as P

HEAD_SIZE = 128

NG = 2
WIN = 2


def passed_along(block, axis, distance):
    devices = range(lax.axis_size(axis))
    route = [(i - distance, i) for i in devices if i - distance in devices]
    return lax.ppermute(block, axis, route)


def from_root(block, axis):
    count = lax.axis_size(axis)
    index = lax.axis_index(axis)
    have = block
    for dist in range(1, count):
        got = lax.ppermute(block, axis, [(0, dist)])
        have = jnp.where(index == dist, got, have)
    return have


def place_kernel(off_ref, src_ref, prev_ref, out_ref):
    out_ref[...] = src_ref[...]


def place_columns(dest, src, block_index):
    return pl.pallas_call(
        place_kernel,
        out_shape=jax.ShapeDtypeStruct(dest.shape, dest.dtype),
        grid_spec=pltpu.PrefetchScalarGridSpec(
            num_scalar_prefetch=1,
            grid=(1,),
            in_specs=[
                pl.BlockSpec(src.shape, lambda i, off: (0, 0, 0)),
                pl.BlockSpec(memory_space=pl.ANY),
            ],
            out_specs=pl.BlockSpec(src.shape, lambda i, off: (0, 0, off[0])),
        ),
        input_output_aliases={2: 0},
        compiler_params=pltpu.CompilerParams(vmem_limit_bytes=48 * 1024 * 1024),
    )(block_index, src, dest)


def attention_kernel(rpos_ref, meta_ref, q_ref, ks_ref, vs_ref, *rest):
    o_ref = rest[-1]
    nb = q_ref.shape[0]
    for k in range(nb):
        attend_one(k, nb * pl.program_id(1) + k, meta_ref, q_ref, ks_ref, vs_ref, rest[10 * k:10 * k + 10], o_ref)


def attend_one(k, b, meta_ref, q_ref, ks_ref, vs_ref, kv_refs, o_ref):
    (g0_ref, g1_ref, r0_ref, r1_ref, r2_ref, w5r_ref, w6r_ref, wl5_ref, wl6_ref, own_ref) = kv_refs
    base = meta_ref[0]
    row_off = meta_ref[1]
    rows = q_ref.shape[1]
    groups = q_ref.shape[2] // HEAD_SIZE
    block_rows = own_ref.shape[1]
    d = HEAD_SIZE

    q = q_ref[k]
    q2 = jnp.concatenate([q[:, h * d:(h + 1) * d] for h in range(groups)], axis=0)

    w5 = jnp.where(b < 2, w5r_ref[0], wl5_ref[0])
    w6 = jnp.where(b < 1, w6r_ref[0], wl6_ref[0])
    blocks = [g0_ref[0], g1_ref[0], r0_ref[0], r1_ref[0], r2_ref[0], w5, w6]
    own = own_ref[0]
    keys = jnp.concatenate([blk[:, :d] for blk in blocks], axis=0)
    vals = jnp.concatenate([blk[:, d:] for blk in blocks], axis=0)
    front = keys.shape[0]

    dims = (((1,), (1,)), ((), ()))
    pv = (((1,), (0,)), ((), ()))
    glob_b = base + b

    def compute(masked):
        ks = ks_ref[k, 0]
        vs = vs_ref[k, 0]
        s_a = lax.dot_general(q2, keys, dims, preferred_element_type=jnp.float32)
        s_a = s_a * ks[:, :front]
        if masked:
            col = lax.broadcasted_iota(jnp.int32, (1, front), 1)
            bad = ((col >= 5 * block_rows) & (col < 6 * block_rows) & (glob_b < 2)) | (
                (col >= 6 * block_rows) & (glob_b < 1)
            )
            s_a = jnp.where(bad, -jnp.inf, s_a)
        s_b = lax.dot_general(q2, own[:, :d], dims, preferred_element_type=jnp.float32)
        s_b = s_b * ks[:, front:]
        kcol = lax.broadcasted_iota(jnp.int32, (1, block_rows), 1)
        row = lax.broadcasted_iota(jnp.int32, (groups * rows, 1), 0) % rows + row_off
        s_b = jnp.where(kcol <= row, s_b, -jnp.inf)
        m = jnp.maximum(jnp.max(s_a, axis=1, keepdims=True), jnp.max(s_b, axis=1, keepdims=True))
        p_a = jnp.exp2(s_a - m)
        p_b = jnp.exp2(s_b - m)
        totals = jnp.sum(p_a, axis=1, keepdims=True) + jnp.sum(p_b, axis=1, keepdims=True)
        w_a = (p_a * vs[:, :front]).astype(jnp.bfloat16)
        w_b = (p_b * vs[:, front:]).astype(jnp.bfloat16)
        acc = lax.dot_general(w_a, vals, pv, preferred_element_type=jnp.float32)
        acc = acc + lax.dot_general(w_b, own[:, d:], pv, preferred_element_type=jnp.float32)
        res = (acc / totals).astype(o_ref.dtype)
        for h in range(groups):
            o_ref[k, :, h * d:(h + 1) * d] = res[h * rows:(h + 1) * rows]

    @pl.when(glob_b < 2)
    def _():
        compute(True)

    @pl.when(glob_b >= 2)
    def _():
        compute(False)


def body(queries, cache_kv, cache_scale, prompt_key_value, prompt_scale, rand_blocks):
    ctx_count = lax.axis_size("ctx")
    ctx_index = lax.axis_index("ctx")
    sub_count = lax.axis_size("sub")
    sub_index = lax.axis_index("sub")
    local_blocks, row_count, query_width = queries.shape
    cache_blocks, block_rows, kv_width = cache_kv.shape
    head_dim = HEAD_SIZE
    kvw = 2 * head_dim
    local_heads = kv_width // kvw
    query_groups = query_width // (local_heads * head_dim)
    qw = query_groups * head_dim
    rand_count = rand_blocks.shape[1]
    capacity = max(2, (local_blocks * rand_count + ctx_count - 1) // ctx_count)
    split = sub_count == 2 and local_heads % 2 == 0
    my_heads = local_heads // 2 if split else local_heads
    head_off = sub_index * my_heads if split else jnp.int32(0)
    swap = [(0, 1), (1, 0)]

    if split:
        partner_q = lax.dynamic_slice_in_dim(
            queries, (1 - sub_index) * my_heads * qw, my_heads * qw, axis=2
        )
        partner_q = lax.ppermute(partner_q, "sub", swap)
        cache_mine = None
        prompt_mine = lax.dynamic_slice_in_dim(
            prompt_key_value[local_blocks - WIN:], head_off * kvw, my_heads * kvw, axis=2
        )
    else:
        cache_mine = cache_kv
        prompt_mine = prompt_key_value[local_blocks - WIN:]

    window_part = passed_along(prompt_mine, "ctx", 1)
    if split:
        global_src = lax.dynamic_slice_in_dim(cache_kv[:NG], head_off * kvw, my_heads * kvw, axis=2)
    else:
        global_src = cache_kv[:NG]
    global_part = from_root(global_src, "ctx")

    per_reader = rand_blocks.reshape(ctx_count, local_blocks * rand_count)
    owners = per_reader // cache_blocks
    owner_hot = (
        owners[:, :, None] == jnp.arange(ctx_count, dtype=jnp.int32)[None, None, :]
    ).astype(jnp.int32)
    slot_rank = jnp.sum((jnp.cumsum(owner_hot, axis=1) - 1) * owner_hot, axis=2)
    picked = (
        (owners == ctx_index)[:, :, None]
        & (slot_rank[:, :, None] == jnp.arange(capacity, dtype=jnp.int32)[None, None, :])
    ).astype(jnp.int32)
    local_ids = jnp.sum(picked * (per_reader % cache_blocks)[:, :, None], axis=1)
    send_ids = local_ids.reshape(-1)
    chunks = 2 if my_heads % 2 == 0 else 1
    chunk_heads = my_heads // chunks
    chunk_width = chunk_heads * kvw
    incoming = []
    for c in range(chunks):
        if split:
            source = lax.dynamic_slice_in_dim(
                cache_kv, (head_off + c * chunk_heads) * kvw, chunk_width, axis=2
            )
        else:
            source = cache_mine[:, :, c * chunk_width:(c + 1) * chunk_width]
        piece = jnp.take(source, send_ids, axis=0, mode="clip")
        if incoming:
            piece, _ = lax.optimization_barrier((piece, incoming[-1]))
        incoming.append(lax.all_to_all(piece, "ctx", split_axis=0, concat_axis=0, tiled=True))

    own_refs = lax.dynamic_index_in_dim(per_reader, ctx_index, 0, keepdims=False)
    own_ranks = lax.dynamic_index_in_dim(slot_rank, ctx_index, 0, keepdims=False)
    own_ranks = jnp.minimum(own_ranks, capacity - 1)
    rpos = (own_refs // cache_blocks * capacity + own_ranks).astype(jnp.int32)
    rpos = rpos.reshape(-1)

    local_order = jnp.arange(local_blocks, dtype=jnp.int32)
    global_order = ctx_index * local_blocks + local_order
    steps_back = jnp.arange(WIN, 0, -1, dtype=jnp.int32)
    back_global = global_order[:, None] - steps_back[None, :]
    cache_ids = jnp.concatenate(
        [
            jnp.broadcast_to(jnp.arange(NG, dtype=jnp.int32)[None, :], (local_blocks, NG)),
            own_refs.reshape(local_blocks, rand_count),
        ],
        axis=1,
    )
    prompt_ids = jnp.concatenate([jnp.maximum(back_global, 0), global_order[:, None]], axis=1)
    scale_row_table = jnp.concatenate(
        [jnp.take(cache_scale, cache_ids, axis=0), jnp.take(prompt_scale, prompt_ids, axis=0)],
        axis=1,
    )
    key_total = scale_row_table.shape[1]
    scale_row_table = scale_row_table.reshape(local_blocks, key_total, local_heads, 2)
    scale_row_table = jnp.transpose(scale_row_table, (0, 2, 3, 1))
    key_scale = scale_row_table[:, :, 0] / math.sqrt(head_dim) * math.log2(math.e)
    key_scale = jnp.repeat(key_scale, block_rows, axis=-1)
    value_scale = jnp.repeat(scale_row_table[:, :, 1], block_rows, axis=-1)
    key_scale = key_scale.reshape(local_blocks, local_heads, 1, key_total * block_rows)
    value_scale = value_scale.reshape(local_blocks, local_heads, 1, key_total * block_rows)

    def run(q_array, q_head_off, row_off, out_width, out_head_off, c, prev):
        c_off = c * chunk_heads
        meta = jnp.stack(
            [ctx_index * local_blocks, row_off, q_head_off + c_off, head_off + c_off,
             out_head_off + c_off, jnp.int32(c_off)]
        )
        meta = meta.astype(jnp.int32)

        def kv_spec(index_fn):
            return pl.BlockSpec((1, block_rows, kvw), index_fn)

        nb = 2 if local_blocks % 2 == 0 else 1
        in_specs = [
            pl.BlockSpec((nb, row_count, qw), lambda g, i, rp, mt: (i, 0, mt[2] + g)),
            pl.BlockSpec((nb, 1, 1, key_total * block_rows), lambda g, i, rp, mt: (i, mt[3] + g, 0, 0)),
            pl.BlockSpec((nb, 1, 1, key_total * block_rows), lambda g, i, rp, mt: (i, mt[3] + g, 0, 0)),
        ]
        args = [q_array, key_scale, value_scale]
        for k in range(nb):
            in_specs += [
                kv_spec(lambda g, i, rp, mt: (0, 0, mt[5] + g)),
                kv_spec(lambda g, i, rp, mt: (1, 0, mt[5] + g)),
                kv_spec(lambda g, i, rp, mt, k=k: (rp[(nb * i + k) * 3], 0, g)),
                kv_spec(lambda g, i, rp, mt, k=k: (rp[(nb * i + k) * 3 + 1], 0, g)),
                kv_spec(lambda g, i, rp, mt, k=k: (rp[(nb * i + k) * 3 + 2], 0, g)),
                kv_spec(lambda g, i, rp, mt, k=k: (jnp.minimum(nb * i + k, 1), 0, mt[5] + g)),
                kv_spec(lambda g, i, rp, mt: (1, 0, mt[5] + g)),
                kv_spec(lambda g, i, rp, mt, k=k: (jnp.maximum(nb * i + k - 2, 0), 0, mt[3] + g)),
                kv_spec(lambda g, i, rp, mt, k=k: (jnp.maximum(nb * i + k - 1, 0), 0, mt[3] + g)),
                kv_spec(lambda g, i, rp, mt, k=k: (nb * i + k, 0, mt[3] + g)),
            ]
            args += [
                global_part, global_part, incoming[c], incoming[c], incoming[c], window_part, window_part,
                prompt_key_value, prompt_key_value, prompt_key_value,
            ]
        aliases = {}
        if prev is not None:
            in_specs.append(pl.BlockSpec(memory_space=pl.ANY))
            aliases = {2 + len(args): 0}
            args.append(prev)
        steps = chunk_heads * local_blocks
        out_spec = pl.BlockSpec((nb, row_count, qw), lambda g, i, rp, mt: (i, 0, mt[4] + g))
        call = pl.pallas_call(
            attention_kernel,
            out_shape=jax.ShapeDtypeStruct((local_blocks, row_count, out_width), queries.dtype),
            grid_spec=pltpu.PrefetchScalarGridSpec(
                num_scalar_prefetch=2,
                grid=(chunk_heads, local_blocks // nb),
                in_specs=in_specs,
                out_specs=out_spec,
            ),
            input_output_aliases=aliases,
            cost_estimate=pl.CostEstimate(
                flops=steps * 4 * query_groups * row_count * key_total * block_rows * head_dim,
                transcendentals=steps * query_groups * row_count * key_total * block_rows,
                bytes_accessed=steps * 2 * (2 * row_count * qw + key_total * block_rows * kvw),
            ),
            compiler_params=pltpu.CompilerParams(
                dimension_semantics=("arbitrary", "arbitrary"),
                vmem_limit_bytes=48 * 1024 * 1024,
            ),
        )
        return call(rpos, meta, *args)

    zero = jnp.int32(0)
    if not split:
        out = None
        for c in range(chunks):
            out = run(queries, zero, sub_index * row_count, query_width, zero, c, out)
        return out
    for_partner = None
    mine = None
    from_partner = None
    partner_in = partner_q
    for c in range(chunks):
        if mine is not None:
            partner_in, mine = lax.optimization_barrier((partner_q, mine))
        for_partner = run(
            partner_in, zero, (1 - sub_index) * row_count, my_heads * qw, zero, c, for_partner
        )
        if c == chunks - 1:
            from_partner = lax.ppermute(for_partner, "sub", swap)
        mine = run(queries, head_off, sub_index * row_count, query_width, head_off, c, mine)
    return place_columns(mine, from_partner, jnp.reshape(1 - sub_index, (1,)).astype(jnp.int32))


def solution(mesh):
    in_specs = (
        P(("group", "ctx"), "sub", "kvh"),
        P(("group", "ctx"), None, "kvh"),
        P("group", "kvh"),
        P(("group", "ctx"), None, "kvh"),
        P("group", "kvh"),
        P("group", None),
    )
    out_specs = P(("group", "ctx"), "sub", "kvh")
    return jax.shard_map(body, mesh=mesh, in_specs=in_specs, out_specs=out_specs, check_vma=False)
```

```python
import math

import jax
import jax.numpy as jnp
from jax import lax
from jax.experimental import pallas as pl
from jax.experimental.pallas import tpu as pltpu
from jax.sharding import PartitionSpec as P

HEAD_SIZE = 128

NG = 2
WIN = 2


def passed_along(block, axis, distance):
    devices = range(lax.axis_size(axis))
    route = [(i - distance, i) for i in devices if i - distance in devices]
    return lax.ppermute(block, axis, route)


def from_root(block, axis):
    count = lax.axis_size(axis)
    index = lax.axis_index(axis)
    have = block
    for dist in range(1, count):
        got = lax.ppermute(block, axis, [(0, dist)])
        have = jnp.where(index == dist, got, have)
    return have


def place_kernel(off_ref, src_ref, prev_ref, out_ref):
    out_ref[...] = src_ref[...]


def place_columns(dest, src, block_index):
    return pl.pallas_call(
        place_kernel,
        out_shape=jax.ShapeDtypeStruct(dest.shape, dest.dtype),
        grid_spec=pltpu.PrefetchScalarGridSpec(
            num_scalar_prefetch=1,
            grid=(1,),
            in_specs=[
                pl.BlockSpec(src.shape, lambda i, off: (0, 0, 0)),
                pl.BlockSpec(memory_space=pl.ANY),
            ],
            out_specs=pl.BlockSpec(src.shape, lambda i, off: (0, 0, off[0])),
        ),
        input_output_aliases={2: 0},
        compiler_params=pltpu.CompilerParams(vmem_limit_bytes=48 * 1024 * 1024),
    )(block_index, src, dest)


def attention_kernel(
    rpos_ref, meta_ref,
    q_ref, ks_ref, vs_ref,
    g0_ref, g1_ref, r0_ref, r1_ref, r2_ref, w5r_ref, w6r_ref,
    wl5_ref, wl6_ref, own_ref, *rest,
):
    o_ref = rest[-1]
    b = pl.program_id(1)
    base = meta_ref[0]
    row_off = meta_ref[1]
    rows = q_ref.shape[1]
    groups = q_ref.shape[2] // HEAD_SIZE
    block_rows = own_ref.shape[1]
    d = HEAD_SIZE

    q = q_ref[0]
    q2 = jnp.concatenate([q[:, h * d:(h + 1) * d] for h in range(groups)], axis=0)

    w5 = jnp.where(b < 2, w5r_ref[0], wl5_ref[0])
    w6 = jnp.where(b < 1, w6r_ref[0], wl6_ref[0])
    blocks = [g0_ref[0], g1_ref[0], r0_ref[0], r1_ref[0], r2_ref[0], w5, w6]
    own = own_ref[0]
    keys = jnp.concatenate([blk[:, :d] for blk in blocks], axis=0)
    vals = jnp.concatenate([blk[:, d:] for blk in blocks], axis=0)
    front = keys.shape[0]

    dims = (((1,), (1,)), ((), ()))
    pv = (((1,), (0,)), ((), ()))
    glob_b = base + b

    def compute(masked):
        ks = ks_ref[0, 0]
        vs = vs_ref[0, 0]
        s_a = lax.dot_general(q2, keys, dims, preferred_element_type=jnp.float32)
        s_a = s_a * ks[:, :front]
        if masked:
            col = lax.broadcasted_iota(jnp.int32, (1, front), 1)
            bad = ((col >= 5 * block_rows) & (col < 6 * block_rows) & (glob_b < 2)) | (
                (col >= 6 * block_rows) & (glob_b < 1)
            )
            s_a = jnp.where(bad, -jnp.inf, s_a)
        s_b = lax.dot_general(q2, own[:, :d], dims, preferred_element_type=jnp.float32)
        s_b = s_b * ks[:, front:]
        kcol = lax.broadcasted_iota(jnp.int32, (1, block_rows), 1)
        row = lax.broadcasted_iota(jnp.int32, (groups * rows, 1), 0) % rows + row_off
        s_b = jnp.where(kcol <= row, s_b, -jnp.inf)
        m = jnp.maximum(jnp.max(s_a, axis=1, keepdims=True), jnp.max(s_b, axis=1, keepdims=True))
        p_a = jnp.exp2(s_a - m)
        p_b = jnp.exp2(s_b - m)
        totals = jnp.sum(p_a, axis=1, keepdims=True) + jnp.sum(p_b, axis=1, keepdims=True)
        w_a = (p_a * vs[:, :front]).astype(jnp.bfloat16)
        w_b = (p_b * vs[:, front:]).astype(jnp.bfloat16)
        acc = lax.dot_general(w_a, vals, pv, preferred_element_type=jnp.float32)
        acc = acc + lax.dot_general(w_b, own[:, d:], pv, preferred_element_type=jnp.float32)
        res = (acc / totals).astype(o_ref.dtype)
        for h in range(groups):
            o_ref[0, :, h * d:(h + 1) * d] = res[h * rows:(h + 1) * rows]

    @pl.when(glob_b < 2)
    def _():
        compute(True)

    @pl.when(glob_b >= 2)
    def _():
        compute(False)


def body(queries, cache_kv, cache_scale, prompt_key_value, prompt_scale, rand_blocks):
    ctx_count = lax.axis_size("ctx")
    ctx_index = lax.axis_index("ctx")
    sub_count = lax.axis_size("sub")
    sub_index = lax.axis_index("sub")
    local_blocks, row_count, query_width = queries.shape
    cache_blocks, block_rows, kv_width = cache_kv.shape
    head_dim = HEAD_SIZE
    kvw = 2 * head_dim
    local_heads = kv_width // kvw
    query_groups = query_width // (local_heads * head_dim)
    qw = query_groups * head_dim
    rand_count = rand_blocks.shape[1]
    capacity = max(2, (local_blocks * rand_count + ctx_count - 1) // ctx_count)
    split = sub_count == 2 and local_heads % 2 == 0
    my_heads = local_heads // 2 if split else local_heads
    head_off = sub_index * my_heads if split else jnp.int32(0)
    swap = [(0, 1), (1, 0)]

    if split:
        partner_q = lax.dynamic_slice_in_dim(
            queries, (1 - sub_index) * my_heads * qw, my_heads * qw, axis=2
        )
        partner_q = lax.ppermute(partner_q, "sub", swap)
        cache_mine = None
        prompt_mine = lax.dynamic_slice_in_dim(
            prompt_key_value[local_blocks - WIN:], head_off * kvw, my_heads * kvw, axis=2
        )
    else:
        cache_mine = cache_kv
        prompt_mine = prompt_key_value[local_blocks - WIN:]

    window_part = passed_along(prompt_mine, "ctx", 1)
    if split:
        global_src = lax.dynamic_slice_in_dim(cache_kv[:NG], head_off * kvw, my_heads * kvw, axis=2)
    else:
        global_src = cache_kv[:NG]
    global_part = from_root(global_src, "ctx")

    per_reader = rand_blocks.reshape(ctx_count, local_blocks * rand_count)
    owners = per_reader // cache_blocks
    owner_hot = (
        owners[:, :, None] == jnp.arange(ctx_count, dtype=jnp.int32)[None, None, :]
    ).astype(jnp.int32)
    slot_rank = jnp.sum((jnp.cumsum(owner_hot, axis=1) - 1) * owner_hot, axis=2)
    picked = (
        (owners == ctx_index)[:, :, None]
        & (slot_rank[:, :, None] == jnp.arange(capacity, dtype=jnp.int32)[None, None, :])
    ).astype(jnp.int32)
    local_ids = jnp.sum(picked * (per_reader % cache_blocks)[:, :, None], axis=1)
    send_ids = local_ids.reshape(-1)
    chunks = 2 if my_heads % 2 == 0 else 1
    chunk_heads = my_heads // chunks
    chunk_width = chunk_heads * kvw
    incoming = []
    for c in range(chunks):
        if split:
            source = lax.dynamic_slice_in_dim(
                cache_kv, (head_off + c * chunk_heads) * kvw, chunk_width, axis=2
            )
        else:
            source = cache_mine[:, :, c * chunk_width:(c + 1) * chunk_width]
        piece = jnp.take(source, send_ids, axis=0, mode="clip")
        if incoming:
            piece, _ = lax.optimization_barrier((piece, incoming[-1]))
        if not incoming:
            incoming.append(lax.all_to_all(piece, "ctx", split_axis=0, concat_axis=0, tiled=True))
        else:
            shifted = []
            for dist in range(ctx_count):
                reader = (ctx_index + dist) % ctx_count
                slots = lax.dynamic_slice_in_dim(piece, reader * capacity, capacity, axis=0)
                if dist:
                    route = [(i, (i + dist) % ctx_count) for i in range(ctx_count)]
                    slots = lax.ppermute(slots, "ctx", route)
                shifted.append(slots)
            incoming.append(jnp.concatenate(shifted, axis=0))

    own_refs = lax.dynamic_index_in_dim(per_reader, ctx_index, 0, keepdims=False)
    own_ranks = lax.dynamic_index_in_dim(slot_rank, ctx_index, 0, keepdims=False)
    own_ranks = jnp.minimum(own_ranks, capacity - 1)
    rpos = (own_refs // cache_blocks * capacity + own_ranks).astype(jnp.int32)
    rpos = rpos.reshape(-1)
    back = (ctx_index - own_refs // cache_blocks) % ctx_count
    rpos_shift = (back * capacity + own_ranks).astype(jnp.int32).reshape(-1)

    local_order = jnp.arange(local_blocks, dtype=jnp.int32)
    global_order = ctx_index * local_blocks + local_order
    steps_back = jnp.arange(WIN, 0, -1, dtype=jnp.int32)
    back_global = global_order[:, None] - steps_back[None, :]
    cache_ids = jnp.concatenate(
        [
            jnp.broadcast_to(jnp.arange(NG, dtype=jnp.int32)[None, :], (local_blocks, NG)),
            own_refs.reshape(local_blocks, rand_count),
        ],
        axis=1,
    )
    prompt_ids = jnp.concatenate([jnp.maximum(back_global, 0), global_order[:, None]], axis=1)
    scale_row_table = jnp.concatenate(
        [jnp.take(cache_scale, cache_ids, axis=0), jnp.take(prompt_scale, prompt_ids, axis=0)],
        axis=1,
    )
    key_total = scale_row_table.shape[1]
    scale_row_table = scale_row_table.reshape(local_blocks, key_total, local_heads, 2)
    scale_row_table = jnp.transpose(scale_row_table, (0, 2, 3, 1))
    key_scale = scale_row_table[:, :, 0] / math.sqrt(head_dim) * math.log2(math.e)
    key_scale = jnp.repeat(key_scale, block_rows, axis=-1)
    value_scale = jnp.repeat(scale_row_table[:, :, 1], block_rows, axis=-1)
    key_scale = key_scale.reshape(local_blocks, local_heads, 1, key_total * block_rows)
    value_scale = value_scale.reshape(local_blocks, local_heads, 1, key_total * block_rows)

    def run(q_array, q_head_off, row_off, out_width, out_head_off, c, prev):
        c_off = c * chunk_heads
        meta = jnp.stack(
            [ctx_index * local_blocks, row_off, q_head_off + c_off, head_off + c_off,
             out_head_off + c_off, jnp.int32(c_off)]
        )
        meta = meta.astype(jnp.int32)

        def kv_spec(index_fn):
            return pl.BlockSpec((1, block_rows, kvw), index_fn)

        in_specs = [
            pl.BlockSpec((1, row_count, qw), lambda g, b, rp, mt: (b, 0, mt[2] + g)),
            pl.BlockSpec((1, 1, 1, key_total * block_rows), lambda g, b, rp, mt: (b, mt[3] + g, 0, 0)),
            pl.BlockSpec((1, 1, 1, key_total * block_rows), lambda g, b, rp, mt: (b, mt[3] + g, 0, 0)),
            kv_spec(lambda g, b, rp, mt: (0, 0, mt[5] + g)),
            kv_spec(lambda g, b, rp, mt: (1, 0, mt[5] + g)),
            kv_spec(lambda g, b, rp, mt: (rp[b * 3], 0, g)),
            kv_spec(lambda g, b, rp, mt: (rp[b * 3 + 1], 0, g)),
            kv_spec(lambda g, b, rp, mt: (rp[b * 3 + 2], 0, g)),
            kv_spec(lambda g, b, rp, mt: (jnp.minimum(b, 1), 0, mt[5] + g)),
            kv_spec(lambda g, b, rp, mt: (1, 0, mt[5] + g)),
            kv_spec(lambda g, b, rp, mt: (jnp.maximum(b - 2, 0), 0, mt[3] + g)),
            kv_spec(lambda g, b, rp, mt: (jnp.maximum(b - 1, 0), 0, mt[3] + g)),
            kv_spec(lambda g, b, rp, mt: (b, 0, mt[3] + g)),
        ]
        args = [
            q_array, key_scale, value_scale,
            global_part, global_part, incoming[c], incoming[c], incoming[c], window_part, window_part,
            prompt_key_value, prompt_key_value, prompt_key_value,
        ]
        aliases = {}
        if prev is not None:
            in_specs.append(pl.BlockSpec(memory_space=pl.ANY))
            aliases = {2 + len(args): 0}
            args.append(prev)
        steps = chunk_heads * local_blocks
        out_spec = pl.BlockSpec((1, row_count, qw), lambda g, b, rp, mt: (b, 0, mt[4] + g))
        call = pl.pallas_call(
            attention_kernel,
            out_shape=jax.ShapeDtypeStruct((local_blocks, row_count, out_width), queries.dtype),
            grid_spec=pltpu.PrefetchScalarGridSpec(
                num_scalar_prefetch=2,
                grid=(chunk_heads, local_blocks),
                in_specs=in_specs,
                out_specs=out_spec,
            ),
            input_output_aliases=aliases,
            cost_estimate=pl.CostEstimate(
                flops=steps * 4 * query_groups * row_count * key_total * block_rows * head_dim,
                transcendentals=steps * query_groups * row_count * key_total * block_rows,
                bytes_accessed=steps * 2 * (2 * row_count * qw + key_total * block_rows * kvw),
            ),
            compiler_params=pltpu.CompilerParams(
                dimension_semantics=("arbitrary", "arbitrary"),
                vmem_limit_bytes=48 * 1024 * 1024,
            ),
        )
        return call(rpos if c == 0 else rpos_shift, meta, *args)

    zero = jnp.int32(0)
    if not split:
        out = None
        for c in range(chunks):
            out = run(queries, zero, sub_index * row_count, query_width, zero, c, out)
        return out
    for_partner = None
    mine = None
    from_partner = None
    partner_in = partner_q
    for c in range(chunks):
        if mine is not None:
            partner_in, mine = lax.optimization_barrier((partner_q, mine))
        for_partner = run(
            partner_in, zero, (1 - sub_index) * row_count, my_heads * qw, zero, c, for_partner
        )
        if c == chunks - 1:
            from_partner = lax.ppermute(for_partner, "sub", swap)
        mine = run(queries, head_off, sub_index * row_count, query_width, head_off, c, mine)
    return place_columns(mine, from_partner, jnp.reshape(1 - sub_index, (1,)).astype(jnp.int32))


def solution(mesh):
    in_specs = (
        P(("group", "ctx"), "sub", "kvh"),
        P(("group", "ctx"), None, "kvh"),
        P("group", "kvh"),
        P(("group", "ctx"), None, "kvh"),
        P("group", "kvh"),
        P("group", None),
    )
    out_specs = P(("group", "ctx"), "sub", "kvh")
    return jax.shard_map(body, mesh=mesh, in_specs=in_specs, out_specs=out_specs, check_vma=False)
```

```python
import math

import jax
import jax.numpy as jnp
from jax import lax
from jax.experimental import pallas as pl
from jax.experimental.pallas import tpu as pltpu
from jax.sharding import PartitionSpec as P

HEAD_SIZE = 128

NG = 2
WIN = 2


def passed_along(block, axis, distance):
    devices = range(lax.axis_size(axis))
    route = [(i - distance, i) for i in devices if i - distance in devices]
    return lax.ppermute(block, axis, route)


def from_root(block, axis):
    count = lax.axis_size(axis)
    index = lax.axis_index(axis)
    half = count // 2
    have = block
    for dist in range(1, half + 1):
        got = lax.ppermute(block, axis, [(0, dist)])
        have = jnp.where(index == dist, got, have)
    relay = have
    for dist in range(half + 1, count):
        got = lax.ppermute(relay, axis, [(half, dist)])
        have = jnp.where(index == dist, got, have)
    return have


def place_kernel(off_ref, src_ref, prev_ref, out_ref):
    out_ref[...] = src_ref[...]


def place_columns(dest, src, block_index):
    return pl.pallas_call(
        place_kernel,
        out_shape=jax.ShapeDtypeStruct(dest.shape, dest.dtype),
        grid_spec=pltpu.PrefetchScalarGridSpec(
            num_scalar_prefetch=1,
            grid=(1,),
            in_specs=[
                pl.BlockSpec(src.shape, lambda i, off: (0, 0, 0)),
                pl.BlockSpec(memory_space=pl.ANY),
            ],
            out_specs=pl.BlockSpec(src.shape, lambda i, off: (0, 0, off[0])),
        ),
        input_output_aliases={2: 0},
        compiler_params=pltpu.CompilerParams(vmem_limit_bytes=48 * 1024 * 1024),
    )(block_index, src, dest)


def attention_kernel(
    rpos_ref, meta_ref,
    q_ref, ks_ref, vs_ref,
    g0_ref, g1_ref, r0_ref, r1_ref, r2_ref, w5r_ref, w6r_ref,
    wl5_ref, wl6_ref, own_ref, *rest,
):
    o_ref = rest[-1]
    b = pl.program_id(1)
    base = meta_ref[0]
    row_off = meta_ref[1]
    rows = q_ref.shape[1]
    groups = q_ref.shape[2] // HEAD_SIZE
    block_rows = own_ref.shape[1]
    d = HEAD_SIZE

    q = q_ref[0]
    q2 = jnp.concatenate([q[:, h * d:(h + 1) * d] for h in range(groups)], axis=0)

    w5 = jnp.where(b < 2, w5r_ref[0], wl5_ref[0])
    w6 = jnp.where(b < 1, w6r_ref[0], wl6_ref[0])
    blocks = [g0_ref[0], g1_ref[0], r0_ref[0], r1_ref[0], r2_ref[0], w5, w6]
    own = own_ref[0]
    keys = jnp.concatenate([blk[:, :d] for blk in blocks], axis=0)
    vals = jnp.concatenate([blk[:, d:] for blk in blocks], axis=0)
    front = keys.shape[0]

    dims = (((1,), (1,)), ((), ()))
    pv = (((1,), (0,)), ((), ()))
    glob_b = base + b

    def compute(masked):
        ks = ks_ref[0, 0]
        vs = vs_ref[0, 0]
        s_a = lax.dot_general(q2, keys, dims, preferred_element_type=jnp.float32)
        s_a = s_a * ks[:, :front]
        if masked:
            col = lax.broadcasted_iota(jnp.int32, (1, front), 1)
            bad = ((col >= 5 * block_rows) & (col < 6 * block_rows) & (glob_b < 2)) | (
                (col >= 6 * block_rows) & (glob_b < 1)
            )
            s_a = jnp.where(bad, -jnp.inf, s_a)
        s_b = lax.dot_general(q2, own[:, :d], dims, preferred_element_type=jnp.float32)
        s_b = s_b * ks[:, front:]
        kcol = lax.broadcasted_iota(jnp.int32, (1, block_rows), 1)
        row = lax.broadcasted_iota(jnp.int32, (groups * rows, 1), 0) % rows + row_off
        s_b = jnp.where(kcol <= row, s_b, -jnp.inf)
        m = jnp.maximum(jnp.max(s_a, axis=1, keepdims=True), jnp.max(s_b, axis=1, keepdims=True))
        p_a = jnp.exp2(s_a - m)
        p_b = jnp.exp2(s_b - m)
        totals = jnp.sum(p_a, axis=1, keepdims=True) + jnp.sum(p_b, axis=1, keepdims=True)
        w_a = (p_a * vs[:, :front]).astype(jnp.bfloat16)
        w_b = (p_b * vs[:, front:]).astype(jnp.bfloat16)
        acc = lax.dot_general(w_a, vals, pv, preferred_element_type=jnp.float32)
        acc = acc + lax.dot_general(w_b, own[:, d:], pv, preferred_element_type=jnp.float32)
        res = (acc / totals).astype(o_ref.dtype)
        for h in range(groups):
            o_ref[0, :, h * d:(h + 1) * d] = res[h * rows:(h + 1) * rows]

    @pl.when(glob_b < 2)
    def _():
        compute(True)

    @pl.when(glob_b >= 2)
    def _():
        compute(False)


def body(queries, cache_kv, cache_scale, prompt_key_value, prompt_scale, rand_blocks):
    ctx_count = lax.axis_size("ctx")
    ctx_index = lax.axis_index("ctx")
    sub_count = lax.axis_size("sub")
    sub_index = lax.axis_index("sub")
    local_blocks, row_count, query_width = queries.shape
    cache_blocks, block_rows, kv_width = cache_kv.shape
    head_dim = HEAD_SIZE
    kvw = 2 * head_dim
    local_heads = kv_width // kvw
    query_groups = query_width // (local_heads * head_dim)
    qw = query_groups * head_dim
    rand_count = rand_blocks.shape[1]
    capacity = max(2, (local_blocks * rand_count + ctx_count - 1) // ctx_count)
    split = sub_count == 2 and local_heads % 2 == 0
    my_heads = local_heads // 2 if split else local_heads
    head_off = sub_index * my_heads if split else jnp.int32(0)
    swap = [(0, 1), (1, 0)]

    if split:
        partner_q = lax.dynamic_slice_in_dim(
            queries, (1 - sub_index) * my_heads * qw, my_heads * qw, axis=2
        )
        partner_q = lax.ppermute(partner_q, "sub", swap)
        cache_mine = None
        prompt_mine = lax.dynamic_slice_in_dim(
            prompt_key_value[local_blocks - WIN:], head_off * kvw, my_heads * kvw, axis=2
        )
    else:
        cache_mine = cache_kv
        prompt_mine = prompt_key_value[local_blocks - WIN:]

    window_part = passed_along(prompt_mine, "ctx", 1)
    if split:
        global_src = lax.dynamic_slice_in_dim(cache_kv[:NG], head_off * kvw, my_heads * kvw, axis=2)
    else:
        global_src = cache_kv[:NG]
    global_part = from_root(global_src, "ctx")

    per_reader = rand_blocks.reshape(ctx_count, local_blocks * rand_count)
    owners = per_reader // cache_blocks
    owner_hot = (
        owners[:, :, None] == jnp.arange(ctx_count, dtype=jnp.int32)[None, None, :]
    ).astype(jnp.int32)
    slot_rank = jnp.sum((jnp.cumsum(owner_hot, axis=1) - 1) * owner_hot, axis=2)
    picked = (
        (owners == ctx_index)[:, :, None]
        & (slot_rank[:, :, None] == jnp.arange(capacity, dtype=jnp.int32)[None, None, :])
    ).astype(jnp.int32)
    local_ids = jnp.sum(picked * (per_reader % cache_blocks)[:, :, None], axis=1)
    send_ids = local_ids.reshape(-1)
    chunks = 2 if my_heads % 2 == 0 else 1
    chunk_heads = my_heads // chunks
    chunk_width = chunk_heads * kvw
    incoming = []
    for c in range(chunks):
        if split:
            source = lax.dynamic_slice_in_dim(
                cache_kv, (head_off + c * chunk_heads) * kvw, chunk_width, axis=2
            )
        else:
            source = cache_mine[:, :, c * chunk_width:(c + 1) * chunk_width]
        piece = jnp.take(source, send_ids, axis=0, mode="clip")
        if incoming:
            piece, _ = lax.optimization_barrier((piece, incoming[-1]))
        incoming.append(lax.all_to_all(piece, "ctx", split_axis=0, concat_axis=0, tiled=True))

    own_refs = lax.dynamic_index_in_dim(per_reader, ctx_index, 0, keepdims=False)
    own_ranks = lax.dynamic_index_in_dim(slot_rank, ctx_index, 0, keepdims=False)
    own_ranks = jnp.minimum(own_ranks, capacity - 1)
    rpos = (own_refs // cache_blocks * capacity + own_ranks).astype(jnp.int32)
    rpos = rpos.reshape(-1)

    local_order = jnp.arange(local_blocks, dtype=jnp.int32)
    global_order = ctx_index * local_blocks + local_order
    steps_back = jnp.arange(WIN, 0, -1, dtype=jnp.int32)
    back_global = global_order[:, None] - steps_back[None, :]
    cache_ids = jnp.concatenate(
        [
            jnp.broadcast_to(jnp.arange(NG, dtype=jnp.int32)[None, :], (local_blocks, NG)),
            own_refs.reshape(local_blocks, rand_count),
        ],
        axis=1,
    )
    prompt_ids = jnp.concatenate([jnp.maximum(back_global, 0), global_order[:, None]], axis=1)
    scale_row_table = jnp.concatenate(
        [jnp.take(cache_scale, cache_ids, axis=0), jnp.take(prompt_scale, prompt_ids, axis=0)],
        axis=1,
    )
    key_total = scale_row_table.shape[1]
    scale_row_table = scale_row_table.reshape(local_blocks, key_total, local_heads, 2)
    scale_row_table = jnp.transpose(scale_row_table, (0, 2, 3, 1))
    key_scale = scale_row_table[:, :, 0] / math.sqrt(head_dim) * math.log2(math.e)
    key_scale = jnp.repeat(key_scale, block_rows, axis=-1)
    value_scale = jnp.repeat(scale_row_table[:, :, 1], block_rows, axis=-1)
    key_scale = key_scale.reshape(local_blocks, local_heads, 1, key_total * block_rows)
    value_scale = value_scale.reshape(local_blocks, local_heads, 1, key_total * block_rows)

    def run(q_array, q_head_off, row_off, out_width, out_head_off, c, prev):
        c_off = c * chunk_heads
        meta = jnp.stack(
            [ctx_index * local_blocks, row_off, q_head_off + c_off, head_off + c_off,
             out_head_off + c_off, jnp.int32(c_off)]
        )
        meta = meta.astype(jnp.int32)

        def kv_spec(index_fn):
            return pl.BlockSpec((1, block_rows, kvw), index_fn)

        in_specs = [
            pl.BlockSpec((1, row_count, qw), lambda g, b, rp, mt: (b, 0, mt[2] + g)),
            pl.BlockSpec((1, 1, 1, key_total * block_rows), lambda g, b, rp, mt: (b, mt[3] + g, 0, 0)),
            pl.BlockSpec((1, 1, 1, key_total * block_rows), lambda g, b, rp, mt: (b, mt[3] + g, 0, 0)),
            kv_spec(lambda g, b, rp, mt: (0, 0, mt[5] + g)),
            kv_spec(lambda g, b, rp, mt: (1, 0, mt[5] + g)),
            kv_spec(lambda g, b, rp, mt: (rp[b * 3], 0, g)),
            kv_spec(lambda g, b, rp, mt: (rp[b * 3 + 1], 0, g)),
            kv_spec(lambda g, b, rp, mt: (rp[b * 3 + 2], 0, g)),
            kv_spec(lambda g, b, rp, mt: (jnp.minimum(b, 1), 0, mt[5] + g)),
            kv_spec(lambda g, b, rp, mt: (1, 0, mt[5] + g)),
            kv_spec(lambda g, b, rp, mt: (jnp.maximum(b - 2, 0), 0, mt[3] + g)),
            kv_spec(lambda g, b, rp, mt: (jnp.maximum(b - 1, 0), 0, mt[3] + g)),
            kv_spec(lambda g, b, rp, mt: (b, 0, mt[3] + g)),
        ]
        args = [
            q_array, key_scale, value_scale,
            global_part, global_part, incoming[c], incoming[c], incoming[c], window_part, window_part,
            prompt_key_value, prompt_key_value, prompt_key_value,
        ]
        aliases = {}
        if prev is not None:
            in_specs.append(pl.BlockSpec(memory_space=pl.ANY))
            aliases = {2 + len(args): 0}
            args.append(prev)
        steps = chunk_heads * local_blocks
        out_spec = pl.BlockSpec((1, row_count, qw), lambda g, b, rp, mt: (b, 0, mt[4] + g))
        call = pl.pallas_call(
            attention_kernel,
            out_shape=jax.ShapeDtypeStruct((local_blocks, row_count, out_width), queries.dtype),
            grid_spec=pltpu.PrefetchScalarGridSpec(
                num_scalar_prefetch=2,
                grid=(chunk_heads, local_blocks),
                in_specs=in_specs,
                out_specs=out_spec,
            ),
            input_output_aliases=aliases,
            cost_estimate=pl.CostEstimate(
                flops=steps * 4 * query_groups * row_count * key_total * block_rows * head_dim,
                transcendentals=steps * query_groups * row_count * key_total * block_rows,
                bytes_accessed=steps * 2 * (2 * row_count * qw + key_total * block_rows * kvw),
            ),
            compiler_params=pltpu.CompilerParams(
                dimension_semantics=("arbitrary", "arbitrary"),
                vmem_limit_bytes=48 * 1024 * 1024,
            ),
        )
        return call(rpos, meta, *args)

    zero = jnp.int32(0)
    if not split:
        out = None
        for c in range(chunks):
            out = run(queries, zero, sub_index * row_count, query_width, zero, c, out)
        return out
    for_partner = None
    mine = None
    from_partner = None
    partner_in = partner_q
    for c in range(chunks):
        if mine is not None:
            partner_in, mine = lax.optimization_barrier((partner_q, mine))
        for_partner = run(
            partner_in, zero, (1 - sub_index) * row_count, my_heads * qw, zero, c, for_partner
        )
        if c == chunks - 1:
            from_partner = lax.ppermute(for_partner, "sub", swap)
        mine = run(queries, head_off, sub_index * row_count, query_width, head_off, c, mine)
    return place_columns(mine, from_partner, jnp.reshape(1 - sub_index, (1,)).astype(jnp.int32))


def solution(mesh):
    in_specs = (
        P(("group", "ctx"), "sub", "kvh"),
        P(("group", "ctx"), None, "kvh"),
        P("group", "kvh"),
        P(("group", "ctx"), None, "kvh"),
        P("group", "kvh"),
        P("group", None),
    )
    out_specs = P(("group", "ctx"), "sub", "kvh")
    return jax.shard_map(body, mesh=mesh, in_specs=in_specs, out_specs=out_specs, check_vma=False)
```

```python
import math

import jax
import jax.numpy as jnp
from jax import lax
from jax.experimental import pallas as pl
from jax.experimental.pallas import tpu as pltpu
from jax.sharding import PartitionSpec as P

HEAD_SIZE = 128

NG = 2
WIN = 2


def passed_along(block, axis, distance):
    devices = range(lax.axis_size(axis))
    route = [(i - distance, i) for i in devices if i - distance in devices]
    return lax.ppermute(block, axis, route)


def from_root(block, axis):
    count = lax.axis_size(axis)
    index = lax.axis_index(axis)
    have = block
    for dist in range(1, count):
        got = lax.ppermute(block, axis, [(0, dist)])
        have = jnp.where(index == dist, got, have)
    return have


def place_kernel(off_ref, src_ref, prev_ref, out_ref):
    out_ref[...] = src_ref[...]


def place_columns(dest, src, block_index):
    steps = 4 if src.shape[0] % 4 == 0 else 1
    piece = (src.shape[0] // steps,) + tuple(src.shape[1:])
    return pl.pallas_call(
        place_kernel,
        out_shape=jax.ShapeDtypeStruct(dest.shape, dest.dtype),
        grid_spec=pltpu.PrefetchScalarGridSpec(
            num_scalar_prefetch=1,
            grid=(steps,),
            in_specs=[
                pl.BlockSpec(piece, lambda i, off: (i, 0, 0)),
                pl.BlockSpec(memory_space=pl.ANY),
            ],
            out_specs=pl.BlockSpec(piece, lambda i, off: (i, 0, off[0])),
        ),
        input_output_aliases={2: 0},
        compiler_params=pltpu.CompilerParams(vmem_limit_bytes=48 * 1024 * 1024),
    )(block_index, src, dest)


def attention_kernel(
    rpos_ref, meta_ref,
    q_ref, ks_ref, vs_ref,
    g0_ref, g1_ref, r0_ref, r1_ref, r2_ref, w5r_ref, w6r_ref,
    wl5_ref, wl6_ref, own_ref, *rest,
):
    o_ref = rest[-1]
    b = pl.program_id(1)
    base = meta_ref[0]
    row_off = meta_ref[1]
    rows = q_ref.shape[1]
    groups = q_ref.shape[2] // HEAD_SIZE
    block_rows = own_ref.shape[1]
    d = HEAD_SIZE

    q = q_ref[0]
    q2 = jnp.concatenate([q[:, h * d:(h + 1) * d] for h in range(groups)], axis=0)

    w5 = jnp.where(b < 2, w5r_ref[0], wl5_ref[0])
    w6 = jnp.where(b < 1, w6r_ref[0], wl6_ref[0])
    blocks = [g0_ref[0], g1_ref[0], r0_ref[0], r1_ref[0], r2_ref[0], w5, w6]
    own = own_ref[0]
    keys = jnp.concatenate([blk[:, :d] for blk in blocks], axis=0)
    vals = jnp.concatenate([blk[:, d:] for blk in blocks], axis=0)
    front = keys.shape[0]

    dims = (((1,), (1,)), ((), ()))
    pv = (((1,), (0,)), ((), ()))
    glob_b = base + b

    def compute(masked):
        ks = ks_ref[0, 0]
        vs = vs_ref[0, 0]
        s_a = lax.dot_general(q2, keys, dims, preferred_element_type=jnp.float32)
        s_a = s_a * ks[:, :front]
        if masked:
            col = lax.broadcasted_iota(jnp.int32, (1, front), 1)
            bad = ((col >= 5 * block_rows) & (col < 6 * block_rows) & (glob_b < 2)) | (
                (col >= 6 * block_rows) & (glob_b < 1)
            )
            s_a = jnp.where(bad, -jnp.inf, s_a)
        s_b = lax.dot_general(q2, own[:, :d], dims, preferred_element_type=jnp.float32)
        s_b = s_b * ks[:, front:]
        kcol = lax.broadcasted_iota(jnp.int32, (1, block_rows), 1)
        row = lax.broadcasted_iota(jnp.int32, (groups * rows, 1), 0) % rows + row_off
        s_b = jnp.where(kcol <= row, s_b, -jnp.inf)
        m = jnp.maximum(jnp.max(s_a, axis=1, keepdims=True), jnp.max(s_b, axis=1, keepdims=True))
        p_a = jnp.exp2(s_a - m)
        p_b = jnp.exp2(s_b - m)
        totals = jnp.sum(p_a, axis=1, keepdims=True) + jnp.sum(p_b, axis=1, keepdims=True)
        w_a = (p_a * vs[:, :front]).astype(jnp.bfloat16)
        w_b = (p_b * vs[:, front:]).astype(jnp.bfloat16)
        acc = lax.dot_general(w_a, vals, pv, preferred_element_type=jnp.float32)
        acc = acc + lax.dot_general(w_b, own[:, d:], pv, preferred_element_type=jnp.float32)
        res = (acc / totals).astype(o_ref.dtype)
        for h in range(groups):
            o_ref[0, :, h * d:(h + 1) * d] = res[h * rows:(h + 1) * rows]

    @pl.when(glob_b < 2)
    def _():
        compute(True)

    @pl.when(glob_b >= 2)
    def _():
        compute(False)


def body(queries, cache_kv, cache_scale, prompt_key_value, prompt_scale, rand_blocks):
    ctx_count = lax.axis_size("ctx")
    ctx_index = lax.axis_index("ctx")
    sub_count = lax.axis_size("sub")
    sub_index = lax.axis_index("sub")
    local_blocks, row_count, query_width = queries.shape
    cache_blocks, block_rows, kv_width = cache_kv.shape
    head_dim = HEAD_SIZE
    kvw = 2 * head_dim
    local_heads = kv_width // kvw
    query_groups = query_width // (local_heads * head_dim)
    qw = query_groups * head_dim
    rand_count = rand_blocks.shape[1]
    capacity = max(2, (local_blocks * rand_count + ctx_count - 1) // ctx_count)
    split = sub_count == 2 and local_heads % 2 == 0
    my_heads = local_heads // 2 if split else local_heads
    head_off = sub_index * my_heads if split else jnp.int32(0)
    swap = [(0, 1), (1, 0)]

    if split:
        partner_q = lax.dynamic_slice_in_dim(
            queries, (1 - sub_index) * my_heads * qw, my_heads * qw, axis=2
        )
        partner_q = lax.ppermute(partner_q, "sub", swap)
        cache_mine = None
        prompt_mine = lax.dynamic_slice_in_dim(
            prompt_key_value[local_blocks - WIN:], head_off * kvw, my_heads * kvw, axis=2
        )
    else:
        cache_mine = cache_kv
        prompt_mine = prompt_key_value[local_blocks - WIN:]

    window_part = passed_along(prompt_mine, "ctx", 1)
    if split:
        global_src = lax.dynamic_slice_in_dim(cache_kv[:NG], head_off * kvw, my_heads * kvw, axis=2)
    else:
        global_src = cache_kv[:NG]
    global_part = from_root(global_src, "ctx")

    per_reader = rand_blocks.reshape(ctx_count, local_blocks * rand_count)
    owners = per_reader // cache_blocks
    owner_hot = (
        owners[:, :, None] == jnp.arange(ctx_count, dtype=jnp.int32)[None, None, :]
    ).astype(jnp.int32)
    slot_rank = jnp.sum((jnp.cumsum(owner_hot, axis=1) - 1) * owner_hot, axis=2)
    picked = (
        (owners == ctx_index)[:, :, None]
        & (slot_rank[:, :, None] == jnp.arange(capacity, dtype=jnp.int32)[None, None, :])
    ).astype(jnp.int32)
    local_ids = jnp.sum(picked * (per_reader % cache_blocks)[:, :, None], axis=1)
    send_ids = local_ids.reshape(-1)
    chunks = 2 if my_heads % 2 == 0 else 1
    chunk_heads = my_heads // chunks
    chunk_width = chunk_heads * kvw
    incoming = []
    for c in range(chunks):
        if split:
            source = lax.dynamic_slice_in_dim(
                cache_kv, (head_off + c * chunk_heads) * kvw, chunk_width, axis=2
            )
        else:
            source = cache_mine[:, :, c * chunk_width:(c + 1) * chunk_width]
        piece = jnp.take(source, send_ids, axis=0, mode="clip")
        if incoming:
            piece, _ = lax.optimization_barrier((piece, incoming[-1]))
        incoming.append(lax.all_to_all(piece, "ctx", split_axis=0, concat_axis=0, tiled=True))

    own_refs = lax.dynamic_index_in_dim(per_reader, ctx_index, 0, keepdims=False)
    own_ranks = lax.dynamic_index_in_dim(slot_rank, ctx_index, 0, keepdims=False)
    own_ranks = jnp.minimum(own_ranks, capacity - 1)
    rpos = (own_refs // cache_blocks * capacity + own_ranks).astype(jnp.int32)
    rpos = rpos.reshape(-1)

    local_order = jnp.arange(local_blocks, dtype=jnp.int32)
    global_order = ctx_index * local_blocks + local_order
    steps_back = jnp.arange(WIN, 0, -1, dtype=jnp.int32)
    back_global = global_order[:, None] - steps_back[None, :]
    cache_ids = jnp.concatenate(
        [
            jnp.broadcast_to(jnp.arange(NG, dtype=jnp.int32)[None, :], (local_blocks, NG)),
            own_refs.reshape(local_blocks, rand_count),
        ],
        axis=1,
    )
    prompt_ids = jnp.concatenate([jnp.maximum(back_global, 0), global_order[:, None]], axis=1)
    scale_row_table = jnp.concatenate(
        [jnp.take(cache_scale, cache_ids, axis=0), jnp.take(prompt_scale, prompt_ids, axis=0)],
        axis=1,
    )
    key_total = scale_row_table.shape[1]
    scale_row_table = scale_row_table.reshape(local_blocks, key_total, local_heads, 2)
    scale_row_table = jnp.transpose(scale_row_table, (0, 2, 3, 1))
    key_scale = scale_row_table[:, :, 0] / math.sqrt(head_dim) * math.log2(math.e)
    key_scale = jnp.repeat(key_scale, block_rows, axis=-1)
    value_scale = jnp.repeat(scale_row_table[:, :, 1], block_rows, axis=-1)
    key_scale = key_scale.reshape(local_blocks, local_heads, 1, key_total * block_rows)
    value_scale = value_scale.reshape(local_blocks, local_heads, 1, key_total * block_rows)

    def run(q_array, q_head_off, row_off, out_width, out_head_off, c, prev):
        c_off = c * chunk_heads
        meta = jnp.stack(
            [ctx_index * local_blocks, row_off, q_head_off + c_off, head_off + c_off,
             out_head_off + c_off, jnp.int32(c_off)]
        )
        meta = meta.astype(jnp.int32)

        def kv_spec(index_fn):
            return pl.BlockSpec((1, block_rows, kvw), index_fn)

        in_specs = [
            pl.BlockSpec((1, row_count, qw), lambda g, b, rp, mt: (b, 0, mt[2] + g)),
            pl.BlockSpec((1, 1, 1, key_total * block_rows), lambda g, b, rp, mt: (b, mt[3] + g, 0, 0)),
            pl.BlockSpec((1, 1, 1, key_total * block_rows), lambda g, b, rp, mt: (b, mt[3] + g, 0, 0)),
            kv_spec(lambda g, b, rp, mt: (0, 0, mt[5] + g)),
            kv_spec(lambda g, b, rp, mt: (1, 0, mt[5] + g)),
            kv_spec(lambda g, b, rp, mt: (rp[b * 3], 0, g)),
            kv_spec(lambda g, b, rp, mt: (rp[b * 3 + 1], 0, g)),
            kv_spec(lambda g, b, rp, mt: (rp[b * 3 + 2], 0, g)),
            kv_spec(lambda g, b, rp, mt: (jnp.minimum(b, 1), 0, mt[5] + g)),
            kv_spec(lambda g, b, rp, mt: (1, 0, mt[5] + g)),
            kv_spec(lambda g, b, rp, mt: (jnp.maximum(b - 2, 0), 0, mt[3] + g)),
            kv_spec(lambda g, b, rp, mt: (jnp.maximum(b - 1, 0), 0, mt[3] + g)),
            kv_spec(lambda g, b, rp, mt: (b, 0, mt[3] + g)),
        ]
        args = [
            q_array, key_scale, value_scale,
            global_part, global_part, incoming[c], incoming[c], incoming[c], window_part, window_part,
            prompt_key_value, prompt_key_value, prompt_key_value,
        ]
        aliases = {}
        if prev is not None:
            in_specs.append(pl.BlockSpec(memory_space=pl.ANY))
            aliases = {2 + len(args): 0}
            args.append(prev)
        steps = chunk_heads * local_blocks
        out_spec = pl.BlockSpec((1, row_count, qw), lambda g, b, rp, mt: (b, 0, mt[4] + g))
        call = pl.pallas_call(
            attention_kernel,
            out_shape=jax.ShapeDtypeStruct((local_blocks, row_count, out_width), queries.dtype),
            grid_spec=pltpu.PrefetchScalarGridSpec(
                num_scalar_prefetch=2,
                grid=(chunk_heads, local_blocks),
                in_specs=in_specs,
                out_specs=out_spec,
            ),
            input_output_aliases=aliases,
            cost_estimate=pl.CostEstimate(
                flops=steps * 4 * query_groups * row_count * key_total * block_rows * head_dim,
                transcendentals=steps * query_groups * row_count * key_total * block_rows,
                bytes_accessed=steps * 2 * (2 * row_count * qw + key_total * block_rows * kvw),
            ),
            compiler_params=pltpu.CompilerParams(
                dimension_semantics=("arbitrary", "arbitrary"),
                vmem_limit_bytes=48 * 1024 * 1024,
            ),
        )
        return call(rpos, meta, *args)

    zero = jnp.int32(0)
    if not split:
        out = None
        for c in range(chunks):
            out = run(queries, zero, sub_index * row_count, query_width, zero, c, out)
        return out
    for_partner = None
    mine = None
    from_partner = None
    partner_in = partner_q
    for c in range(chunks):
        if mine is not None:
            partner_in, mine = lax.optimization_barrier((partner_q, mine))
        for_partner = run(
            partner_in, zero, (1 - sub_index) * row_count, my_heads * qw, zero, c, for_partner
        )
        if c == chunks - 1:
            from_partner = lax.ppermute(for_partner, "sub", swap)
        mine = run(queries, head_off, sub_index * row_count, query_width, head_off, c, mine)
    return place_columns(mine, from_partner, jnp.reshape(1 - sub_index, (1,)).astype(jnp.int32))


def solution(mesh):
    in_specs = (
        P(("group", "ctx"), "sub", "kvh"),
        P(("group", "ctx"), None, "kvh"),
        P("group", "kvh"),
        P(("group", "ctx"), None, "kvh"),
        P("group", "kvh"),
        P("group", None),
    )
    out_specs = P(("group", "ctx"), "sub", "kvh")
    return jax.shard_map(body, mesh=mesh, in_specs=in_specs, out_specs=out_specs, check_vma=False)
```

```python
import math

import jax
import jax.numpy as jnp
from jax import lax
from jax.experimental import pallas as pl
from jax.experimental.pallas import tpu as pltpu
from jax.sharding import PartitionSpec as P

HEAD_SIZE = 128

NG = 2
WIN = 2


def passed_along(block, axis, distance):
    devices = range(lax.axis_size(axis))
    route = [(i - distance, i) for i in devices if i - distance in devices]
    return lax.ppermute(block, axis, route)


def from_root(block, axis):
    count = lax.axis_size(axis)
    index = lax.axis_index(axis)
    have = block
    for dist in range(1, count):
        got = lax.ppermute(block, axis, [(0, dist)])
        have = jnp.where(index == dist, got, have)
    return have


def place_kernel(off_ref, src_ref, prev_ref, out_ref):
    out_ref[...] = src_ref[...]


def place_columns(dest, src, block_index):
    return pl.pallas_call(
        place_kernel,
        out_shape=jax.ShapeDtypeStruct(dest.shape, dest.dtype),
        grid_spec=pltpu.PrefetchScalarGridSpec(
            num_scalar_prefetch=1,
            grid=(1,),
            in_specs=[
                pl.BlockSpec(src.shape, lambda i, off: (0, 0, 0)),
                pl.BlockSpec(memory_space=pl.ANY),
            ],
            out_specs=pl.BlockSpec(src.shape, lambda i, off: (0, 0, off[0])),
        ),
        input_output_aliases={2: 0},
        compiler_params=pltpu.CompilerParams(vmem_limit_bytes=48 * 1024 * 1024),
    )(block_index, src, dest)


def attention_kernel(
    rpos_ref, meta_ref,
    q_ref, ks_ref, vs_ref,
    g0_ref, g1_ref, r0_ref, r1_ref, r2_ref, w5r_ref, w6r_ref,
    wl5_ref, wl6_ref, own_ref, *rest,
):
    o_ref = rest[-1]
    b = pl.program_id(1)
    base = meta_ref[0]
    row_off = meta_ref[1]
    rows = q_ref.shape[1]
    groups = q_ref.shape[2] // HEAD_SIZE
    block_rows = own_ref.shape[1]
    d = HEAD_SIZE

    q = q_ref[0]
    q2 = jnp.concatenate([q[:, h * d:(h + 1) * d] for h in range(groups)], axis=0)

    w5 = jnp.where(b < 2, w5r_ref[0], wl5_ref[0])
    w6 = jnp.where(b < 1, w6r_ref[0], wl6_ref[0])
    blocks = [g0_ref[0], g1_ref[0], r0_ref[0], r1_ref[0], r2_ref[0], w5, w6]
    own = own_ref[0]
    keys = jnp.concatenate([blk[:, :d] for blk in blocks], axis=0)
    vals = jnp.concatenate([blk[:, d:] for blk in blocks], axis=0)
    front = keys.shape[0]

    dims = (((1,), (1,)), ((), ()))
    pv = (((1,), (0,)), ((), ()))
    glob_b = base + b

    def compute(masked):
        ks = ks_ref[0, 0]
        vs = vs_ref[0, 0]
        s_a = lax.dot_general(q2, keys, dims, preferred_element_type=jnp.float32)
        s_a = s_a * ks[:, :front]
        if masked:
            col = lax.broadcasted_iota(jnp.int32, (1, front), 1)
            bad = ((col >= 5 * block_rows) & (col < 6 * block_rows) & (glob_b < 2)) | (
                (col >= 6 * block_rows) & (glob_b < 1)
            )
            s_a = jnp.where(bad, -jnp.inf, s_a)
        s_b = lax.dot_general(q2, own[:, :d], dims, preferred_element_type=jnp.float32)
        s_b = s_b * ks[:, front:]
        kcol = lax.broadcasted_iota(jnp.int32, (1, block_rows), 1)
        row = lax.broadcasted_iota(jnp.int32, (groups * rows, 1), 0) % rows + row_off
        s_b = jnp.where(kcol <= row, s_b, -jnp.inf)
        m = jnp.maximum(jnp.max(s_a, axis=1, keepdims=True), jnp.max(s_b, axis=1, keepdims=True))
        p_a = jnp.exp2(s_a - m)
        p_b = jnp.exp2(s_b - m)
        totals = jnp.sum(p_a, axis=1, keepdims=True) + jnp.sum(p_b, axis=1, keepdims=True)
        w_a = (p_a * vs[:, :front]).astype(jnp.bfloat16)
        w_b = (p_b * vs[:, front:]).astype(jnp.bfloat16)
        acc = lax.dot_general(w_a, vals, pv, preferred_element_type=jnp.float32)
        acc = acc + lax.dot_general(w_b, own[:, d:], pv, preferred_element_type=jnp.float32)
        res = (acc / totals).astype(o_ref.dtype)
        for h in range(groups):
            o_ref[0, :, h * d:(h + 1) * d] = res[h * rows:(h + 1) * rows]

    @pl.when(glob_b < 2)
    def _():
        compute(True)

    @pl.when(glob_b >= 2)
    def _():
        compute(False)


def body(queries, cache_kv, cache_scale, prompt_key_value, prompt_scale, rand_blocks):
    ctx_count = lax.axis_size("ctx")
    ctx_index = lax.axis_index("ctx")
    sub_count = lax.axis_size("sub")
    sub_index = lax.axis_index("sub")
    local_blocks, row_count, query_width = queries.shape
    cache_blocks, block_rows, kv_width = cache_kv.shape
    head_dim = HEAD_SIZE
    kvw = 2 * head_dim
    local_heads = kv_width // kvw
    query_groups = query_width // (local_heads * head_dim)
    qw = query_groups * head_dim
    rand_count = rand_blocks.shape[1]
    capacity = max(2, (local_blocks * rand_count + ctx_count - 1) // ctx_count)
    split = sub_count == 2 and local_heads % 2 == 0
    my_heads = local_heads // 2 if split else local_heads
    head_off = sub_index * my_heads if split else jnp.int32(0)
    swap = [(0, 1), (1, 0)]

    if split:
        partner_q = lax.dynamic_slice_in_dim(
            queries, (1 - sub_index) * my_heads * qw, my_heads * qw, axis=2
        )
        partner_q = lax.ppermute(partner_q, "sub", swap)
        cache_mine = None
        prompt_mine = lax.dynamic_slice_in_dim(
            prompt_key_value[local_blocks - WIN:], head_off * kvw, my_heads * kvw, axis=2
        )
    else:
        cache_mine = cache_kv
        prompt_mine = prompt_key_value[local_blocks - WIN:]

    window_part = passed_along(prompt_mine, "ctx", 1)
    if split:
        global_src = lax.dynamic_slice_in_dim(cache_kv[:NG], head_off * kvw, my_heads * kvw, axis=2)
    else:
        global_src = cache_kv[:NG]
    global_part = from_root(global_src, "ctx")

    per_reader = rand_blocks.reshape(ctx_count, local_blocks * rand_count)
    owners = per_reader // cache_blocks
    owner_hot = (
        owners[:, :, None] == jnp.arange(ctx_count, dtype=jnp.int32)[None, None, :]
    ).astype(jnp.int32)
    slot_rank = jnp.sum((jnp.cumsum(owner_hot, axis=1) - 1) * owner_hot, axis=2)
    picked = (
        (owners == ctx_index)[:, :, None]
        & (slot_rank[:, :, None] == jnp.arange(capacity, dtype=jnp.int32)[None, None, :])
    ).astype(jnp.int32)
    local_ids = jnp.sum(picked * (per_reader % cache_blocks)[:, :, None], axis=1)
    send_ids = local_ids.reshape(-1)
    chunks = 2 if my_heads % 2 == 0 else 1
    chunk_heads = my_heads // chunks
    chunk_width = chunk_heads * kvw
    incoming = []
    for c in range(chunks):
        if split:
            source = lax.dynamic_slice_in_dim(
                cache_kv, (head_off + c * chunk_heads) * kvw, chunk_width, axis=2
            )
        else:
            source = cache_mine[:, :, c * chunk_width:(c + 1) * chunk_width]
        piece = jnp.take(source, send_ids, axis=0, mode="clip")
        if incoming:
            piece, _ = lax.optimization_barrier((piece, incoming[-1]))
        incoming.append(lax.all_to_all(piece, "ctx", split_axis=0, concat_axis=0, tiled=True))

    own_refs = lax.dynamic_index_in_dim(per_reader, ctx_index, 0, keepdims=False)
    own_ranks = lax.dynamic_index_in_dim(slot_rank, ctx_index, 0, keepdims=False)
    own_ranks = jnp.minimum(own_ranks, capacity - 1)
    rpos = (own_refs // cache_blocks * capacity + own_ranks).astype(jnp.int32)
    rpos = rpos.reshape(-1)

    local_order = jnp.arange(local_blocks, dtype=jnp.int32)
    global_order = ctx_index * local_blocks + local_order
    steps_back = jnp.arange(WIN, 0, -1, dtype=jnp.int32)
    back_global = global_order[:, None] - steps_back[None, :]
    cache_ids = jnp.concatenate(
        [
            jnp.broadcast_to(jnp.arange(NG, dtype=jnp.int32)[None, :], (local_blocks, NG)),
            own_refs.reshape(local_blocks, rand_count),
        ],
        axis=1,
    )
    prompt_ids = jnp.concatenate([jnp.maximum(back_global, 0), global_order[:, None]], axis=1)
    scale_row_table = jnp.concatenate(
        [jnp.take(cache_scale, cache_ids, axis=0), jnp.take(prompt_scale, prompt_ids, axis=0)],
        axis=1,
    )
    key_total = scale_row_table.shape[1]
    scale_row_table = scale_row_table.reshape(local_blocks, key_total, local_heads, 2)
    scale_row_table = jnp.transpose(scale_row_table, (0, 2, 3, 1))
    key_scale = scale_row_table[:, :, 0] / math.sqrt(head_dim) * math.log2(math.e)
    key_scale = jnp.repeat(key_scale, block_rows, axis=-1)
    value_scale = jnp.repeat(scale_row_table[:, :, 1], block_rows, axis=-1)
    key_scale = key_scale.reshape(local_blocks, local_heads, 1, key_total * block_rows)
    value_scale = value_scale.reshape(local_blocks, local_heads, 1, key_total * block_rows)

    def run(q_array, q_head_off, row_off, out_width, out_head_off, c, prev):
        c_off = c * chunk_heads
        meta = jnp.stack(
            [ctx_index * local_blocks, row_off, q_head_off + c_off, head_off + c_off,
             out_head_off + c_off, jnp.int32(c_off)]
        )
        meta = meta.astype(jnp.int32)

        def kv_spec(index_fn):
            return pl.BlockSpec((1, block_rows, kvw), index_fn)

        in_specs = [
            pl.BlockSpec((1, row_count, qw), lambda g, b, rp, mt: (b, 0, mt[2] + g)),
            pl.BlockSpec((1, 1, 1, key_total * block_rows), lambda g, b, rp, mt: (b, mt[3] + g, 0, 0)),
            pl.BlockSpec((1, 1, 1, key_total * block_rows), lambda g, b, rp, mt: (b, mt[3] + g, 0, 0)),
            kv_spec(lambda g, b, rp, mt: (0, 0, mt[5] + g)),
            kv_spec(lambda g, b, rp, mt: (1, 0, mt[5] + g)),
            kv_spec(lambda g, b, rp, mt: (rp[b * 3], 0, g)),
            kv_spec(lambda g, b, rp, mt: (rp[b * 3 + 1], 0, g)),
            kv_spec(lambda g, b, rp, mt: (rp[b * 3 + 2], 0, g)),
            kv_spec(lambda g, b, rp, mt: (jnp.minimum(b, 1), 0, mt[5] + g)),
            kv_spec(lambda g, b, rp, mt: (1, 0, mt[5] + g)),
            kv_spec(lambda g, b, rp, mt: (jnp.maximum(b - 2, 0), 0, mt[3] + g)),
            kv_spec(lambda g, b, rp, mt: (jnp.maximum(b - 1, 0), 0, mt[3] + g)),
            kv_spec(lambda g, b, rp, mt: (b, 0, mt[3] + g)),
        ]
        args = [
            q_array, key_scale, value_scale,
            global_part, global_part, incoming[c], incoming[c], incoming[c], window_part, window_part,
            prompt_key_value, prompt_key_value, prompt_key_value,
        ]
        aliases = {}
        if prev is not None:
            in_specs.append(pl.BlockSpec(memory_space=pl.ANY))
            aliases = {2 + len(args): 0}
            args.append(prev)
        steps = chunk_heads * local_blocks
        out_spec = pl.BlockSpec((1, row_count, qw), lambda g, b, rp, mt: (b, 0, mt[4] + g))
        call = pl.pallas_call(
            attention_kernel,
            out_shape=jax.ShapeDtypeStruct((local_blocks, row_count, out_width), queries.dtype),
            grid_spec=pltpu.PrefetchScalarGridSpec(
                num_scalar_prefetch=2,
                grid=(chunk_heads, local_blocks),
                in_specs=in_specs,
                out_specs=out_spec,
            ),
            input_output_aliases=aliases,
            cost_estimate=pl.CostEstimate(
                flops=steps * 4 * query_groups * row_count * key_total * block_rows * head_dim,
                transcendentals=steps * query_groups * row_count * key_total * block_rows,
                bytes_accessed=steps * 2 * (2 * row_count * qw + key_total * block_rows * kvw),
            ),
            compiler_params=pltpu.CompilerParams(
                dimension_semantics=("arbitrary", "arbitrary"),
                vmem_limit_bytes=48 * 1024 * 1024,
            ),
        )
        return call(rpos, meta, *args)

    zero = jnp.int32(0)
    if not split:
        out = None
        for c in range(chunks):
            out = run(queries, zero, sub_index * row_count, query_width, zero, c, out)
        return out
    mine = None
    sent = []
    partner_in = partner_q
    for c in range(chunks):
        if mine is not None:
            partner_in, mine = lax.optimization_barrier((partner_q, mine))
        for_partner = run(
            partner_in, zero, (1 - sub_index) * row_count, chunk_heads * qw,
            jnp.int32(-c * chunk_heads), c, None,
        )
        sent.append(lax.ppermute(for_partner, "sub", swap))
        mine = run(queries, head_off, sub_index * row_count, query_width, head_off, c, mine)
    for c in range(chunks):
        where = jnp.reshape((1 - sub_index) * chunks + c, (1,)).astype(jnp.int32)
        mine = place_columns(mine, sent[c], where)
    return mine


def solution(mesh):
    in_specs = (
        P(("group", "ctx"), "sub", "kvh"),
        P(("group", "ctx"), None, "kvh"),
        P("group", "kvh"),
        P(("group", "ctx"), None, "kvh"),
        P("group", "kvh"),
        P("group", None),
    )
    out_specs = P(("group", "ctx"), "sub", "kvh")
    return jax.shard_map(body, mesh=mesh, in_specs=in_specs, out_specs=out_specs, check_vma=False)
```
